32 devices in a mesh: grp: 4 (over z), gx: 4 (over y, core), gy: 2 (over x).
Axes of the slice: x: 2, y: 2, z: 4, core: 2. Of those that a mesh axis runs over, the one named last changes fastest.
Arguments:
- source: float32 [64, 32, 512], P('gx', 'gy', 'grp'), may hold values from -13 to 13
- conductance: float32 [64, 32, 512], P('gx', 'gy', 'grp'), may hold values from 0.2 to 5
- storage: float32 [64, 32, 512], P('gx', 'gy', 'grp'), may hold values from 0.05 to 1
- aggregate_ids: int32 [64, 32, 512], P('gx', 'gy', 'grp'), may hold values from 0 to 511, as said below
- coarse_values: float32 [256, 64, 256], P(('grp', 'gx', 'gy')), as said below
- coarse_columns: int32 [256, 4], P(('grp', 'gx', 'gy')), may hold values from 0 to 255, as said below
Outputs:
- solution: float32 [64, 32, 512], P('gx', 'gy', 'grp')
- coarse_error: float32 [16384], P(('grp', 'gx', 'gy'))
The draws below stay inside these ranges and needn't reach their ends.
Inputs may be any that keep to these rules, and one draw needn't show every extreme that they name: `aggregate_ids`: on each device, every id names exactly the 64 cells of one aligned 4 x 4 x 4 box of the device's block, and different boxes have different ids. `coarse_columns`: entry 0 of block row b is b itself; every other entry names a block of a device whose gx and gy indices differ from those of row b's device by at most one. `coarse_values`: in every row of the coarse operator the diagonal entry of the first stored block exceeds the sum of the magnitudes of all other stored entries of that row.
All inputs are finite; a program needn't handle non-finite values.
Results may differ from the reference program's by a relative error of at most 0.0001.
Values sent between devices are 32-bit elements; how exact they have to be, the bound alone decides.
No kernel may reach another device: no remote copies, remote signals or barrier semaphores. Data moves between devices by JAX's collectives and lax.ppermute only.
A program may use at most 64 MiB of HBM per device.

```python
import math
import jax
import jax.numpy as jnp
from jax import lax

CX = 16
CY = 16
CZ = 128
NU = 2
CITER = 4
K = 4
NX = 64
NY = 32
NZ = 512
NC_DEV = 512
BDEV = 8
NC = 16384
NB = 256


TWO_PI = 6.283185307179586


def one_permutation(single_key):
    return jax.random.permutation(single_key, NC_DEV).astype(jnp.int32)


def draw_source(key, part):
    key_list = jax.random.split(key, 3)
    phases = jax.random.uniform(key_list[0], (3,), jnp.float32, 0.0, TWO_PI)
    amplitude = jax.random.uniform(key_list[1], (), jnp.float32, 1.5, 2.5)
    rough = jnp.clip(3.0 * jax.random.normal(key_list[2], (NX, NY, NZ), jnp.float32), -9.0, 9.0)
    pos_x = lax.broadcasted_iota(jnp.int32, (NX, NY, NZ), 0).astype(jnp.float32) / NX
    pos_y = lax.broadcasted_iota(jnp.int32, (NX, NY, NZ), 1).astype(jnp.float32) / NY
    pos_z = lax.broadcasted_iota(jnp.int32, (NX, NY, NZ), 2).astype(jnp.float32) / NZ
    wave = jnp.sin(TWO_PI * pos_x + phases[0]) * jnp.sin(TWO_PI * pos_y + phases[1]) * jnp.sin(TWO_PI * pos_z + phases[2])
    return rough + amplitude * (1.0 + 0.5 * wave)


def draw_aggregate_ids(key, part):
    grid_x = NX // CX
    grid_y = NY // CY
    groups = NZ // CZ
    key_list = jax.random.split(key, grid_x * grid_y * groups)
    perm_table = jax.vmap(one_permutation)(key_list)
    cell_x = lax.broadcasted_iota(jnp.int32, (NX, NY, NZ), 0)
    cell_y = lax.broadcasted_iota(jnp.int32, (NX, NY, NZ), 1)
    cell_z = lax.broadcasted_iota(jnp.int32, (NX, NY, NZ), 2)
    device_ids = (cell_z // CZ * grid_x + cell_x // CX) * grid_y + cell_y // CY
    box_ids = (cell_x % CX // 4 * (CY // 4) + cell_y % CY // 4) * (CZ // 4) + cell_z % CZ // 4
    return perm_table[device_ids, box_ids]


def draw_coarse_columns(key, part):
    grid_x = NX // CX
    grid_y = NY // CY
    groups = NZ // CZ
    row_ids = lax.broadcasted_iota(jnp.int32, (NB, K), 0)
    slot_ids = lax.broadcasted_iota(jnp.int32, (NB, K), 1)
    device_ids = row_ids // BDEV
    home_y = device_ids % grid_y
    home_x = device_ids // grid_y % grid_x
    key_list = jax.random.split(key, 4)
    step_x = jax.random.randint(key_list[0], (NB, K), -1, 2)
    step_y = jax.random.randint(key_list[1], (NB, K), -1, 2)
    member_ids = jax.random.randint(key_list[2], (NB, K), 0, groups)
    within_ids = jax.random.randint(key_list[3], (NB, K), 0, BDEV)
    target_x = jnp.clip(home_x + step_x, 0, grid_x - 1)
    target_y = jnp.clip(home_y + step_y, 0, grid_y - 1)
    columns = ((member_ids * grid_x + target_x) * grid_y + target_y) * BDEV + within_ids
    return jnp.where(slot_ids == 0, row_ids, columns).astype(jnp.int32)


def draw_coarse_values(key, part):
    key_list = jax.random.split(key, 2)
    off_part = jax.random.uniform(key_list[0], (NB, 64, K * 64), jnp.float32, 0.5, 1.0)
    main_part = jax.random.uniform(key_list[1], (NB, 64), jnp.float32, 1.01, 1.1)
    identity = jnp.eye(64, dtype=jnp.float32)
    marker = jnp.concatenate([identity, jnp.zeros((64, (K - 1) * 64), jnp.float32)], axis=1)
    leading = (K * 64 - 1) * main_part
    values = -off_part * (1.0 - marker[None]) + marker[None] * leading[:, :, None]
    return values


def block_scale(rng, shape, pieces, smallest, largest):
    level = 1.0
    for dim, blocks in pieces:
        heights = jax.random.uniform(jax.random.fold_in(jax.random.fold_in(rng, 6), dim), (blocks,), jnp.float32, smallest / len(pieces), largest / len(pieces))
        level = level * jnp.repeat(jnp.exp(heights), shape[dim] // blocks).reshape((-1,) + (1,) * (len(shape) - 1 - dim))
    return level


def setup_inputs(seed: int = 0) -> dict:
    splits = jax.random.split(jax.random.key(seed), 7)
    return {
        "source": draw_source(jax.random.fold_in(splits[6], 71), 0),
        "conductance": jnp.clip(jnp.exp(math.log(5.0) - 3.218876 * jax.random.uniform(splits[1], (NX, NY, NZ), jnp.float32) ** block_scale(splits[1], (NX, NY, NZ), ((0, 4), (1, 2), (2, 4)), -0.2, 0.2)), 0.2, 5.0),
        "storage": jnp.clip(jnp.exp(math.log(1.0) - 2.9957323 * jax.random.uniform(splits[2], (NX, NY, NZ), jnp.float32) ** block_scale(splits[2], (NX, NY, NZ), ((0, 4), (1, 2), (2, 4)), -0.2, 0.2)), 0.05, 1.0),
        "aggregate_ids": draw_aggregate_ids(jax.random.fold_in(splits[6], 71), 0),
        "coarse_values": draw_coarse_values(jax.random.fold_in(splits[6], 71), 0),
        "coarse_columns": draw_coarse_columns(jax.random.fold_in(splits[6], 71), 0),
    }


WEIGHT = 2.0 / 3.0
PAIRS = ((0, 1), (0, -1), (1, 1), (1, -1), (2, 1), (2, -1))


def shifted(padded, dimension, offset):
    window = [slice(1, -1), slice(1, -1), slice(1, -1)]
    window[dimension] = slice(1 + offset, padded.shape[dimension] - 1 + offset)
    return padded[tuple(window)]


def face_terms(conductance):
    padded = jnp.pad(conductance, 1)
    return [0.5 * (conductance + shifted(padded, dimension, offset)) for dimension, offset in PAIRS]


def operate(field, storage, face_list):
    padded = jnp.pad(field, 1)
    summed = storage * field
    for position in range(6):
        dimension, offset = PAIRS[position]
        summed = summed + face_list[position] * (field - shifted(padded, dimension, offset))
    return summed


def coarse_apply(vector, coarse_values, coarse_columns):
    blocks = vector.reshape(-1, 64)[coarse_columns]
    blocks = blocks.reshape(blocks.shape[0], -1)
    return jnp.einsum("bim,bm->bi", coarse_values, blocks, precision=lax.Precision.HIGHEST).reshape(-1)


def reference(source, conductance, storage, aggregate_ids, coarse_values, coarse_columns):
    face_list = face_terms(conductance)
    diagonal = storage
    for position in range(6):
        diagonal = diagonal + face_list[position]
    solution = WEIGHT * source / diagonal
    for sweep_number in range(NU - 1):
        solution = solution + WEIGHT * (source - operate(solution, storage, face_list)) / diagonal
    residual = source - operate(solution, storage, face_list)
    smoothed = residual - WEIGHT * operate(residual / diagonal, storage, face_list)
    cell_x = lax.broadcasted_iota(jnp.int32, source.shape, 0)
    cell_y = lax.broadcasted_iota(jnp.int32, source.shape, 1)
    cell_z = lax.broadcasted_iota(jnp.int32, source.shape, 2)
    device_ids = ((cell_z // CZ) * (NX // CX) + cell_x // CX) * (NY // CY) + cell_y // CY
    global_ids = (device_ids * NC_DEV + aggregate_ids).astype(jnp.int32)
    coarse_rhs = jax.ops.segment_sum(smoothed.reshape(-1), global_ids.reshape(-1), num_segments=NC)
    coarse_diag = jnp.diagonal(coarse_values[:, :, :64], axis1=1, axis2=2).reshape(-1)
    coarse_error = coarse_rhs / coarse_diag
    for sweep_number in range(CITER - 1):
        applied = coarse_apply(coarse_error, coarse_values, coarse_columns)
        coarse_error = coarse_error + (coarse_rhs - applied) / coarse_diag
    lifted = coarse_error[global_ids]
    solution = solution + (lifted - WEIGHT * operate(lifted, storage, face_list) / diagonal)
    for sweep_number in range(NU):
        solution = solution + WEIGHT * (source - operate(solution, storage, face_list)) / diagonal
    return (solution, coarse_error)
```

```python
import jax
import jax.numpy as jnp
from jax import lax
from jax.sharding import PartitionSpec as P

NU = 2
CITER = 4
BOX = 4
HALO = 4

WEIGHT = 2.0 / 3.0
PAIRS = ((0, 1), (0, -1), (1, 1), (1, -1), (2, 1), (2, -1))
ALL_AXES = ("grp", "gx", "gy")


def exchange(cells, sides, width):
    for axis, dim in sides:
        count = lax.axis_size(axis)
        size = cells.shape[dim]
        head = lax.slice_in_dim(cells, 0, width, axis=dim)
        tail = lax.slice_in_dim(cells, size - width, size, axis=dim)
        if count == 1:
            before = jnp.zeros_like(tail)
            after = jnp.zeros_like(head)
        elif count == 2:
            index = lax.axis_index(axis)
            sent = jnp.where(index == 0, tail, head)
            got = lax.ppermute(sent, axis, [(0, 1), (1, 0)])
            before = jnp.where(index == 1, got, 0.0)
            after = jnp.where(index == 0, got, 0.0)
        else:
            before = lax.ppermute(tail, axis, [(i, i + 1) for i in range(count - 1)])
            after = lax.ppermute(head, axis, [(i + 1, i) for i in range(count - 1)])
        cells = jnp.concatenate([before, cells, after], axis=dim)
    return cells


def shifted(padded, dimension, offset):
    window = [slice(1, -1), slice(1, -1), slice(1, -1)]
    window[dimension] = slice(1 + offset, padded.shape[dimension] - 1 + offset)
    return padded[tuple(window)]


def face_terms(conductance):
    padded = jnp.pad(conductance, 1)
    return [0.5 * (conductance + shifted(padded, dimension, offset)) for dimension, offset in PAIRS]


def operate(field, storage, face_list):
    padded = jnp.pad(field, 1)
    summed = storage * field
    for position in range(6):
        dimension, offset = PAIRS[position]
        summed = summed + face_list[position] * (field - shifted(padded, dimension, offset))
    return summed


def inside_mask(shape):
    mask = None
    for dim, axis in ((0, "gx"), (1, "gy"), (2, "grp")):
        block = shape[dim] - 2 * HALO
        start = lax.axis_index(axis) * block - HALO
        coords = start + lax.broadcasted_iota(jnp.int32, shape, dim)
        ok = (coords >= 0) & (coords < block * lax.axis_size(axis))
        mask = ok if mask is None else mask & ok
    return mask


def trimmed(array):
    return array[HALO:-HALO, HALO:-HALO, HALO:-HALO]


def local(source, conductance, storage, aggregate_ids, coarse_values, coarse_columns):
    size_x, size_y, size_z = source.shape
    stacked = jnp.stack([source, conductance, storage])
    wide = exchange(stacked, (("grp", 3), ("gx", 1), ("gy", 2)), HALO)
    src, cond, stor = wide[0], wide[1], wide[2]
    mask = inside_mask(src.shape)
    face_list = face_terms(cond)
    diagonal = stor
    for position in range(6):
        diagonal = diagonal + face_list[position]

    def op(field):
        return operate(field, stor, face_list)

    solution = jnp.where(mask, WEIGHT * src / diagonal, 0.0)
    for sweep_number in range(NU - 1):
        solution = jnp.where(mask, solution + WEIGHT * (src - op(solution)) / diagonal, 0.0)
    residual = src - op(solution)
    scaled = jnp.where(mask, residual / diagonal, 0.0)
    smoothed = trimmed(residual - WEIGHT * op(scaled))

    box_labels = aggregate_ids[::BOX, ::BOX, ::BOX].reshape(-1)
    box_totals = (
        smoothed.reshape(size_x // BOX, BOX, size_y // BOX, BOX, size_z // BOX, BOX)
        .sum(axis=(1, 3, 5))
        .reshape(-1)
    )
    coarse_rhs = jnp.zeros(box_totals.shape, source.dtype).at[box_labels].set(box_totals)
    coarse_diag = jnp.diagonal(coarse_values[:, :, :64], axis1=1, axis2=2).reshape(-1)
    block_rows = coarse_values.shape[0]
    coarse_error = coarse_rhs / coarse_diag
    for sweep_number in range(CITER - 1):
        pooled = lax.all_gather(coarse_error, ALL_AXES, axis=0, tiled=True)
        blocks = pooled.reshape(-1, 64)[coarse_columns]
        blocks = blocks.reshape(block_rows, -1)
        applied = jnp.einsum(
            "bim,bm->bi", coarse_values, blocks, precision=lax.Precision.HIGHEST
        ).reshape(-1)
        coarse_error = coarse_error + (coarse_rhs - applied) / coarse_diag

    bx, by, bz = size_x // BOX, size_y // BOX, size_z // BOX
    groups = lax.axis_size("grp")
    grid_x = lax.axis_size("gx")
    grid_y = lax.axis_size("gy")
    small = coarse_error[box_labels]
    every = lax.all_gather(small, ALL_AXES, axis=0, tiled=True)
    every = every.reshape(groups, grid_x, grid_y, bx, by, bz)
    boxes = every.transpose(1, 3, 2, 4, 0, 5).reshape(grid_x * bx, grid_y * by, groups * bz)
    boxes = jnp.pad(boxes, 1)
    window = lax.dynamic_slice(
        boxes,
        (lax.axis_index("gx") * bx, lax.axis_index("gy") * by, lax.axis_index("grp") * bz),
        (bx + 2, by + 2, bz + 2),
    )
    lifted = jnp.repeat(jnp.repeat(jnp.repeat(window, BOX, axis=0), BOX, axis=1), BOX, axis=2)
    solution = jnp.where(mask, solution + (lifted - WEIGHT * op(lifted) / diagonal), 0.0)
    for sweep_number in range(NU):
        solution = jnp.where(mask, solution + WEIGHT * (src - op(solution)) / diagonal, 0.0)
    return (trimmed(solution), coarse_error)


def solution(mesh):
    return jax.shard_map(
        local,
        mesh=mesh,
        in_specs=(
            P("gx", "gy", "grp"),
            P("gx", "gy", "grp"),
            P("gx", "gy", "grp"),
            P("gx", "gy", "grp"),
            P(("grp", "gx", "gy"), None, None),
            P(("grp", "gx", "gy"), None),
        ),
        out_specs=(P("gx", "gy", "grp"), P(("grp", "gx", "gy"))),
        check_vma=False,
    )
```

```python
import jax
import jax.numpy as jnp
from jax import lax
from jax.sharding import PartitionSpec as P

NU = 2
CITER = 4
BOX = 4
HALO = 4

WEIGHT = 2.0 / 3.0
PAIRS = ((0, 1), (0, -1), (1, 1), (1, -1), (2, 1), (2, -1))


def exchange(cells, sides, width):
    for axis, dim in sides:
        count = lax.axis_size(axis)
        size = cells.shape[dim]
        head = lax.slice_in_dim(cells, 0, width, axis=dim)
        tail = lax.slice_in_dim(cells, size - width, size, axis=dim)
        if count == 1:
            before = jnp.zeros_like(tail)
            after = jnp.zeros_like(head)
        elif count == 2:
            index = lax.axis_index(axis)
            sent = jnp.where(index == 0, tail, head)
            got = lax.ppermute(sent, axis, [(0, 1), (1, 0)])
            before = jnp.where(index == 1, got, 0.0)
            after = jnp.where(index == 0, got, 0.0)
        else:
            before = lax.ppermute(tail, axis, [(i, i + 1) for i in range(count - 1)])
            after = lax.ppermute(head, axis, [(i + 1, i) for i in range(count - 1)])
        cells = jnp.concatenate([before, cells, after], axis=dim)
    return cells


def flat_shift(padded, rows, width, stride, dx, dy, dz):
    lead = stride + dy * stride + dz
    return padded[1 + dx:1 + dx + rows, lead:lead + width]


def neighbours(field, stride):
    rows, width = field.shape
    padded = jnp.pad(field, ((1, 1), (stride, stride)))
    steps = ((1, 0, 0), (-1, 0, 0), (0, 1, 0), (0, -1, 0), (0, 0, 1), (0, 0, -1))
    return [flat_shift(padded, rows, width, stride, *step) for step in steps]


def face_terms(conductance, stride):
    return [0.5 * (conductance + other) for other in neighbours(conductance, stride)]


def operate(field, storage, face_list, stride):
    summed = storage * field
    for face, other in zip(face_list, neighbours(field, stride)):
        summed = summed + face * (field - other)
    return summed


def inside_mask(rows, span_y, span_z):
    shape = (rows, span_y * span_z)
    column = lax.broadcasted_iota(jnp.int32, shape, 1)
    coords = (
        (lax.broadcasted_iota(jnp.int32, shape, 0), rows, "gx"),
        (column // span_z, span_y, "gy"),
        (column % span_z, span_z, "grp"),
    )
    mask = None
    for local_index, span, axis in coords:
        block = span - 2 * HALO
        where = lax.axis_index(axis) * block - HALO + local_index
        ok = (where >= 0) & (where < block * lax.axis_size(axis))
        mask = ok if mask is None else mask & ok
    return mask


def trimmed(flat, span_y, span_z):
    cube = flat.reshape(flat.shape[0], span_y, span_z)
    return cube[HALO:-HALO, HALO:-HALO, HALO:-HALO]


def grp_pool(vector):
    groups = lax.axis_size("grp")
    index = lax.axis_index("grp")
    parts = [vector]
    for step in range(1, groups):
        parts.append(lax.ppermute(vector, "grp", [(i, (i + step) % groups) for i in range(groups)]))
    stacked = jnp.stack(parts)
    order = (index - jnp.arange(groups)) % groups
    return jnp.take(stacked, order, axis=0)


def local(source, conductance, storage, aggregate_ids, coarse_values, coarse_columns):
    size_x, size_y, size_z = source.shape
    assert HALO == BOX and HALO >= 2 * NU and HALO >= NU + 2
    stacked = jnp.stack([source, conductance, storage])
    wide = exchange(stacked, (("gx", 1), ("gy", 2), ("grp", 3)), HALO)
    rows, span_y, span_z = wide.shape[1:]
    stride = span_z
    wide = wide.reshape(3, rows, span_y * span_z)
    src, cond, stor = wide[0], wide[1], wide[2]
    mask = inside_mask(rows, span_y, span_z)
    face_list = face_terms(cond, stride)
    diagonal = stor
    for position in range(6):
        diagonal = diagonal + face_list[position]

    def op(field):
        return operate(field, stor, face_list, stride)

    solution = jnp.where(mask, WEIGHT * src / diagonal, 0.0)
    for sweep_number in range(NU - 1):
        solution = jnp.where(mask, solution + WEIGHT * (src - op(solution)) / diagonal, 0.0)
    residual = src - op(solution)
    scaled = jnp.where(mask, residual / diagonal, 0.0)
    smoothed = trimmed(residual - WEIGHT * op(scaled), span_y, span_z)

    box_labels = aggregate_ids[::BOX, ::BOX, ::BOX].reshape(-1)
    box_totals = (
        smoothed.reshape(size_x // BOX, BOX, size_y // BOX, BOX, size_z // BOX, BOX)
        .sum(axis=(1, 3, 5))
        .reshape(-1)
    )
    coarse_rhs = jnp.zeros(box_totals.shape, source.dtype).at[box_labels].set(box_totals)
    coarse_diag = jnp.diagonal(coarse_values[:, :, :64], axis1=1, axis2=2).reshape(-1)
    block_rows = coarse_values.shape[0]
    grid_x = lax.axis_size("gx")
    grid_y = lax.axis_size("gy")
    groups = lax.axis_size("grp")
    within_ids = coarse_columns % block_rows
    device_ids = coarse_columns // block_rows
    target_y = device_ids % grid_y
    target_x = device_ids // grid_y % grid_x
    member_ids = device_ids // (grid_y * grid_x)
    delta_x = target_x - lax.axis_index("gx") + 1
    delta_y = target_y - lax.axis_index("gy") + 1
    local_columns = ((delta_x * 3 + delta_y) * groups + member_ids) * block_rows + within_ids
    coarse_error = coarse_rhs / coarse_diag
    for sweep_number in range(CITER - 1):
        pooled = grp_pool(coarse_error)
        beside_all = exchange(pooled.reshape(1, 1, -1), (("gx", 0), ("gy", 1)), 1)
        blocks = beside_all.reshape(-1, 64)[local_columns]
        blocks = blocks.reshape(blocks.shape[0], -1)
        applied = jnp.einsum(
            "bim,bm->bi", coarse_values, blocks, precision=lax.Precision.HIGHEST
        ).reshape(-1)
        coarse_error = coarse_error + (coarse_rhs - applied) / coarse_diag

    bx, by, bz = size_x // BOX, size_y // BOX, size_z // BOX
    small = coarse_error[box_labels].reshape(bx, by, bz)
    window = exchange(small, (("gx", 0), ("gy", 1), ("grp", 2)), 1)
    lifted = jnp.repeat(jnp.repeat(jnp.repeat(window, BOX, axis=0), BOX, axis=1), BOX, axis=2)
    lifted = lifted.reshape(rows, span_y * span_z)
    solution = jnp.where(mask, solution + (lifted - WEIGHT * op(lifted) / diagonal), 0.0)
    for sweep_number in range(NU):
        solution = jnp.where(mask, solution + WEIGHT * (src - op(solution)) / diagonal, 0.0)
    return (trimmed(solution, span_y, span_z), coarse_error)


def solution(mesh):
    return jax.shard_map(
        local,
        mesh=mesh,
        in_specs=(
            P("gx", "gy", "grp"),
            P("gx", "gy", "grp"),
            P("gx", "gy", "grp"),
            P("gx", "gy", "grp"),
            P(("grp", "gx", "gy"), None, None),
            P(("grp", "gx", "gy"), None),
        ),
        out_specs=(P("gx", "gy", "grp"), P(("grp", "gx", "gy"))),
        check_vma=False,
    )
```

```python
import jax
import jax.numpy as jnp
from jax import lax
from jax.sharding import PartitionSpec as P

NU = 2
CITER = 4
BOX = 4
HALO = 4

WEIGHT = 2.0 / 3.0
PAIRS = ((0, 1), (0, -1), (1, 1), (1, -1), (2, 1), (2, -1))


def exchange(cells, sides, width):
    for axis, dim in sides:
        count = lax.axis_size(axis)
        size = cells.shape[dim]
        head = lax.slice_in_dim(cells, 0, width, axis=dim)
        tail = lax.slice_in_dim(cells, size - width, size, axis=dim)
        if count == 1:
            before = jnp.zeros_like(tail)
            after = jnp.zeros_like(head)
        elif count == 2:
            index = lax.axis_index(axis)
            sent = jnp.where(index == 0, tail, head)
            got = lax.ppermute(sent, axis, [(0, 1), (1, 0)])
            before = jnp.where(index == 1, got, 0.0)
            after = jnp.where(index == 0, got, 0.0)
        else:
            before = lax.ppermute(tail, axis, [(i, i + 1) for i in range(count - 1)])
            after = lax.ppermute(head, axis, [(i + 1, i) for i in range(count - 1)])
        cells = jnp.concatenate([before, cells, after], axis=dim)
    return cells


def flat_shift(padded, rows, width, stride, dx, dy, dz):
    lead = stride + dy * stride + dz
    return padded[1 + dx:1 + dx + rows, lead:lead + width]


def neighbours(field, stride):
    rows, width = field.shape
    padded = jnp.pad(field, ((1, 1), (stride, stride)))
    steps = ((1, 0, 0), (-1, 0, 0), (0, 1, 0), (0, -1, 0), (0, 0, 1), (0, 0, -1))
    return [flat_shift(padded, rows, width, stride, *step) for step in steps]


def face_terms(conductance, stride):
    return [0.5 * (conductance + other) for other in neighbours(conductance, stride)]


def operate(field, storage, face_list, stride):
    summed = storage * field
    for face, other in zip(face_list, neighbours(field, stride)):
        summed = summed + face * (field - other)
    return summed


def inside_mask(rows, span_y, span_z):
    shape = (rows, span_y * span_z)
    column = lax.broadcasted_iota(jnp.int32, shape, 1)
    coords = (
        (lax.broadcasted_iota(jnp.int32, shape, 0), rows, "gx"),
        (column // span_z, span_y, "gy"),
        (column % span_z, span_z, "grp"),
    )
    mask = None
    for local_index, span, axis in coords:
        block = span - 2 * HALO
        where = lax.axis_index(axis) * block - HALO + local_index
        ok = (where >= 0) & (where < block * lax.axis_size(axis))
        mask = ok if mask is None else mask & ok
    return mask


def trimmed(flat, span_y, span_z):
    cube = flat.reshape(flat.shape[0], span_y, span_z)
    return cube[HALO:-HALO, HALO:-HALO, HALO:-HALO]


def grp_pool(vector):
    groups = lax.axis_size("grp")
    index = lax.axis_index("grp")
    parts = [vector]
    for step in range(1, groups):
        parts.append(lax.ppermute(vector, "grp", [(i, (i + step) % groups) for i in range(groups)]))
    stacked = jnp.stack(parts)
    order = (index - jnp.arange(groups)) % groups
    return jnp.take(stacked, order, axis=0)


def dot(left, right):
    return jnp.dot(left, right, precision=lax.Precision.HIGHEST)


def box_matrix(boxes, cells, stride, offset, live, inner=None):
    box = lax.broadcasted_iota(jnp.int32, (boxes, cells), 0)
    cell = lax.broadcasted_iota(jnp.int32, (boxes, cells), 1)
    if inner is None:
        hit = (cell - offset >= box * BOX) & (cell - offset < box * BOX + BOX)
    else:
        outer_cell, inner_cell = cell // stride - offset, cell % stride - offset
        outer_box, inner_box = box // inner, box % inner
        hit = (outer_cell >= outer_box * BOX) & (outer_cell < outer_box * BOX + BOX)
        hit = hit & (inner_cell >= inner_box * BOX) & (inner_cell < inner_box * BOX + BOX)
    return (hit & live).astype(jnp.float32)


def local(source, conductance, storage, aggregate_ids, coarse_values, coarse_columns):
    size_x, size_y, size_z = source.shape
    assert HALO == BOX and HALO >= 2 * NU and HALO >= NU + 2
    stacked = jnp.stack([source, conductance, storage])
    wide = exchange(stacked, (("grp", 3),), HALO)
    span_z = wide.shape[3]
    stride = span_z
    wide = wide.reshape(3, size_x, size_y * span_z)
    wide = exchange(wide, (("gy", 2),), HALO * span_z)
    wide = exchange(wide, (("gx", 1),), HALO)
    rows = wide.shape[1]
    span_y = wide.shape[2] // span_z
    src, cond, stor = wide[0], wide[1], wide[2]
    mask = inside_mask(rows, span_y, span_z)
    face_list = face_terms(cond, stride)
    diagonal = stor
    for position in range(6):
        diagonal = diagonal + face_list[position]

    def op(field):
        return operate(field, stor, face_list, stride)

    solution = jnp.where(mask, WEIGHT * src / diagonal, 0.0)
    for sweep_number in range(NU - 1):
        solution = jnp.where(mask, solution + WEIGHT * (src - op(solution)) / diagonal, 0.0)
    residual = src - op(solution)
    scaled = jnp.where(mask, residual / diagonal, 0.0)
    smoothed = residual - WEIGHT * op(scaled)

    bx, by, bz = size_x // BOX, size_y // BOX, size_z // BOX
    live = lax.axis_index("grp") >= 0
    pick_x = box_matrix(bx, rows, 1, HALO, live)
    pick_yz = box_matrix(by * bz, span_y * span_z, span_z, HALO, live, bz).T
    box_totals = dot(pick_x, dot(smoothed, pick_yz)).reshape(-1)
    box_labels = aggregate_ids[::BOX, ::BOX, ::BOX].reshape(-1)
    placed = (
        box_labels[:, None] == lax.broadcasted_iota(jnp.int32, (box_labels.shape[0],) * 2, 1)
    ).astype(source.dtype)
    coarse_rhs = dot(box_totals[None, :], placed)[0]
    coarse_diag = jnp.diagonal(coarse_values[:, :, :64], axis1=1, axis2=2).reshape(-1)
    block_rows = coarse_values.shape[0]
    grid_x = lax.axis_size("gx")
    grid_y = lax.axis_size("gy")
    groups = lax.axis_size("grp")
    within_ids = coarse_columns % block_rows
    device_ids = coarse_columns // block_rows
    target_y = device_ids % grid_y
    target_x = device_ids // grid_y % grid_x
    member_ids = device_ids // (grid_y * grid_x)
    delta_x = target_x - lax.axis_index("gx") + 1
    delta_y = target_y - lax.axis_index("gy") + 1
    local_columns = ((delta_x * 3 + delta_y) * groups + member_ids) * block_rows + within_ids
    coarse_error = coarse_rhs / coarse_diag
    for sweep_number in range(CITER - 1):
        pooled = grp_pool(coarse_error)
        beside_all = exchange(pooled.reshape(1, 1, -1), (("gx", 0), ("gy", 1)), 1)
        blocks = beside_all.reshape(-1, 64)[local_columns]
        blocks = blocks.reshape(blocks.shape[0], -1)
        applied = jnp.einsum(
            "bim,bm->bi", coarse_values, blocks, precision=lax.Precision.HIGHEST
        ).reshape(-1)
        coarse_error = coarse_error + (coarse_rhs - applied) / coarse_diag

    small = dot(placed, coarse_error[:, None]).reshape(bx, by, bz)
    window = exchange(small, (("gx", 0), ("gy", 1), ("grp", 2)), 1)
    window = window.reshape(bx + 2, (by + 2) * (bz + 2))
    spread_x = box_matrix(bx + 2, rows, 1, 0, live).T
    spread_yz = box_matrix((by + 2) * (bz + 2), span_y * span_z, span_z, 0, live, bz + 2)
    lifted = dot(spread_x, dot(window, spread_yz))
    solution = jnp.where(mask, solution + (lifted - WEIGHT * op(lifted) / diagonal), 0.0)
    for sweep_number in range(NU):
        solution = jnp.where(mask, solution + WEIGHT * (src - op(solution)) / diagonal, 0.0)
    return (trimmed(solution, span_y, span_z), coarse_error)


def solution(mesh):
    return jax.shard_map(
        local,
        mesh=mesh,
        in_specs=(
            P("gx", "gy", "grp"),
            P("gx", "gy", "grp"),
            P("gx", "gy", "grp"),
            P("gx", "gy", "grp"),
            P(("grp", "gx", "gy"), None, None),
            P(("grp", "gx", "gy"), None),
        ),
        out_specs=(P("gx", "gy", "grp"), P(("grp", "gx", "gy"))),
        check_vma=False,
    )
```

```python
import jax
import jax.numpy as jnp
from jax import lax
from jax.sharding import PartitionSpec as P

NU = 2
CITER = 4
BOX = 4
HALO = 4

WEIGHT = 2.0 / 3.0
PAIRS = ((0, 1), (0, -1), (1, 1), (1, -1), (2, 1), (2, -1))


def exchange(cells, sides, width):
    for axis, dim in sides:
        count = lax.axis_size(axis)
        size = cells.shape[dim]
        head = lax.slice_in_dim(cells, 0, width, axis=dim)
        tail = lax.slice_in_dim(cells, size - width, size, axis=dim)
        if count == 1:
            before = jnp.zeros_like(tail)
            after = jnp.zeros_like(head)
        elif count == 2:
            index = lax.axis_index(axis)
            sent = jnp.where(index == 0, tail, head)
            got = lax.ppermute(sent, axis, [(0, 1), (1, 0)])
            before = jnp.where(index == 1, got, 0.0)
            after = jnp.where(index == 0, got, 0.0)
        else:
            before = lax.ppermute(tail, axis, [(i, i + 1) for i in range(count - 1)])
            after = lax.ppermute(head, axis, [(i + 1, i) for i in range(count - 1)])
        cells = jnp.concatenate([before, cells, after], axis=dim)
    return cells


def flat_shift(padded, rows, width, stride, dx, dy, dz):
    lead = stride + dy * stride + dz
    return padded[1 + dx:1 + dx + rows, lead:lead + width]


def neighbours(field, stride):
    rows, width = field.shape
    padded = jnp.pad(field, ((1, 1), (stride, stride)))
    steps = ((1, 0, 0), (-1, 0, 0), (0, 1, 0), (0, -1, 0), (0, 0, 1), (0, 0, -1))
    return [flat_shift(padded, rows, width, stride, *step) for step in steps]


def face_terms(conductance, stride):
    return [0.5 * (conductance + other) for other in neighbours(conductance, stride)]


def operate(field, storage, face_list, stride):
    summed = storage * field
    for face, other in zip(face_list, neighbours(field, stride)):
        summed = summed + face * (field - other)
    return summed


def inside_mask(rows, span_y, span_z):
    shape = (rows, span_y * span_z)
    column = lax.broadcasted_iota(jnp.int32, shape, 1)
    coords = (
        (lax.broadcasted_iota(jnp.int32, shape, 0), rows, "gx"),
        (column // span_z, span_y, "gy"),
        (column % span_z, span_z, "grp"),
    )
    mask = None
    for local_index, span, axis in coords:
        block = span - 2 * HALO
        where = lax.axis_index(axis) * block - HALO + local_index
        ok = (where >= 0) & (where < block * lax.axis_size(axis))
        mask = ok if mask is None else mask & ok
    return mask


def trimmed(flat, span_y, span_z):
    cube = flat.reshape(flat.shape[0], span_y, span_z)
    return cube[HALO:-HALO, HALO:-HALO, HALO:-HALO]


def grp_pool(vector):
    groups = lax.axis_size("grp")
    index = lax.axis_index("grp")
    parts = [vector]
    for step in range(1, groups):
        parts.append(lax.ppermute(vector, "grp", [(i, (i + step) % groups) for i in range(groups)]))
    stacked = jnp.stack(parts)
    order = (index - jnp.arange(groups)) % groups
    return jnp.take(stacked, order, axis=0)


def dot(left, right):
    return jnp.dot(left, right, precision=lax.Precision.HIGHEST)


def box_matrix(boxes, cells, stride, offset, live, inner=None):
    box = lax.broadcasted_iota(jnp.int32, (boxes, cells), 0)
    cell = lax.broadcasted_iota(jnp.int32, (boxes, cells), 1)
    if inner is None:
        hit = (cell - offset >= box * BOX) & (cell - offset < box * BOX + BOX)
    else:
        outer_cell, inner_cell = cell // stride - offset, cell % stride - offset
        outer_box, inner_box = box // inner, box % inner
        hit = (outer_cell >= outer_box * BOX) & (outer_cell < outer_box * BOX + BOX)
        hit = hit & (inner_cell >= inner_box * BOX) & (inner_cell < inner_box * BOX + BOX)
    return (hit & live).astype(jnp.float32)


def neighbourhood(block):
    size_x, size_y = lax.axis_size("gx"), lax.axis_size("gy")
    index_y = lax.axis_index("gy")
    axes = ("gx", "gy")

    def pairs_for(dx, dy_of):
        pairs = []
        for x in range(size_x):
            for y in range(size_y):
                sx, sy = x + dx, dy_of(y)
                if 0 <= sx < size_x and 0 <= sy < size_y:
                    pairs.append((sx * size_y + sy, x * size_y + y))
        return pairs

    def sent(pairs):
        return lax.ppermute(block, axes, pairs) if pairs else jnp.zeros_like(block)

    slots = {(0, 0): block}
    for dx in (-1, 0, 1):
        if size_y == 2:
            got = sent(pairs_for(dx, lambda y: 1 - y))
            slots[(dx, 1)] = jnp.where(index_y == 0, got, 0.0)
            slots[(dx, -1)] = jnp.where(index_y == 1, got, 0.0)
            if dx != 0:
                slots[(dx, 0)] = sent(pairs_for(dx, lambda y: y))
        else:
            for dy in (-1, 0, 1):
                if (dx, dy) != (0, 0):
                    slots[(dx, dy)] = sent(pairs_for(dx, lambda y, dy=dy: y + dy))
    return jnp.stack([jnp.stack([slots[(dx, dy)] for dy in (-1, 0, 1)]) for dx in (-1, 0, 1)])


def local(source, conductance, storage, aggregate_ids, coarse_values, coarse_columns):
    size_x, size_y, size_z = source.shape
    assert HALO == BOX and HALO >= 2 * NU and HALO >= NU + 2
    stacked = jnp.stack([source, conductance, storage])
    wide = exchange(stacked, (("grp", 3),), HALO)
    span_z = wide.shape[3]
    stride = span_z
    wide = wide.reshape(3, size_x, size_y * span_z)
    wide = exchange(wide, (("gy", 2),), HALO * span_z)
    wide = exchange(wide, (("gx", 1),), HALO)
    rows = wide.shape[1]
    span_y = wide.shape[2] // span_z
    src, cond, stor = wide[0], wide[1], wide[2]
    mask = inside_mask(rows, span_y, span_z)
    face_list = face_terms(cond, stride)
    diagonal = stor
    for position in range(6):
        diagonal = diagonal + face_list[position]

    def op(field):
        return operate(field, stor, face_list, stride)

    solution = jnp.where(mask, WEIGHT * src / diagonal, 0.0)
    for sweep_number in range(NU - 1):
        solution = jnp.where(mask, solution + WEIGHT * (src - op(solution)) / diagonal, 0.0)
    residual = src - op(solution)
    scaled = jnp.where(mask, residual / diagonal, 0.0)
    smoothed = residual - WEIGHT * op(scaled)

    bx, by, bz = size_x // BOX, size_y // BOX, size_z // BOX
    live = lax.axis_index("grp") >= 0
    pick_x = box_matrix(bx, rows, 1, HALO, live)
    pick_yz = box_matrix(by * bz, span_y * span_z, span_z, HALO, live, bz).T
    box_totals = dot(pick_x, dot(smoothed, pick_yz)).reshape(-1)
    box_labels = aggregate_ids[::BOX, ::BOX, ::BOX].reshape(-1)
    placed = (
        box_labels[:, None] == lax.broadcasted_iota(jnp.int32, (box_labels.shape[0],) * 2, 1)
    ).astype(source.dtype)
    coarse_rhs = dot(box_totals[None, :], placed)[0]
    coarse_diag = jnp.diagonal(coarse_values[:, :, :64], axis1=1, axis2=2).reshape(-1)
    block_rows = coarse_values.shape[0]
    grid_x = lax.axis_size("gx")
    grid_y = lax.axis_size("gy")
    groups = lax.axis_size("grp")
    within_ids = coarse_columns % block_rows
    device_ids = coarse_columns // block_rows
    target_y = device_ids % grid_y
    target_x = device_ids // grid_y % grid_x
    member_ids = device_ids // (grid_y * grid_x)
    delta_x = target_x - lax.axis_index("gx") + 1
    delta_y = target_y - lax.axis_index("gy") + 1
    local_columns = ((delta_x * 3 + delta_y) * groups + member_ids) * block_rows + within_ids
    rhs_blocks = coarse_rhs.reshape(block_rows, 64)
    diag_blocks = coarse_diag.reshape(block_rows, 64)
    tables = 9 * groups * block_rows
    pick = (
        local_columns.reshape(-1, 1) == lax.broadcasted_iota(jnp.int32, (local_columns.size, tables), 1)
    ).astype(source.dtype)
    error_blocks = rhs_blocks / diag_blocks
    for sweep_number in range(CITER - 1):
        pooled = grp_pool(error_blocks)
        table = neighbourhood(pooled).reshape(tables, 64)
        blocks = dot(pick, table).reshape(block_rows, -1)
        applied = jnp.einsum(
            "bim,bm->bi", coarse_values, blocks, precision=lax.Precision.HIGHEST
        )
        error_blocks = error_blocks + (rhs_blocks - applied) / diag_blocks
    coarse_error = error_blocks.reshape(-1)

    small = dot(placed, coarse_error[:, None]).reshape(bx, by, bz)
    small = exchange(small, (("grp", 2),), 1)
    around = neighbourhood(small).transpose(0, 2, 1, 3, 4).reshape(3 * bx, 3 * by, bz + 2)
    window = around[bx - 1:2 * bx + 1, by - 1:2 * by + 1]
    window = window.reshape(bx + 2, (by + 2) * (bz + 2))
    spread_x = box_matrix(bx + 2, rows, 1, 0, live).T
    spread_yz = box_matrix((by + 2) * (bz + 2), span_y * span_z, span_z, 0, live, bz + 2)
    lifted = dot(spread_x, dot(window, spread_yz))
    solution = jnp.where(mask, solution + (lifted - WEIGHT * op(lifted) / diagonal), 0.0)
    for sweep_number in range(NU):
        solution = jnp.where(mask, solution + WEIGHT * (src - op(solution)) / diagonal, 0.0)
    return (trimmed(solution, span_y, span_z), coarse_error)


def solution(mesh):
    return jax.shard_map(
        local,
        mesh=mesh,
        in_specs=(
            P("gx", "gy", "grp"),
            P("gx", "gy", "grp"),
            P("gx", "gy", "grp"),
            P("gx", "gy", "grp"),
            P(("grp", "gx", "gy"), None, None),
            P(("grp", "gx", "gy"), None),
        ),
        out_specs=(P("gx", "gy", "grp"), P(("grp", "gx", "gy"))),
        check_vma=False,
    )
```

```python
import jax
import jax.numpy as jnp
from jax import lax
from jax.sharding import PartitionSpec as P

NU = 2
CITER = 4
BOX = 4
HALO = 4

WEIGHT = 2.0 / 3.0
ALL_AXES = ("grp", "gx", "gy")
PAIRS = ((0, 1), (0, -1), (1, 1), (1, -1), (2, 1), (2, -1))


def exchange(cells, sides, width):
    for axis, dim in sides:
        count = lax.axis_size(axis)
        size = cells.shape[dim]
        head = lax.slice_in_dim(cells, 0, width, axis=dim)
        tail = lax.slice_in_dim(cells, size - width, size, axis=dim)
        if count == 1:
            before = jnp.zeros_like(tail)
            after = jnp.zeros_like(head)
        elif count == 2:
            index = lax.axis_index(axis)
            sent = jnp.where(index == 0, tail, head)
            got = lax.ppermute(sent, axis, [(0, 1), (1, 0)])
            before = jnp.where(index == 1, got, 0.0)
            after = jnp.where(index == 0, got, 0.0)
        else:
            before = lax.ppermute(tail, axis, [(i, i + 1) for i in range(count - 1)])
            after = lax.ppermute(head, axis, [(i + 1, i) for i in range(count - 1)])
        cells = jnp.concatenate([before, cells, after], axis=dim)
    return cells


def flat_shift(padded, rows, width, stride, dx, dy, dz):
    lead = stride + dy * stride + dz
    return padded[1 + dx:1 + dx + rows, lead:lead + width]


def neighbours(field, stride):
    rows, width = field.shape
    padded = jnp.pad(field, ((1, 1), (stride, stride)))
    steps = ((1, 0, 0), (-1, 0, 0), (0, 1, 0), (0, -1, 0), (0, 0, 1), (0, 0, -1))
    return [flat_shift(padded, rows, width, stride, *step) for step in steps]


def face_terms(conductance, stride):
    return [0.5 * (conductance + other) for other in neighbours(conductance, stride)]


def operate(field, storage, face_list, stride):
    summed = storage * field
    for face, other in zip(face_list, neighbours(field, stride)):
        summed = summed + face * (field - other)
    return summed


def inside_mask(rows, span_y, span_z):
    shape = (rows, span_y * span_z)
    column = lax.broadcasted_iota(jnp.int32, shape, 1)
    coords = (
        (lax.broadcasted_iota(jnp.int32, shape, 0), rows, "gx"),
        (column // span_z, span_y, "gy"),
        (column % span_z, span_z, "grp"),
    )
    mask = None
    for local_index, span, axis in coords:
        block = span - 2 * HALO
        where = lax.axis_index(axis) * block - HALO + local_index
        ok = (where >= 0) & (where < block * lax.axis_size(axis))
        mask = ok if mask is None else mask & ok
    return mask


def trimmed(flat, span_y, span_z):
    cube = flat.reshape(flat.shape[0], span_y, span_z)
    return cube[HALO:-HALO, HALO:-HALO, HALO:-HALO]


def grp_pool(vector):
    groups = lax.axis_size("grp")
    index = lax.axis_index("grp")
    parts = [vector]
    for step in range(1, groups):
        parts.append(lax.ppermute(vector, "grp", [(i, (i + step) % groups) for i in range(groups)]))
    stacked = jnp.stack(parts)
    order = (index - jnp.arange(groups)) % groups
    return jnp.take(stacked, order, axis=0)


def dot(left, right):
    return jnp.dot(left, right, precision=lax.Precision.HIGHEST)


def box_matrix(boxes, cells, stride, offset, live, inner=None):
    box = lax.broadcasted_iota(jnp.int32, (boxes, cells), 0)
    cell = lax.broadcasted_iota(jnp.int32, (boxes, cells), 1)
    if inner is None:
        hit = (cell - offset >= box * BOX) & (cell - offset < box * BOX + BOX)
    else:
        outer_cell, inner_cell = cell // stride - offset, cell % stride - offset
        outer_box, inner_box = box // inner, box % inner
        hit = (outer_cell >= outer_box * BOX) & (outer_cell < outer_box * BOX + BOX)
        hit = hit & (inner_cell >= inner_box * BOX) & (inner_cell < inner_box * BOX + BOX)
    return (hit & live).astype(jnp.float32)


def everyone(vector):
    count = lax.axis_size(ALL_AXES)
    copies = jnp.broadcast_to(vector[None], (count,) + vector.shape)
    return lax.all_to_all(copies, ALL_AXES, 0, 0, tiled=True).reshape(-1)


def local(source, conductance, storage, aggregate_ids, coarse_values, coarse_columns):
    size_x, size_y, size_z = source.shape
    assert HALO == BOX and HALO >= 2 * NU and HALO >= NU + 2
    stacked = jnp.stack([source, conductance, storage])
    wide = exchange(stacked, (("grp", 3),), HALO)
    span_z = wide.shape[3]
    stride = span_z
    wide = wide.reshape(3, size_x, size_y * span_z)
    wide = exchange(wide, (("gy", 2),), HALO * span_z)
    wide = exchange(wide, (("gx", 1),), HALO)
    rows = wide.shape[1]
    span_y = wide.shape[2] // span_z
    src, cond, stor = wide[0], wide[1], wide[2]
    mask = inside_mask(rows, span_y, span_z)
    face_list = face_terms(cond, stride)
    diagonal = stor
    for position in range(6):
        diagonal = diagonal + face_list[position]

    def op(field):
        return operate(field, stor, face_list, stride)

    solution = jnp.where(mask, WEIGHT * src / diagonal, 0.0)
    for sweep_number in range(NU - 1):
        solution = jnp.where(mask, solution + WEIGHT * (src - op(solution)) / diagonal, 0.0)
    residual = src - op(solution)
    scaled = jnp.where(mask, residual / diagonal, 0.0)
    smoothed = residual - WEIGHT * op(scaled)

    bx, by, bz = size_x // BOX, size_y // BOX, size_z // BOX
    live = lax.axis_index("grp") >= 0
    pick_x = box_matrix(bx, rows, 1, HALO, live)
    pick_yz = box_matrix(by * bz, span_y * span_z, span_z, HALO, live, bz).T
    box_totals = dot(pick_x, dot(smoothed, pick_yz)).reshape(-1)
    box_labels = aggregate_ids[::BOX, ::BOX, ::BOX].reshape(-1)
    placed = (
        box_labels[:, None] == lax.broadcasted_iota(jnp.int32, (box_labels.shape[0],) * 2, 1)
    ).astype(source.dtype)
    coarse_rhs = dot(box_totals[None, :], placed)[0]
    coarse_diag = jnp.diagonal(coarse_values[:, :, :64], axis1=1, axis2=2).reshape(-1)
    block_rows = coarse_values.shape[0]
    grid_x = lax.axis_size("gx")
    grid_y = lax.axis_size("gy")
    groups = lax.axis_size("grp")
    coarse_error = coarse_rhs / coarse_diag
    for sweep_number in range(CITER - 1):
        pooled = everyone(coarse_error)
        blocks = pooled.reshape(-1, 64)[coarse_columns]
        blocks = blocks.reshape(block_rows, -1)
        applied = jnp.einsum(
            "bim,bm->bi", coarse_values, blocks, precision=lax.Precision.HIGHEST
        ).reshape(-1)
        coarse_error = coarse_error + (coarse_rhs - applied) / coarse_diag

    small = dot(placed, coarse_error[:, None]).reshape(-1)
    every = everyone(small).reshape(groups, grid_x, grid_y, bx, by, bz)
    boxes = every.transpose(1, 3, 2, 4, 0, 5).reshape(grid_x * bx, grid_y * by, groups * bz)
    boxes = jnp.pad(boxes, 1)
    window = lax.dynamic_slice(
        boxes,
        (lax.axis_index("gx") * bx, lax.axis_index("gy") * by, lax.axis_index("grp") * bz),
        (bx + 2, by + 2, bz + 2),
    )
    window = window.reshape(bx + 2, (by + 2) * (bz + 2))
    spread_x = box_matrix(bx + 2, rows, 1, 0, live).T
    spread_yz = box_matrix((by + 2) * (bz + 2), span_y * span_z, span_z, 0, live, bz + 2)
    lifted = dot(spread_x, dot(window, spread_yz))
    solution = jnp.where(mask, solution + (lifted - WEIGHT * op(lifted) / diagonal), 0.0)
    for sweep_number in range(NU):
        solution = jnp.where(mask, solution + WEIGHT * (src - op(solution)) / diagonal, 0.0)
    return (trimmed(solution, span_y, span_z), coarse_error)


def solution(mesh):
    return jax.shard_map(
        local,
        mesh=mesh,
        in_specs=(
            P("gx", "gy", "grp"),
            P("gx", "gy", "grp"),
            P("gx", "gy", "grp"),
            P("gx", "gy", "grp"),
            P(("grp", "gx", "gy"), None, None),
            P(("grp", "gx", "gy"), None),
        ),
        out_specs=(P("gx", "gy", "grp"), P(("grp", "gx", "gy"))),
        check_vma=False,
    )
```

```python
import jax
import jax.numpy as jnp
from jax import lax
from jax.sharding import PartitionSpec as P

NU = 2
CITER = 4
BOX = 4
HALO = 4

WEIGHT = 2.0 / 3.0
ALL_AXES = ("grp", "gx", "gy")
PAIRS = ((0, 1), (0, -1), (1, 1), (1, -1), (2, 1), (2, -1))


def exchange(cells, sides, width):
    for axis, dim in sides:
        count = lax.axis_size(axis)
        size = cells.shape[dim]
        head = lax.slice_in_dim(cells, 0, width, axis=dim)
        tail = lax.slice_in_dim(cells, size - width, size, axis=dim)
        if count == 1:
            before = jnp.zeros_like(tail)
            after = jnp.zeros_like(head)
        elif count == 2:
            index = lax.axis_index(axis)
            sent = jnp.where(index == 0, tail, head)
            got = lax.ppermute(sent, axis, [(0, 1), (1, 0)])
            before = jnp.where(index == 1, got, 0.0)
            after = jnp.where(index == 0, got, 0.0)
        else:
            before = lax.ppermute(tail, axis, [(i, i + 1) for i in range(count - 1)])
            after = lax.ppermute(head, axis, [(i + 1, i) for i in range(count - 1)])
        cells = jnp.concatenate([before, cells, after], axis=dim)
    return cells


def flat_shift(padded, rows, width, stride, dx, dy, dz):
    lead = stride + dy * stride + dz
    return padded[1 + dx:1 + dx + rows, lead:lead + width]


def neighbours(field, stride):
    rows, width = field.shape
    padded = jnp.pad(field, ((1, 1), (stride, stride)))
    steps = ((1, 0, 0), (-1, 0, 0), (0, 1, 0), (0, -1, 0), (0, 0, 1), (0, 0, -1))
    return [flat_shift(padded, rows, width, stride, *step) for step in steps]


def face_terms(conductance, stride):
    return [0.5 * (conductance + other) for other in neighbours(conductance, stride)]


def operate(field, storage, face_list, stride):
    summed = storage * field
    for face, other in zip(face_list, neighbours(field, stride)):
        summed = summed + face * (field - other)
    return summed


def inside_mask(rows, span_y, span_z):
    shape = (rows, span_y * span_z)
    column = lax.broadcasted_iota(jnp.int32, shape, 1)
    coords = (
        (lax.broadcasted_iota(jnp.int32, shape, 0), rows, "gx"),
        (column // span_z, span_y, "gy"),
        (column % span_z, span_z, "grp"),
    )
    mask = None
    for local_index, span, axis in coords:
        block = span - 2 * HALO
        where = lax.axis_index(axis) * block - HALO + local_index
        ok = (where >= 0) & (where < block * lax.axis_size(axis))
        mask = ok if mask is None else mask & ok
    return mask


def trimmed(flat, span_y, span_z):
    cube = flat.reshape(flat.shape[0], span_y, span_z)
    return cube[HALO:-HALO, HALO:-HALO, HALO:-HALO]


def grp_pool(vector):
    groups = lax.axis_size("grp")
    index = lax.axis_index("grp")
    parts = [vector]
    for step in range(1, groups):
        parts.append(lax.ppermute(vector, "grp", [(i, (i + step) % groups) for i in range(groups)]))
    stacked = jnp.stack(parts)
    order = (index - jnp.arange(groups)) % groups
    return jnp.take(stacked, order, axis=0)


def dot(left, right):
    return jnp.dot(left, right, precision=lax.Precision.HIGHEST)


def box_matrix(boxes, cells, stride, offset, live, inner=None):
    box = lax.broadcasted_iota(jnp.int32, (boxes, cells), 0)
    cell = lax.broadcasted_iota(jnp.int32, (boxes, cells), 1)
    if inner is None:
        hit = (cell - offset >= box * BOX) & (cell - offset < box * BOX + BOX)
    else:
        outer_cell, inner_cell = cell // stride - offset, cell % stride - offset
        outer_box, inner_box = box // inner, box % inner
        hit = (outer_cell >= outer_box * BOX) & (outer_cell < outer_box * BOX + BOX)
        hit = hit & (inner_cell >= inner_box * BOX) & (inner_cell < inner_box * BOX + BOX)
    return (hit & live).astype(jnp.float32)


def everyone(vector):
    count = lax.axis_size(ALL_AXES)
    copies = jnp.broadcast_to(vector[None], (count,) + vector.shape)
    return lax.all_to_all(copies, ALL_AXES, 0, 0, tiled=True)


def local(source, conductance, storage, aggregate_ids, coarse_values, coarse_columns):
    size_x, size_y, size_z = source.shape
    assert HALO == BOX and HALO >= 2 * NU and HALO >= NU + 2
    stacked = jnp.stack([source, conductance, storage])
    wide = exchange(stacked, (("grp", 3),), HALO)
    span_z = wide.shape[3]
    stride = span_z
    wide = wide.reshape(3, size_x, size_y * span_z)
    wide = exchange(wide, (("gy", 2),), HALO * span_z)
    wide = exchange(wide, (("gx", 1),), HALO)
    rows = wide.shape[1]
    span_y = wide.shape[2] // span_z
    src, cond, stor = wide[0], wide[1], wide[2]
    mask = inside_mask(rows, span_y, span_z)
    face_list = face_terms(cond, stride)
    diagonal = stor
    for position in range(6):
        diagonal = diagonal + face_list[position]

    def op(field):
        return operate(field, stor, face_list, stride)

    solution = jnp.where(mask, WEIGHT * src / diagonal, 0.0)
    for sweep_number in range(NU - 1):
        solution = jnp.where(mask, solution + WEIGHT * (src - op(solution)) / diagonal, 0.0)
    residual = src - op(solution)
    scaled = jnp.where(mask, residual / diagonal, 0.0)
    smoothed = residual - WEIGHT * op(scaled)

    bx, by, bz = size_x // BOX, size_y // BOX, size_z // BOX
    live = lax.axis_index("grp") >= 0
    pick_x = box_matrix(bx, rows, 1, HALO, live)
    pick_yz = box_matrix(by * bz, span_y * span_z, span_z, HALO, live, bz).T
    box_totals = dot(pick_x, dot(smoothed, pick_yz)).reshape(-1)
    box_labels = aggregate_ids[::BOX, ::BOX, ::BOX].reshape(-1)
    placed = (
        box_labels[:, None] == lax.broadcasted_iota(jnp.int32, (box_labels.shape[0],) * 2, 1)
    ).astype(source.dtype)
    coarse_rhs = dot(box_totals[None, :], placed)[0]
    block_rows = coarse_values.shape[0]
    leading = coarse_values[:, :, :64]
    eye = lax.broadcasted_iota(jnp.int32, (64, 64), 0) == lax.broadcasted_iota(jnp.int32, (64, 64), 1)
    diag_blocks = jnp.sum(jnp.where(eye[None], leading, 0.0), axis=2)
    rhs_blocks = coarse_rhs.reshape(block_rows, 64)
    grid_x = lax.axis_size("gx")
    grid_y = lax.axis_size("gy")
    groups = lax.axis_size("grp")
    tables = groups * grid_x * grid_y * block_rows
    pick = (
        coarse_columns.reshape(-1, 1) == lax.broadcasted_iota(jnp.int32, (coarse_columns.size, tables), 1)
    ).astype(source.dtype)
    error_blocks = rhs_blocks / diag_blocks
    for sweep_number in range(CITER - 1):
        table = everyone(error_blocks).reshape(tables, 64)
        blocks = dot(pick, table).reshape(block_rows, -1)
        applied = jnp.einsum(
            "bim,bm->bi", coarse_values, blocks, precision=lax.Precision.HIGHEST
        )
        error_blocks = error_blocks + (rhs_blocks - applied) / diag_blocks
    coarse_error = error_blocks.reshape(-1)

    small = dot(placed, coarse_error[:, None]).reshape(bx * by, bz)
    every = everyone(small).reshape(groups, grid_x, grid_y, bx, by, bz)
    boxes = every.transpose(1, 3, 2, 4, 0, 5).reshape(grid_x * bx, grid_y * by, groups * bz)
    boxes = jnp.pad(boxes, 1)
    window = lax.dynamic_slice(
        boxes,
        (lax.axis_index("gx") * bx, lax.axis_index("gy") * by, lax.axis_index("grp") * bz),
        (bx + 2, by + 2, bz + 2),
    )
    window = window.reshape(bx + 2, (by + 2) * (bz + 2))
    spread_x = box_matrix(bx + 2, rows, 1, 0, live).T
    spread_yz = box_matrix((by + 2) * (bz + 2), span_y * span_z, span_z, 0, live, bz + 2)
    lifted = dot(spread_x, dot(window, spread_yz))
    solution = jnp.where(mask, solution + (lifted - WEIGHT * op(lifted) / diagonal), 0.0)
    for sweep_number in range(NU):
        solution = jnp.where(mask, solution + WEIGHT * (src - op(solution)) / diagonal, 0.0)
    return (trimmed(solution, span_y, span_z), coarse_error)


def solution(mesh):
    return jax.shard_map(
        local,
        mesh=mesh,
        in_specs=(
            P("gx", "gy", "grp"),
            P("gx", "gy", "grp"),
            P("gx", "gy", "grp"),
            P("gx", "gy", "grp"),
            P(("grp", "gx", "gy"), None, None),
            P(("grp", "gx", "gy"), None),
        ),
        out_specs=(P("gx", "gy", "grp"), P(("grp", "gx", "gy"))),
        check_vma=False,
    )
```

```python
import jax
import jax.numpy as jnp
from jax import lax
from jax.sharding import PartitionSpec as P

NU = 2
CITER = 4
BOX = 4
HALO = 4

WEIGHT = 2.0 / 3.0
ALL_AXES = ("grp", "gx", "gy")
PAIRS = ((0, 1), (0, -1), (1, 1), (1, -1), (2, 1), (2, -1))


def exchange(cells, sides, width):
    for axis, dim in sides:
        count = lax.axis_size(axis)
        size = cells.shape[dim]
        head = lax.slice_in_dim(cells, 0, width, axis=dim)
        tail = lax.slice_in_dim(cells, size - width, size, axis=dim)
        if count == 1:
            before = jnp.zeros_like(tail)
            after = jnp.zeros_like(head)
        elif count == 2:
            index = lax.axis_index(axis)
            sent = jnp.where(index == 0, tail, head)
            got = lax.ppermute(sent, axis, [(0, 1), (1, 0)])
            before = jnp.where(index == 1, got, 0.0)
            after = jnp.where(index == 0, got, 0.0)
        else:
            before = lax.ppermute(tail, axis, [(i, i + 1) for i in range(count - 1)])
            after = lax.ppermute(head, axis, [(i + 1, i) for i in range(count - 1)])
        cells = jnp.concatenate([before, cells, after], axis=dim)
    return cells


def flat_shift(padded, rows, width, stride, dx, dy, dz):
    lead = stride + dy * stride + dz
    return padded[1 + dx:1 + dx + rows, lead:lead + width]


def neighbours(field, stride):
    rows, width = field.shape
    padded = jnp.pad(field, ((1, 1), (stride, stride)))
    steps = ((1, 0, 0), (-1, 0, 0), (0, 1, 0), (0, -1, 0), (0, 0, 1), (0, 0, -1))
    return [flat_shift(padded, rows, width, stride, *step) for step in steps]


def face_terms(conductance, stride):
    return [0.5 * (conductance + other) for other in neighbours(conductance, stride)]


def operate(field, storage, face_list, stride):
    summed = storage * field
    for face, other in zip(face_list, neighbours(field, stride)):
        summed = summed + face * (field - other)
    return summed


def inside_mask(rows, span_y, span_z):
    shape = (rows, span_y * span_z)
    column = lax.broadcasted_iota(jnp.int32, shape, 1)
    coords = (
        (lax.broadcasted_iota(jnp.int32, shape, 0), rows, "gx"),
        (column // span_z, span_y, "gy"),
        (column % span_z, span_z, "grp"),
    )
    mask = None
    for local_index, span, axis in coords:
        block = span - 2 * HALO
        where = lax.axis_index(axis) * block - HALO + local_index
        ok = (where >= 0) & (where < block * lax.axis_size(axis))
        mask = ok if mask is None else mask & ok
    return mask


def trimmed(flat, span_y, span_z):
    cube = flat.reshape(flat.shape[0], span_y, span_z)
    return cube[HALO:-HALO, HALO:-HALO, HALO:-HALO]


def grp_pool(vector):
    groups = lax.axis_size("grp")
    index = lax.axis_index("grp")
    parts = [vector]
    for step in range(1, groups):
        parts.append(lax.ppermute(vector, "grp", [(i, (i + step) % groups) for i in range(groups)]))
    stacked = jnp.stack(parts)
    order = (index - jnp.arange(groups)) % groups
    return jnp.take(stacked, order, axis=0)


def dot(left, right):
    return jnp.dot(left, right, precision=lax.Precision.HIGHEST)


def box_matrix(boxes, cells, stride, offset, live, inner=None):
    box = lax.broadcasted_iota(jnp.int32, (boxes, cells), 0)
    cell = lax.broadcasted_iota(jnp.int32, (boxes, cells), 1)
    if inner is None:
        hit = (cell - offset >= box * BOX) & (cell - offset < box * BOX + BOX)
    else:
        outer_cell, inner_cell = cell // stride - offset, cell % stride - offset
        outer_box, inner_box = box // inner, box % inner
        hit = (outer_cell >= outer_box * BOX) & (outer_cell < outer_box * BOX + BOX)
        hit = hit & (inner_cell >= inner_box * BOX) & (inner_cell < inner_box * BOX + BOX)
    return (hit & live).astype(jnp.float32)


def everyone(vector):
    count = lax.axis_size(ALL_AXES)
    copies = jnp.broadcast_to(vector[None], (count,) + vector.shape)
    return lax.all_to_all(copies, ALL_AXES, 0, 0, tiled=True).reshape(-1)


def local(source, conductance, storage, aggregate_ids, coarse_values, coarse_columns):
    size_x, size_y, size_z = source.shape
    assert HALO == BOX and HALO >= 2 * NU and HALO >= NU + 2
    stacked = jnp.stack([source, conductance, storage])
    wide = exchange(stacked, (("grp", 3),), HALO)
    span_z = wide.shape[3]
    stride = span_z
    wide = wide.reshape(3, size_x, size_y * span_z)
    wide = exchange(wide, (("gy", 2),), HALO * span_z)
    wide = exchange(wide, (("gx", 1),), HALO)
    rows = wide.shape[1]
    span_y = wide.shape[2] // span_z
    src, cond, stor = wide[0], wide[1], wide[2]
    mask = inside_mask(rows, span_y, span_z)
    face_list = face_terms(cond, stride)
    diagonal = stor
    for position in range(6):
        diagonal = diagonal + face_list[position]

    def op(field):
        return operate(field, stor, face_list, stride)

    solution = jnp.where(mask, WEIGHT * src / diagonal, 0.0)
    for sweep_number in range(NU - 1):
        solution = jnp.where(mask, solution + WEIGHT * (src - op(solution)) / diagonal, 0.0)
    residual = src - op(solution)
    scaled = jnp.where(mask, residual / diagonal, 0.0)
    smoothed = residual - WEIGHT * op(scaled)

    bx, by, bz = size_x // BOX, size_y // BOX, size_z // BOX
    live = lax.axis_index("grp") >= 0
    pick_x = box_matrix(bx, rows, 1, HALO, live)
    pick_yz = box_matrix(by * bz, span_y * span_z, span_z, HALO, live, bz).T
    box_totals = dot(pick_x, dot(smoothed, pick_yz)).reshape(-1)
    box_labels = aggregate_ids[::BOX, ::BOX, ::BOX].reshape(-1)
    placed = (
        box_labels[:, None] == lax.broadcasted_iota(jnp.int32, (box_labels.shape[0],) * 2, 1)
    ).astype(source.dtype)
    coarse_rhs = dot(box_totals[None, :], placed)[0]
    eye = lax.broadcasted_iota(jnp.int32, (64, 64), 0) == lax.broadcasted_iota(jnp.int32, (64, 64), 1)
    coarse_diag = jnp.sum(jnp.where(eye[None], coarse_values[:, :, :64], 0.0), axis=2).reshape(-1)
    block_rows = coarse_values.shape[0]
    grid_x = lax.axis_size("gx")
    grid_y = lax.axis_size("gy")
    groups = lax.axis_size("grp")
    tables = groups * grid_x * grid_y * block_rows
    pick = (
        coarse_columns.reshape(-1, 1) == lax.broadcasted_iota(jnp.int32, (coarse_columns.size, tables), 1)
    ).astype(source.dtype)
    coarse_error = coarse_rhs / coarse_diag
    for sweep_number in range(CITER - 1):
        pooled = everyone(coarse_error)
        blocks = dot(pick, pooled.reshape(tables, 64))
        blocks = blocks.reshape(block_rows, -1)
        applied = jnp.einsum(
            "bim,bm->bi", coarse_values, blocks, precision=lax.Precision.HIGHEST
        ).reshape(-1)
        coarse_error = coarse_error + (coarse_rhs - applied) / coarse_diag

    small = dot(placed, coarse_error[:, None]).reshape(-1)
    every = everyone(small).reshape(groups, grid_x, grid_y, bx, by, bz)
    boxes = every.transpose(1, 3, 2, 4, 0, 5).reshape(grid_x * bx, grid_y * by, groups * bz)
    boxes = jnp.pad(boxes, 1)
    window = lax.dynamic_slice(
        boxes,
        (lax.axis_index("gx") * bx, lax.axis_index("gy") * by, lax.axis_index("grp") * bz),
        (bx + 2, by + 2, bz + 2),
    )
    window = window.reshape(bx + 2, (by + 2) * (bz + 2))
    spread_x = box_matrix(bx + 2, rows, 1, 0, live).T
    spread_yz = box_matrix((by + 2) * (bz + 2), span_y * span_z, span_z, 0, live, bz + 2)
    lifted = dot(spread_x, dot(window, spread_yz))
    solution = jnp.where(mask, solution + (lifted - WEIGHT * op(lifted) / diagonal), 0.0)
    for sweep_number in range(NU):
        solution = jnp.where(mask, solution + WEIGHT * (src - op(solution)) / diagonal, 0.0)
    return (trimmed(solution, span_y, span_z), coarse_error)


def solution(mesh):
    return jax.shard_map(
        local,
        mesh=mesh,
        in_specs=(
            P("gx", "gy", "grp"),
            P("gx", "gy", "grp"),
            P("gx", "gy", "grp"),
            P("gx", "gy", "grp"),
            P(("grp", "gx", "gy"), None, None),
            P(("grp", "gx", "gy"), None),
        ),
        out_specs=(P("gx", "gy", "grp"), P(("grp", "gx", "gy"))),
        check_vma=False,
    )
```

```python
import jax
import jax.numpy as jnp
from jax import lax
from jax.sharding import PartitionSpec as P

NU = 2
CITER = 4
BOX = 4
HALO = 4

WEIGHT = 2.0 / 3.0
ALL_AXES = ("grp", "gx", "gy")
PAIRS = ((0, 1), (0, -1), (1, 1), (1, -1), (2, 1), (2, -1))


def padded_size(shape):
    size = -(-shape[-1] // 128) * 128
    if len(shape) > 1:
        size *= -(-shape[-2] // 8) * 8
    for extent in shape[:-2]:
        size *= extent
    return size


def permute(slab, axis, pairs):
    count = slab.size
    if count % 128 == 0 and padded_size(slab.shape) > count + count // 4:
        return lax.ppermute(slab.reshape(-1, 128), axis, pairs).reshape(slab.shape)
    return lax.ppermute(slab, axis, pairs)


def exchange(cells, sides, width):
    for axis, dim in sides:
        count = lax.axis_size(axis)
        size = cells.shape[dim]
        head = lax.slice_in_dim(cells, 0, width, axis=dim)
        tail = lax.slice_in_dim(cells, size - width, size, axis=dim)
        if count == 1:
            before = jnp.zeros_like(tail)
            after = jnp.zeros_like(head)
        elif count == 2:
            index = lax.axis_index(axis)
            sent = jnp.where(index == 0, tail, head)
            got = permute(sent, axis, [(0, 1), (1, 0)])
            before = jnp.where(index == 1, got, 0.0)
            after = jnp.where(index == 0, got, 0.0)
        else:
            before = permute(tail, axis, [(i, i + 1) for i in range(count - 1)])
            after = permute(head, axis, [(i + 1, i) for i in range(count - 1)])
        cells = jnp.concatenate([before, cells, after], axis=dim)
    return cells


def flat_shift(padded, rows, width, stride, dx, dy, dz):
    lead = stride + dy * stride + dz
    return padded[1 + dx:1 + dx + rows, lead:lead + width]


def neighbours(field, stride):
    rows, width = field.shape
    padded = jnp.pad(field, ((1, 1), (stride, stride)))
    steps = ((1, 0, 0), (-1, 0, 0), (0, 1, 0), (0, -1, 0), (0, 0, 1), (0, 0, -1))
    return [flat_shift(padded, rows, width, stride, *step) for step in steps]


def face_terms(conductance, stride):
    return [0.5 * (conductance + other) for other in neighbours(conductance, stride)]


def operate(field, storage, face_list, stride):
    summed = storage * field
    for face, other in zip(face_list, neighbours(field, stride)):
        summed = summed + face * (field - other)
    return summed


def inside_mask(rows, span_y, span_z):
    shape = (rows, span_y * span_z)
    column = lax.broadcasted_iota(jnp.int32, shape, 1)
    coords = (
        (lax.broadcasted_iota(jnp.int32, shape, 0), rows, "gx"),
        (column // span_z, span_y, "gy"),
        (column % span_z, span_z, "grp"),
    )
    mask = None
    for local_index, span, axis in coords:
        block = span - 2 * HALO
        where = lax.axis_index(axis) * block - HALO + local_index
        ok = (where >= 0) & (where < block * lax.axis_size(axis))
        mask = ok if mask is None else mask & ok
    return mask


def trimmed(flat, span_y, span_z):
    cube = flat.reshape(flat.shape[0], span_y, span_z)
    return cube[HALO:-HALO, HALO:-HALO, HALO:-HALO]


def grp_pool(vector):
    groups = lax.axis_size("grp")
    index = lax.axis_index("grp")
    parts = [vector]
    for step in range(1, groups):
        parts.append(lax.ppermute(vector, "grp", [(i, (i + step) % groups) for i in range(groups)]))
    stacked = jnp.stack(parts)
    order = (index - jnp.arange(groups)) % groups
    return jnp.take(stacked, order, axis=0)


def dot(left, right):
    return jnp.dot(left, right, precision=lax.Precision.HIGHEST)


def box_matrix(boxes, cells, stride, offset, live, inner=None):
    box = lax.broadcasted_iota(jnp.int32, (boxes, cells), 0)
    cell = lax.broadcasted_iota(jnp.int32, (boxes, cells), 1)
    if inner is None:
        hit = (cell - offset >= box * BOX) & (cell - offset < box * BOX + BOX)
    else:
        outer_cell, inner_cell = cell // stride - offset, cell % stride - offset
        outer_box, inner_box = box // inner, box % inner
        hit = (outer_cell >= outer_box * BOX) & (outer_cell < outer_box * BOX + BOX)
        hit = hit & (inner_cell >= inner_box * BOX) & (inner_cell < inner_box * BOX + BOX)
    return (hit & live).astype(jnp.float32)


def everyone(vector):
    count = lax.axis_size(ALL_AXES)
    copies = jnp.broadcast_to(vector[None], (count,) + vector.shape)
    return lax.all_to_all(copies, ALL_AXES, 0, 0, tiled=True).reshape(-1)


def local(source, conductance, storage, aggregate_ids, coarse_values, coarse_columns):
    size_x, size_y, size_z = source.shape
    assert HALO == BOX and HALO >= 2 * NU and HALO >= NU + 2
    stacked = jnp.stack([source, conductance, storage])
    wide = exchange(stacked, (("grp", 3),), HALO)
    span_z = wide.shape[3]
    stride = span_z
    wide = wide.reshape(3, size_x, size_y * span_z)
    wide = exchange(wide, (("gy", 2),), HALO * span_z)
    wide = exchange(wide, (("gx", 1),), HALO)
    rows = wide.shape[1]
    span_y = wide.shape[2] // span_z
    src, cond, stor = wide[0], wide[1], wide[2]
    mask = inside_mask(rows, span_y, span_z)
    face_list = face_terms(cond, stride)
    diagonal = stor
    for position in range(6):
        diagonal = diagonal + face_list[position]

    def op(field):
        return operate(field, stor, face_list, stride)

    solution = jnp.where(mask, WEIGHT * src / diagonal, 0.0)
    for sweep_number in range(NU - 1):
        solution = jnp.where(mask, solution + WEIGHT * (src - op(solution)) / diagonal, 0.0)
    residual = src - op(solution)
    scaled = jnp.where(mask, residual / diagonal, 0.0)
    smoothed = residual - WEIGHT * op(scaled)

    bx, by, bz = size_x // BOX, size_y // BOX, size_z // BOX
    live = lax.axis_index("grp") >= 0
    pick_x = box_matrix(bx, rows, 1, HALO, live)
    pick_yz = box_matrix(by * bz, span_y * span_z, span_z, HALO, live, bz).T
    box_totals = dot(pick_x, dot(smoothed, pick_yz)).reshape(-1)
    box_labels = aggregate_ids[::BOX, ::BOX, ::BOX].reshape(-1)
    placed = (
        box_labels[:, None] == lax.broadcasted_iota(jnp.int32, (box_labels.shape[0],) * 2, 1)
    ).astype(source.dtype)
    coarse_rhs = dot(box_totals[None, :], placed)[0]
    eye = lax.broadcasted_iota(jnp.int32, (64, 64), 0) == lax.broadcasted_iota(jnp.int32, (64, 64), 1)
    coarse_diag = jnp.sum(jnp.where(eye[None], coarse_values[:, :, :64], 0.0), axis=2).reshape(-1)
    block_rows = coarse_values.shape[0]
    grid_x = lax.axis_size("gx")
    grid_y = lax.axis_size("gy")
    groups = lax.axis_size("grp")
    tables = groups * grid_x * grid_y * block_rows
    pick = (
        coarse_columns.reshape(-1, 1) == lax.broadcasted_iota(jnp.int32, (coarse_columns.size, tables), 1)
    ).astype(source.dtype)
    coarse_error = coarse_rhs / coarse_diag
    for sweep_number in range(CITER - 1):
        pooled = everyone(coarse_error)
        blocks = dot(pick, pooled.reshape(tables, 64))
        blocks = blocks.reshape(block_rows, -1)
        applied = jnp.einsum(
            "bim,bm->bi", coarse_values, blocks, precision=lax.Precision.HIGHEST
        ).reshape(-1)
        coarse_error = coarse_error + (coarse_rhs - applied) / coarse_diag

    small = dot(placed, coarse_error[:, None]).reshape(-1)
    every = everyone(small).reshape(groups, grid_x, grid_y, bx, by, bz)
    boxes = every.transpose(1, 3, 2, 4, 0, 5).reshape(grid_x * bx, grid_y * by, groups * bz)
    boxes = jnp.pad(boxes, 1)
    window = lax.dynamic_slice(
        boxes,
        (lax.axis_index("gx") * bx, lax.axis_index("gy") * by, lax.axis_index("grp") * bz),
        (bx + 2, by + 2, bz + 2),
    )
    window = window.reshape(bx + 2, (by + 2) * (bz + 2))
    spread_x = box_matrix(bx + 2, rows, 1, 0, live).T
    spread_yz = box_matrix((by + 2) * (bz + 2), span_y * span_z, span_z, 0, live, bz + 2)
    lifted = dot(spread_x, dot(window, spread_yz))
    solution = jnp.where(mask, solution + (lifted - WEIGHT * op(lifted) / diagonal), 0.0)
    for sweep_number in range(NU):
        solution = jnp.where(mask, solution + WEIGHT * (src - op(solution)) / diagonal, 0.0)
    return (trimmed(solution, span_y, span_z), coarse_error)


def solution(mesh):
    return jax.shard_map(
        local,
        mesh=mesh,
        in_specs=(
            P("gx", "gy", "grp"),
            P("gx", "gy", "grp"),
            P("gx", "gy", "grp"),
            P("gx", "gy", "grp"),
            P(("grp", "gx", "gy"), None, None),
            P(("grp", "gx", "gy"), None),
        ),
        out_specs=(P("gx", "gy", "grp"), P(("grp", "gx", "gy"))),
        check_vma=False,
    )
```

```python
import jax
import jax.numpy as jnp
from jax import lax
from jax.sharding import PartitionSpec as P

NU = 2
CITER = 4
BOX = 4
HALO = 4

WEIGHT = 2.0 / 3.0
ALL_AXES = ("grp", "gx", "gy")
PAIRS = ((0, 1), (0, -1), (1, 1), (1, -1), (2, 1), (2, -1))


def padded_size(shape):
    size = -(-shape[-1] // 128) * 128
    if len(shape) > 1:
        size *= -(-shape[-2] // 8) * 8
    for extent in shape[:-2]:
        size *= extent
    return size


def permute(slab, axis, pairs):
    count = slab.size
    if count % 128 == 0 and padded_size(slab.shape) > count + count // 4:
        return lax.ppermute(slab.reshape(-1, 128), axis, pairs).reshape(slab.shape)
    return lax.ppermute(slab, axis, pairs)


def exchange(cells, sides, width):
    for axis, dim in sides:
        count = lax.axis_size(axis)
        size = cells.shape[dim]
        head = lax.slice_in_dim(cells, 0, width, axis=dim)
        tail = lax.slice_in_dim(cells, size - width, size, axis=dim)
        if count == 1:
            before = jnp.zeros_like(tail)
            after = jnp.zeros_like(head)
        elif count == 2:
            index = lax.axis_index(axis)
            sent = jnp.where(index == 0, tail, head)
            got = permute(sent, axis, [(0, 1), (1, 0)])
            before = jnp.where(index == 1, got, 0.0)
            after = jnp.where(index == 0, got, 0.0)
        else:
            before = permute(tail, axis, [(i, i + 1) for i in range(count - 1)])
            after = permute(head, axis, [(i + 1, i) for i in range(count - 1)])
        cells = jnp.concatenate([before, cells, after], axis=dim)
    return cells


def flat_shift(padded, rows, width, stride, dx, dy, dz):
    lead = stride + dy * stride + dz
    return padded[1 + dx:1 + dx + rows, lead:lead + width]


def neighbours(field, stride):
    rows, width = field.shape
    padded = jnp.pad(field, ((1, 1), (stride, stride)))
    steps = ((1, 0, 0), (-1, 0, 0), (0, 1, 0), (0, -1, 0), (0, 0, 1), (0, 0, -1))
    return [flat_shift(padded, rows, width, stride, *step) for step in steps]


def face_terms(conductance, stride):
    return [0.5 * (conductance + other) for other in neighbours(conductance, stride)]


def operate(field, storage, face_list, stride):
    summed = storage * field
    for face, other in zip(face_list, neighbours(field, stride)):
        summed = summed + face * (field - other)
    return summed


def inside_mask(rows, span_y, span_z):
    shape = (rows, span_y * span_z)
    column = lax.broadcasted_iota(jnp.int32, shape, 1)
    coords = (
        (lax.broadcasted_iota(jnp.int32, shape, 0), rows, "gx"),
        (column // span_z, span_y, "gy"),
        (column % span_z, span_z, "grp"),
    )
    mask = None
    for local_index, span, axis in coords:
        block = span - 2 * HALO
        where = lax.axis_index(axis) * block - HALO + local_index
        ok = (where >= 0) & (where < block * lax.axis_size(axis))
        mask = ok if mask is None else mask & ok
    return mask


def trimmed(flat, span_y, span_z):
    cube = flat.reshape(flat.shape[0], span_y, span_z)
    return cube[HALO:-HALO, HALO:-HALO, HALO:-HALO]


def grp_pool(vector):
    groups = lax.axis_size("grp")
    index = lax.axis_index("grp")
    parts = [vector]
    for step in range(1, groups):
        parts.append(lax.ppermute(vector, "grp", [(i, (i + step) % groups) for i in range(groups)]))
    stacked = jnp.stack(parts)
    order = (index - jnp.arange(groups)) % groups
    return jnp.take(stacked, order, axis=0)


def dot(left, right):
    return jnp.dot(left, right, precision=lax.Precision.HIGHEST)


def box_matrix(boxes, cells, stride, offset, live, inner=None):
    box = lax.broadcasted_iota(jnp.int32, (boxes, cells), 0)
    cell = lax.broadcasted_iota(jnp.int32, (boxes, cells), 1)
    if inner is None:
        hit = (cell - offset >= box * BOX) & (cell - offset < box * BOX + BOX)
    else:
        outer_cell, inner_cell = cell // stride - offset, cell % stride - offset
        outer_box, inner_box = box // inner, box % inner
        hit = (outer_cell >= outer_box * BOX) & (outer_cell < outer_box * BOX + BOX)
        hit = hit & (inner_cell >= inner_box * BOX) & (inner_cell < inner_box * BOX + BOX)
    return (hit & live).astype(jnp.float32)


def everyone(vector):
    count = lax.axis_size(ALL_AXES)
    copies = jnp.broadcast_to(vector[None], (count,) + vector.shape)
    return lax.all_to_all(copies, ALL_AXES, 0, 0, tiled=True).reshape(-1)


def local(source, conductance, storage, aggregate_ids, coarse_values, coarse_columns):
    size_x, size_y, size_z = source.shape
    assert HALO == BOX and HALO >= 2 * NU and HALO >= NU + 2
    stacked = jnp.stack([source, conductance, storage])
    wide = exchange(stacked, (("grp", 3),), HALO)
    span_z = wide.shape[3]
    stride = span_z
    wide = wide.reshape(3, size_x, size_y * span_z)
    wide = exchange(wide, (("gy", 2),), HALO * span_z)
    wide = exchange(wide, (("gx", 1),), HALO)
    rows = wide.shape[1]
    span_y = wide.shape[2] // span_z
    src, cond, stor = wide[0], wide[1], wide[2]
    mask = inside_mask(rows, span_y, span_z)
    face_list = face_terms(cond, stride)
    diagonal = stor
    for position in range(6):
        diagonal = diagonal + face_list[position]

    def op(field):
        return operate(field, stor, face_list, stride)

    solution = jnp.where(mask, WEIGHT * src / diagonal, 0.0)
    for sweep_number in range(NU - 1):
        solution = jnp.where(mask, solution + WEIGHT * (src - op(solution)) / diagonal, 0.0)
    residual = src - op(solution)
    scaled = jnp.where(mask, residual / diagonal, 0.0)
    smoothed = residual - WEIGHT * op(scaled)

    bx, by, bz = size_x // BOX, size_y // BOX, size_z // BOX
    live = lax.axis_index("grp") >= 0
    pick_x = box_matrix(bx, rows, 1, HALO, live)
    pick_yz = box_matrix(by * bz, span_y * span_z, span_z, HALO, live, bz).T
    box_labels = aggregate_ids[::BOX, ::BOX, ::BOX].reshape(-1)
    placed = (
        box_labels[:, None] == lax.broadcasted_iota(jnp.int32, (box_labels.shape[0],) * 2, 1)
    ).astype(source.dtype)
    spread_x = box_matrix(bx + 2, rows, 1, 0, live).T
    spread_yz = box_matrix((by + 2) * (bz + 2), span_y * span_z, span_z, 0, live, bz + 2)
    pick_x, pick_yz, placed, spread_x, spread_yz = lax.optimization_barrier(
        (pick_x, pick_yz, placed, spread_x, spread_yz)
    )
    box_totals = dot(pick_x, dot(smoothed, pick_yz)).reshape(-1)
    coarse_rhs = dot(box_totals[None, :], placed)[0]
    eye = lax.broadcasted_iota(jnp.int32, (64, 64), 0) == lax.broadcasted_iota(jnp.int32, (64, 64), 1)
    coarse_diag = jnp.sum(jnp.where(eye[None], coarse_values[:, :, :64], 0.0), axis=2).reshape(-1)
    block_rows = coarse_values.shape[0]
    grid_x = lax.axis_size("gx")
    grid_y = lax.axis_size("gy")
    groups = lax.axis_size("grp")
    tables = groups * grid_x * grid_y * block_rows
    pick = (
        coarse_columns.reshape(-1, 1) == lax.broadcasted_iota(jnp.int32, (coarse_columns.size, tables), 1)
    ).astype(source.dtype)
    pick = lax.optimization_barrier(pick)
    coarse_error = coarse_rhs / coarse_diag
    for sweep_number in range(CITER - 1):
        pooled = everyone(coarse_error)
        blocks = dot(pick, pooled.reshape(tables, 64))
        blocks = blocks.reshape(block_rows, -1)
        applied = jnp.einsum(
            "bim,bm->bi", coarse_values, blocks, precision=lax.Precision.HIGHEST
        ).reshape(-1)
        coarse_error = coarse_error + (coarse_rhs - applied) / coarse_diag

    small = dot(placed, coarse_error[:, None]).reshape(-1)
    every = everyone(small).reshape(groups, grid_x, grid_y, bx, by, bz)
    boxes = every.transpose(1, 3, 2, 4, 0, 5).reshape(grid_x * bx, grid_y * by, groups * bz)
    boxes = jnp.pad(boxes, 1)
    window = lax.dynamic_slice(
        boxes,
        (lax.axis_index("gx") * bx, lax.axis_index("gy") * by, lax.axis_index("grp") * bz),
        (bx + 2, by + 2, bz + 2),
    )
    window = window.reshape(bx + 2, (by + 2) * (bz + 2))
    lifted = dot(spread_x, dot(window, spread_yz))
    solution = jnp.where(mask, solution + (lifted - WEIGHT * op(lifted) / diagonal), 0.0)
    for sweep_number in range(NU):
        solution = jnp.where(mask, solution + WEIGHT * (src - op(solution)) / diagonal, 0.0)
    return (trimmed(solution, span_y, span_z), coarse_error)


def solution(mesh):
    return jax.shard_map(
        local,
        mesh=mesh,
        in_specs=(
            P("gx", "gy", "grp"),
            P("gx", "gy", "grp"),
            P("gx", "gy", "grp"),
            P("gx", "gy", "grp"),
            P(("grp", "gx", "gy"), None, None),
            P(("grp", "gx", "gy"), None),
        ),
        out_specs=(P("gx", "gy", "grp"), P(("grp", "gx", "gy"))),
        check_vma=False,
    )
```

```python
import jax
import jax.numpy as jnp
from jax import lax
from jax.sharding import PartitionSpec as P

NU = 2
CITER = 4
BOX = 4
HALO = 4

WEIGHT = 2.0 / 3.0
ALL_AXES = ("grp", "gx", "gy")
PAIRS = ((0, 1), (0, -1), (1, 1), (1, -1), (2, 1), (2, -1))


def padded_size(shape):
    size = -(-shape[-1] // 128) * 128
    if len(shape) > 1:
        size *= -(-shape[-2] // 8) * 8
    for extent in shape[:-2]:
        size *= extent
    return size


def permute(slab, axis, pairs):
    count = slab.size
    if count % 128 == 0 and padded_size(slab.shape) > count + count // 4:
        return lax.ppermute(slab.reshape(-1, 128), axis, pairs).reshape(slab.shape)
    return lax.ppermute(slab, axis, pairs)


def exchange(cells, sides, width):
    for axis, dim in sides:
        count = lax.axis_size(axis)
        size = cells.shape[dim]
        head = lax.slice_in_dim(cells, 0, width, axis=dim)
        tail = lax.slice_in_dim(cells, size - width, size, axis=dim)
        if count == 1:
            before = jnp.zeros_like(tail)
            after = jnp.zeros_like(head)
        elif count == 2:
            index = lax.axis_index(axis)
            sent = jnp.where(index == 0, tail, head)
            got = permute(sent, axis, [(0, 1), (1, 0)])
            before = jnp.where(index == 1, got, 0.0)
            after = jnp.where(index == 0, got, 0.0)
        elif count % 2 == 0:
            index = lax.axis_index(axis)
            even = index % 2 == 0
            first = [(i + d, i + 1 - d) for i in range(0, count, 2) for d in (0, 1)]
            second = [(i + d, i + 1 - d) for i in range(1, count - 1, 2) for d in (0, 1)]
            got_first = permute(jnp.where(even, tail, head), axis, first)
            got_second = permute(jnp.where(even, head, tail), axis, second)
            before = jnp.where(even, got_second, got_first)
            after = jnp.where(even, got_first, got_second)
        else:
            before = permute(tail, axis, [(i, i + 1) for i in range(count - 1)])
            after = permute(head, axis, [(i + 1, i) for i in range(count - 1)])
        cells = jnp.concatenate([before, cells, after], axis=dim)
    return cells


def flat_shift(padded, rows, width, stride, dx, dy, dz):
    lead = stride + dy * stride + dz
    return padded[1 + dx:1 + dx + rows, lead:lead + width]


def neighbours(field, stride):
    rows, width = field.shape
    padded = jnp.pad(field, ((1, 1), (stride, stride)))
    steps = ((1, 0, 0), (-1, 0, 0), (0, 1, 0), (0, -1, 0), (0, 0, 1), (0, 0, -1))
    return [flat_shift(padded, rows, width, stride, *step) for step in steps]


def face_terms(conductance, stride):
    return [0.5 * (conductance + other) for other in neighbours(conductance, stride)]


def operate(field, storage, face_list, stride):
    summed = storage * field
    for face, other in zip(face_list, neighbours(field, stride)):
        summed = summed + face * (field - other)
    return summed


def inside_mask(rows, span_y, span_z):
    shape = (rows, span_y * span_z)
    column = lax.broadcasted_iota(jnp.int32, shape, 1)
    coords = (
        (lax.broadcasted_iota(jnp.int32, shape, 0), rows, "gx"),
        (column // span_z, span_y, "gy"),
        (column % span_z, span_z, "grp"),
    )
    mask = None
    for local_index, span, axis in coords:
        block = span - 2 * HALO
        where = lax.axis_index(axis) * block - HALO + local_index
        ok = (where >= 0) & (where < block * lax.axis_size(axis))
        mask = ok if mask is None else mask & ok
    return mask


def trimmed(flat, span_y, span_z):
    cube = flat.reshape(flat.shape[0], span_y, span_z)
    return cube[HALO:-HALO, HALO:-HALO, HALO:-HALO]


def grp_pool(vector):
    groups = lax.axis_size("grp")
    index = lax.axis_index("grp")
    parts = [vector]
    for step in range(1, groups):
        parts.append(lax.ppermute(vector, "grp", [(i, (i + step) % groups) for i in range(groups)]))
    stacked = jnp.stack(parts)
    order = (index - jnp.arange(groups)) % groups
    return jnp.take(stacked, order, axis=0)


def dot(left, right):
    return jnp.dot(left, right, precision=lax.Precision.HIGHEST)


def box_matrix(boxes, cells, stride, offset, live, inner=None):
    box = lax.broadcasted_iota(jnp.int32, (boxes, cells), 0)
    cell = lax.broadcasted_iota(jnp.int32, (boxes, cells), 1)
    if inner is None:
        hit = (cell - offset >= box * BOX) & (cell - offset < box * BOX + BOX)
    else:
        outer_cell, inner_cell = cell // stride - offset, cell % stride - offset
        outer_box, inner_box = box // inner, box % inner
        hit = (outer_cell >= outer_box * BOX) & (outer_cell < outer_box * BOX + BOX)
        hit = hit & (inner_cell >= inner_box * BOX) & (inner_cell < inner_box * BOX + BOX)
    return (hit & live).astype(jnp.float32)


def everyone(vector):
    count = lax.axis_size(ALL_AXES)
    copies = jnp.broadcast_to(vector[None], (count,) + vector.shape)
    return lax.all_to_all(copies, ALL_AXES, 0, 0, tiled=True).reshape(-1)


def local(source, conductance, storage, aggregate_ids, coarse_values, coarse_columns):
    size_x, size_y, size_z = source.shape
    assert HALO == BOX and HALO >= 2 * NU and HALO >= NU + 2
    stacked = jnp.stack([source, conductance, storage])
    wide = exchange(stacked, (("grp", 3),), HALO)
    span_z = wide.shape[3]
    stride = span_z
    wide = wide.reshape(3, size_x, size_y * span_z)
    wide = exchange(wide, (("gy", 2),), HALO * span_z)
    wide = exchange(wide, (("gx", 1),), HALO)
    rows = wide.shape[1]
    span_y = wide.shape[2] // span_z
    src, cond, stor = wide[0], wide[1], wide[2]
    mask = inside_mask(rows, span_y, span_z)
    face_list = face_terms(cond, stride)
    diagonal = stor
    for position in range(6):
        diagonal = diagonal + face_list[position]

    def op(field):
        return operate(field, stor, face_list, stride)

    solution = jnp.where(mask, WEIGHT * src / diagonal, 0.0)
    for sweep_number in range(NU - 1):
        solution = jnp.where(mask, solution + WEIGHT * (src - op(solution)) / diagonal, 0.0)
    residual = src - op(solution)
    scaled = jnp.where(mask, residual / diagonal, 0.0)
    smoothed = residual - WEIGHT * op(scaled)

    bx, by, bz = size_x // BOX, size_y // BOX, size_z // BOX
    live = lax.axis_index("grp") >= 0
    pick_x = box_matrix(bx, rows, 1, HALO, live)
    pick_yz = box_matrix(by * bz, span_y * span_z, span_z, HALO, live, bz).T
    box_totals = dot(pick_x, dot(smoothed, pick_yz)).reshape(-1)
    box_labels = aggregate_ids[::BOX, ::BOX, ::BOX].reshape(-1)
    placed = (
        box_labels[:, None] == lax.broadcasted_iota(jnp.int32, (box_labels.shape[0],) * 2, 1)
    ).astype(source.dtype)
    coarse_rhs = dot(box_totals[None, :], placed)[0]
    eye = lax.broadcasted_iota(jnp.int32, (64, 64), 0) == lax.broadcasted_iota(jnp.int32, (64, 64), 1)
    coarse_diag = jnp.sum(jnp.where(eye[None], coarse_values[:, :, :64], 0.0), axis=2).reshape(-1)
    block_rows = coarse_values.shape[0]
    grid_x = lax.axis_size("gx")
    grid_y = lax.axis_size("gy")
    groups = lax.axis_size("grp")
    tables = groups * grid_x * grid_y * block_rows
    pick = (
        coarse_columns.reshape(-1, 1) == lax.broadcasted_iota(jnp.int32, (coarse_columns.size, tables), 1)
    ).astype(source.dtype)
    coarse_error = coarse_rhs / coarse_diag
    for sweep_number in range(CITER - 1):
        pooled = everyone(coarse_error)
        blocks = dot(pick, pooled.reshape(tables, 64))
        blocks = blocks.reshape(block_rows, -1)
        applied = jnp.einsum(
            "bim,bm->bi", coarse_values, blocks, precision=lax.Precision.HIGHEST
        ).reshape(-1)
        coarse_error = coarse_error + (coarse_rhs - applied) / coarse_diag

    small = dot(placed, coarse_error[:, None]).reshape(-1)
    every = everyone(small).reshape(groups, grid_x, grid_y, bx, by, bz)
    boxes = every.transpose(1, 3, 2, 4, 0, 5).reshape(grid_x * bx, grid_y * by, groups * bz)
    boxes = jnp.pad(boxes, 1)
    window = lax.dynamic_slice(
        boxes,
        (lax.axis_index("gx") * bx, lax.axis_index("gy") * by, lax.axis_index("grp") * bz),
        (bx + 2, by + 2, bz + 2),
    )
    window = window.reshape(bx + 2, (by + 2) * (bz + 2))
    spread_x = box_matrix(bx + 2, rows, 1, 0, live).T
    spread_yz = box_matrix((by + 2) * (bz + 2), span_y * span_z, span_z, 0, live, bz + 2)
    lifted = dot(spread_x, dot(window, spread_yz))
    solution = jnp.where(mask, solution + (lifted - WEIGHT * op(lifted) / diagonal), 0.0)
    for sweep_number in range(NU):
        solution = jnp.where(mask, solution + WEIGHT * (src - op(solution)) / diagonal, 0.0)
    return (trimmed(solution, span_y, span_z), coarse_error)


def solution(mesh):
    return jax.shard_map(
        local,
        mesh=mesh,
        in_specs=(
            P("gx", "gy", "grp"),
            P("gx", "gy", "grp"),
            P("gx", "gy", "grp"),
            P("gx", "gy", "grp"),
            P(("grp", "gx", "gy"), None, None),
            P(("grp", "gx", "gy"), None),
        ),
        out_specs=(P("gx", "gy", "grp"), P(("grp", "gx", "gy"))),
        check_vma=False,
    )
```

```python
import jax
import jax.numpy as jnp
from jax import lax
from jax.sharding import PartitionSpec as P

NU = 2
CITER = 4
BOX = 4
HALO = 4

WEIGHT = 2.0 / 3.0
ALL_AXES = ("grp", "gx", "gy")
PAIRS = ((0, 1), (0, -1), (1, 1), (1, -1), (2, 1), (2, -1))


def padded_size(shape):
    size = -(-shape[-1] // 128) * 128
    if len(shape) > 1:
        size *= -(-shape[-2] // 8) * 8
    for extent in shape[:-2]:
        size *= extent
    return size


def permute(slab, axis, pairs):
    count = slab.size
    if count % 128 == 0 and padded_size(slab.shape) > count + count // 4:
        return lax.ppermute(slab.reshape(-1, 128), axis, pairs).reshape(slab.shape)
    return lax.ppermute(slab, axis, pairs)


def exchange(cells, sides, width):
    for axis, dim in sides:
        count = lax.axis_size(axis)
        size = cells.shape[dim]
        head = lax.slice_in_dim(cells, 0, width, axis=dim)
        tail = lax.slice_in_dim(cells, size - width, size, axis=dim)
        if count == 1:
            before = jnp.zeros_like(tail)
            after = jnp.zeros_like(head)
        elif count == 2:
            index = lax.axis_index(axis)
            sent = jnp.where(index == 0, tail, head)
            got = permute(sent, axis, [(0, 1), (1, 0)])
            before = jnp.where(index == 1, got, 0.0)
            after = jnp.where(index == 0, got, 0.0)
        elif count % 2 == 0:
            index = lax.axis_index(axis)
            even = index % 2 == 0
            first = [(i + d, i + 1 - d) for i in range(0, count, 2) for d in (0, 1)]
            second = [(i + d, i + 1 - d) for i in range(1, count - 1, 2) for d in (0, 1)]
            got_first = permute(jnp.where(even, tail, head), axis, first)
            got_second = permute(jnp.where(even, head, tail), axis, second)
            before = jnp.where(even, got_second, got_first)
            after = jnp.where(even, got_first, got_second)
        else:
            before = permute(tail, axis, [(i, i + 1) for i in range(count - 1)])
            after = permute(head, axis, [(i + 1, i) for i in range(count - 1)])
        cells = jnp.concatenate([before, cells, after], axis=dim)
    return cells


def flat_shift(padded, rows, width, stride, dx, dy, dz):
    lead = stride + dy * stride + dz
    return padded[1 + dx:1 + dx + rows, lead:lead + width]


def neighbours(field, stride):
    rows, width = field.shape
    padded = jnp.pad(field, ((1, 1), (stride, stride)))
    steps = ((1, 0, 0), (-1, 0, 0), (0, 1, 0), (0, -1, 0), (0, 0, 1), (0, 0, -1))
    return [flat_shift(padded, rows, width, stride, *step) for step in steps]


def face_terms(conductance, stride):
    return [0.5 * (conductance + other) for other in neighbours(conductance, stride)]


def operate(field, storage, face_list, stride):
    summed = storage * field
    for face, other in zip(face_list, neighbours(field, stride)):
        summed = summed + face * (field - other)
    return summed


def inside_mask(rows, span_y, span_z):
    shape = (rows, span_y * span_z)
    column = lax.broadcasted_iota(jnp.int32, shape, 1)
    coords = (
        (lax.broadcasted_iota(jnp.int32, shape, 0), rows, "gx"),
        (column // span_z, span_y, "gy"),
        (column % span_z, span_z, "grp"),
    )
    mask = None
    for local_index, span, axis in coords:
        block = span - 2 * HALO
        where = lax.axis_index(axis) * block - HALO + local_index
        ok = (where >= 0) & (where < block * lax.axis_size(axis))
        mask = ok if mask is None else mask & ok
    return mask


def trimmed(flat, span_y, span_z):
    cube = flat.reshape(flat.shape[0], span_y, span_z)
    return cube[HALO:-HALO, HALO:-HALO, HALO:-HALO]


def grp_pool(vector):
    groups = lax.axis_size("grp")
    index = lax.axis_index("grp")
    parts = [vector]
    for step in range(1, groups):
        parts.append(lax.ppermute(vector, "grp", [(i, (i + step) % groups) for i in range(groups)]))
    stacked = jnp.stack(parts)
    order = (index - jnp.arange(groups)) % groups
    return jnp.take(stacked, order, axis=0)


def dot(left, right):
    return jnp.dot(left, right, precision=lax.Precision.HIGHEST)


def box_matrix(boxes, cells, stride, offset, live, inner=None):
    box = lax.broadcasted_iota(jnp.int32, (boxes, cells), 0)
    cell = lax.broadcasted_iota(jnp.int32, (boxes, cells), 1)
    if inner is None:
        hit = (cell - offset >= box * BOX) & (cell - offset < box * BOX + BOX)
    else:
        outer_cell, inner_cell = cell // stride - offset, cell % stride - offset
        outer_box, inner_box = box // inner, box % inner
        hit = (outer_cell >= outer_box * BOX) & (outer_cell < outer_box * BOX + BOX)
        hit = hit & (inner_cell >= inner_box * BOX) & (inner_cell < inner_box * BOX + BOX)
    return (hit & live).astype(jnp.float32)


def everyone(vector):
    count = lax.axis_size(ALL_AXES)
    copies = jnp.broadcast_to(vector[None], (count,) + vector.shape)
    return lax.all_to_all(copies, ALL_AXES, 0, 0, tiled=True).reshape(-1)


def local(source, conductance, storage, aggregate_ids, coarse_values, coarse_columns):
    size_x, size_y, size_z = source.shape
    assert HALO == BOX and HALO >= 2 * NU and HALO >= NU + 2
    stacked = jnp.stack([source, conductance, storage])
    wide = exchange(stacked, (("grp", 3),), HALO)
    span_z = wide.shape[3]
    stride = span_z
    wide = wide.reshape(3, size_x, size_y * span_z)
    wide = exchange(wide, (("gy", 2),), HALO * span_z)
    wide = exchange(wide, (("gx", 1),), HALO)
    rows = wide.shape[1]
    span_y = wide.shape[2] // span_z
    src, cond, stor = wide[0], wide[1], wide[2]
    mask = inside_mask(rows, span_y, span_z)
    face_list = face_terms(cond, stride)
    diagonal = stor
    for position in range(6):
        diagonal = diagonal + face_list[position]

    def op(field):
        return operate(field, stor, face_list, stride)

    solution = jnp.where(mask, WEIGHT * src / diagonal, 0.0)
    for sweep_number in range(NU - 1):
        solution = jnp.where(mask, solution + WEIGHT * (src - op(solution)) / diagonal, 0.0)
    residual = src - op(solution)
    scaled = jnp.where(mask, residual / diagonal, 0.0)
    smoothed = residual - WEIGHT * op(scaled)

    bx, by, bz = size_x // BOX, size_y // BOX, size_z // BOX
    live = lax.axis_index("grp") >= 0
    pick_x = box_matrix(bx, rows, 1, HALO, live)
    pick_y = box_matrix(by, span_y, 1, HALO, live)
    pick_z = box_matrix(bz, span_z, 1, HALO, live)
    rows_summed = dot(pick_x, smoothed).reshape(bx, span_y, span_z)
    box_totals = jnp.einsum(
        "ayz,by,cz->abc", rows_summed, pick_y, pick_z, precision=lax.Precision.HIGHEST
    ).reshape(-1)
    corner_ids = aggregate_ids[::BOX, ::BOX].reshape(bx * by, size_z).astype(source.dtype)
    first_z = lax.broadcasted_iota(jnp.int32, (size_z, bz), 0) == BOX * lax.broadcasted_iota(jnp.int32, (size_z, bz), 1)
    box_labels = dot(corner_ids, first_z.astype(source.dtype)).astype(jnp.int32).reshape(-1)
    placed = (
        box_labels[:, None] == lax.broadcasted_iota(jnp.int32, (box_labels.shape[0],) * 2, 1)
    ).astype(source.dtype)
    coarse_rhs = dot(box_totals[None, :], placed)[0]
    eye = lax.broadcasted_iota(jnp.int32, (64, 64), 0) == lax.broadcasted_iota(jnp.int32, (64, 64), 1)
    coarse_diag = jnp.sum(jnp.where(eye[None], coarse_values[:, :, :64], 0.0), axis=2).reshape(-1)
    block_rows = coarse_values.shape[0]
    grid_x = lax.axis_size("gx")
    grid_y = lax.axis_size("gy")
    groups = lax.axis_size("grp")
    tables = groups * grid_x * grid_y * block_rows
    pick = (
        coarse_columns.reshape(-1, 1) == lax.broadcasted_iota(jnp.int32, (coarse_columns.size, tables), 1)
    ).astype(source.dtype)
    coarse_error = coarse_rhs / coarse_diag
    for sweep_number in range(CITER - 1):
        pooled = everyone(coarse_error)
        blocks = dot(pick, pooled.reshape(tables, 64))
        blocks = blocks.reshape(block_rows, -1)
        applied = jnp.einsum(
            "bim,bm->bi", coarse_values, blocks, precision=lax.Precision.HIGHEST
        ).reshape(-1)
        coarse_error = coarse_error + (coarse_rhs - applied) / coarse_diag

    small = dot(placed, coarse_error[:, None]).reshape(-1)
    every = everyone(small).reshape(groups, grid_x, grid_y, bx, by, bz)
    boxes = every.transpose(1, 3, 2, 4, 0, 5).reshape(grid_x * bx, grid_y * by, groups * bz)
    boxes = jnp.pad(boxes, 1)
    window = lax.dynamic_slice(
        boxes,
        (lax.axis_index("gx") * bx, lax.axis_index("gy") * by, lax.axis_index("grp") * bz),
        (bx + 2, by + 2, bz + 2),
    )
    window = window.reshape(bx + 2, (by + 2) * (bz + 2))
    spread_x = box_matrix(bx + 2, rows, 1, 0, live).T
    spread_yz = box_matrix((by + 2) * (bz + 2), span_y * span_z, span_z, 0, live, bz + 2)
    lifted = dot(spread_x, dot(window, spread_yz))
    solution = jnp.where(mask, solution + (lifted - WEIGHT * op(lifted) / diagonal), 0.0)
    for sweep_number in range(NU):
        solution = jnp.where(mask, solution + WEIGHT * (src - op(solution)) / diagonal, 0.0)
    return (trimmed(solution, span_y, span_z), coarse_error)


def solution(mesh):
    return jax.shard_map(
        local,
        mesh=mesh,
        in_specs=(
            P("gx", "gy", "grp"),
            P("gx", "gy", "grp"),
            P("gx", "gy", "grp"),
            P("gx", "gy", "grp"),
            P(("grp", "gx", "gy"), None, None),
            P(("grp", "gx", "gy"), None),
        ),
        out_specs=(P("gx", "gy", "grp"), P(("grp", "gx", "gy"))),
        check_vma=False,
    )
```

```python
import jax
import jax.numpy as jnp
from jax import lax
from jax.sharding import PartitionSpec as P

NU = 2
CITER = 4
BOX = 4
HALO = 4

WEIGHT = 2.0 / 3.0
ALL_AXES = ("grp", "gx", "gy")
PAIRS = ((0, 1), (0, -1), (1, 1), (1, -1), (2, 1), (2, -1))


def padded_size(shape):
    size = -(-shape[-1] // 128) * 128
    if len(shape) > 1:
        size *= -(-shape[-2] // 8) * 8
    for extent in shape[:-2]:
        size *= extent
    return size


def permute(slab, axis, pairs):
    count = slab.size
    if count % 128 == 0 and padded_size(slab.shape) > count + count // 4:
        return lax.ppermute(slab.reshape(-1, 128), axis, pairs).reshape(slab.shape)
    return lax.ppermute(slab, axis, pairs)


def exchange(cells, sides, width):
    for axis, dim in sides:
        count = lax.axis_size(axis)
        size = cells.shape[dim]
        head = lax.slice_in_dim(cells, 0, width, axis=dim)
        tail = lax.slice_in_dim(cells, size - width, size, axis=dim)
        if count == 1:
            before = jnp.zeros_like(tail)
            after = jnp.zeros_like(head)
        elif count == 2:
            index = lax.axis_index(axis)
            sent = jnp.where(index == 0, tail, head)
            got = permute(sent, axis, [(0, 1), (1, 0)])
            before = jnp.where(index == 1, got, 0.0)
            after = jnp.where(index == 0, got, 0.0)
        elif count % 2 == 0:
            index = lax.axis_index(axis)
            even = index % 2 == 0
            first = [(i + d, i + 1 - d) for i in range(0, count, 2) for d in (0, 1)]
            second = [(i + d, i + 1 - d) for i in range(1, count - 1, 2) for d in (0, 1)]
            got_first = permute(jnp.where(even, tail, head), axis, first)
            got_second = permute(jnp.where(even, head, tail), axis, second)
            before = jnp.where(even, got_second, got_first)
            after = jnp.where(even, got_first, got_second)
        else:
            before = permute(tail, axis, [(i, i + 1) for i in range(count - 1)])
            after = permute(head, axis, [(i + 1, i) for i in range(count - 1)])
        cells = jnp.concatenate([before, cells, after], axis=dim)
    return cells


def flat_shift(padded, rows, width, stride, dx, dy, dz):
    lead = stride + dy * stride + dz
    return padded[1 + dx:1 + dx + rows, lead:lead + width]


def neighbours(field, stride):
    rows, width = field.shape
    padded = jnp.pad(field, ((1, 1), (stride, stride)))
    steps = ((1, 0, 0), (-1, 0, 0), (0, 1, 0), (0, -1, 0), (0, 0, 1), (0, 0, -1))
    return [flat_shift(padded, rows, width, stride, *step) for step in steps]


def face_terms(conductance, stride):
    return [0.5 * (conductance + other) for other in neighbours(conductance, stride)]


def operate(field, storage, face_list, stride):
    summed = storage * field
    for face, other in zip(face_list, neighbours(field, stride)):
        summed = summed + face * (field - other)
    return summed


def inside_mask(rows, span_y, span_z):
    shape = (rows, span_y * span_z)
    column = lax.broadcasted_iota(jnp.int32, shape, 1)
    coords = (
        (lax.broadcasted_iota(jnp.int32, shape, 0), rows, "gx"),
        (column // span_z, span_y, "gy"),
        (column % span_z, span_z, "grp"),
    )
    mask = None
    for local_index, span, axis in coords:
        block = span - 2 * HALO
        where = lax.axis_index(axis) * block - HALO + local_index
        ok = (where >= 0) & (where < block * lax.axis_size(axis))
        mask = ok if mask is None else mask & ok
    return mask


def trimmed(flat, span_y, span_z):
    cube = flat.reshape(flat.shape[0], span_y, span_z)
    return cube[HALO:-HALO, HALO:-HALO, HALO:-HALO]


def grp_pool(vector):
    groups = lax.axis_size("grp")
    index = lax.axis_index("grp")
    parts = [vector]
    for step in range(1, groups):
        parts.append(lax.ppermute(vector, "grp", [(i, (i + step) % groups) for i in range(groups)]))
    stacked = jnp.stack(parts)
    order = (index - jnp.arange(groups)) % groups
    return jnp.take(stacked, order, axis=0)


def dot(left, right):
    return jnp.dot(left, right, precision=lax.Precision.HIGHEST)


def box_matrix(boxes, cells, stride, offset, live, inner=None):
    box = lax.broadcasted_iota(jnp.int32, (boxes, cells), 0)
    cell = lax.broadcasted_iota(jnp.int32, (boxes, cells), 1)
    if inner is None:
        hit = (cell - offset >= box * BOX) & (cell - offset < box * BOX + BOX)
    else:
        outer_cell, inner_cell = cell // stride - offset, cell % stride - offset
        outer_box, inner_box = box // inner, box % inner
        hit = (outer_cell >= outer_box * BOX) & (outer_cell < outer_box * BOX + BOX)
        hit = hit & (inner_cell >= inner_box * BOX) & (inner_cell < inner_box * BOX + BOX)
    return (hit & live).astype(jnp.float32)


def everyone(vector):
    count = lax.axis_size(ALL_AXES)
    copies = jnp.broadcast_to(vector[None], (count,) + vector.shape)
    return lax.all_to_all(copies, ALL_AXES, 0, 0, tiled=True).reshape(-1)


def local(source, conductance, storage, aggregate_ids, coarse_values, coarse_columns):
    size_x, size_y, size_z = source.shape
    assert HALO == BOX and HALO >= 2 * NU and HALO >= NU + 2
    stacked = jnp.stack([source, conductance, storage])
    wide = exchange(stacked, (("grp", 3),), HALO)
    span_z = wide.shape[3]
    stride = span_z
    wide = wide.reshape(3, size_x, size_y * span_z)
    wide = exchange(wide, (("gy", 2),), HALO * span_z)
    wide = exchange(wide, (("gx", 1),), HALO)
    rows = wide.shape[1]
    span_y = wide.shape[2] // span_z
    src, cond, stor = wide[0], wide[1], wide[2]
    mask = inside_mask(rows, span_y, span_z)
    face_list = face_terms(cond, stride)
    diagonal = stor
    for position in range(6):
        diagonal = diagonal + face_list[position]

    def op(field):
        return operate(field, stor, face_list, stride)

    solution = jnp.where(mask, WEIGHT * src / diagonal, 0.0)
    for sweep_number in range(NU - 1):
        solution = jnp.where(mask, solution + WEIGHT * (src - op(solution)) / diagonal, 0.0)
    residual = src - op(solution)
    scaled = jnp.where(mask, residual / diagonal, 0.0)
    smoothed = residual - WEIGHT * op(scaled)

    bx, by, bz = size_x // BOX, size_y // BOX, size_z // BOX
    live = lax.axis_index("grp") >= 0
    pick_x = box_matrix(bx, rows, 1, HALO, live)
    pick_yz = box_matrix(by * bz, span_y * span_z, span_z, HALO, live, bz).T
    box_totals = dot(pick_x, dot(smoothed, pick_yz)).reshape(-1)
    corner_ids = aggregate_ids[::BOX, ::BOX].reshape(bx * by, size_z).astype(source.dtype)
    first_z = lax.broadcasted_iota(jnp.int32, (size_z, bz), 0) == BOX * lax.broadcasted_iota(jnp.int32, (size_z, bz), 1)
    box_labels = dot(corner_ids, first_z.astype(source.dtype)).astype(jnp.int32).reshape(-1)
    placed = (
        box_labels[:, None] == lax.broadcasted_iota(jnp.int32, (box_labels.shape[0],) * 2, 1)
    ).astype(source.dtype)
    coarse_rhs = dot(box_totals[None, :], placed)[0]
    eye = lax.broadcasted_iota(jnp.int32, (64, 64), 0) == lax.broadcasted_iota(jnp.int32, (64, 64), 1)
    coarse_diag = jnp.sum(jnp.where(eye[None], coarse_values[:, :, :64], 0.0), axis=2).reshape(-1)
    block_rows = coarse_values.shape[0]
    grid_x = lax.axis_size("gx")
    grid_y = lax.axis_size("gy")
    groups = lax.axis_size("grp")
    tables = groups * grid_x * grid_y * block_rows
    pick = (
        coarse_columns.reshape(-1, 1) == lax.broadcasted_iota(jnp.int32, (coarse_columns.size, tables), 1)
    ).astype(source.dtype)
    coarse_error = coarse_rhs / coarse_diag
    for sweep_number in range(CITER - 1):
        pooled = everyone(coarse_error)
        blocks = dot(pick, pooled.reshape(tables, 64))
        blocks = blocks.reshape(block_rows, -1)
        applied = jnp.einsum(
            "bim,bm->bi", coarse_values, blocks, precision=lax.Precision.HIGHEST
        ).reshape(-1)
        coarse_error = coarse_error + (coarse_rhs - applied) / coarse_diag

    small = dot(placed, coarse_error[:, None]).reshape(-1)
    every = everyone(small).reshape(groups, grid_x, grid_y, bx, by, bz)
    boxes = every.transpose(1, 3, 2, 4, 0, 5).reshape(grid_x * bx, grid_y * by, groups * bz)
    boxes = jnp.pad(boxes, 1)
    window = lax.dynamic_slice(
        boxes,
        (lax.axis_index("gx") * bx, lax.axis_index("gy") * by, lax.axis_index("grp") * bz),
        (bx + 2, by + 2, bz + 2),
    )
    window = window.reshape(bx + 2, (by + 2) * (bz + 2))
    spread_x = box_matrix(bx + 2, rows, 1, 0, live).T
    spread_yz = box_matrix((by + 2) * (bz + 2), span_y * span_z, span_z, 0, live, bz + 2)
    lifted = dot(spread_x, dot(window, spread_yz))
    solution = jnp.where(mask, solution + (lifted - WEIGHT * op(lifted) / diagonal), 0.0)
    for sweep_number in range(NU):
        solution = jnp.where(mask, solution + WEIGHT * (src - op(solution)) / diagonal, 0.0)
    return (trimmed(solution, span_y, span_z), coarse_error)


def solution(mesh):
    return jax.shard_map(
        local,
        mesh=mesh,
        in_specs=(
            P("gx", "gy", "grp"),
            P("gx", "gy", "grp"),
            P("gx", "gy", "grp"),
            P("gx", "gy", "grp"),
            P(("grp", "gx", "gy"), None, None),
            P(("grp", "gx", "gy"), None),
        ),
        out_specs=(P("gx", "gy", "grp"), P(("grp", "gx", "gy"))),
        check_vma=False,
    )
```

```python
import jax
import jax.numpy as jnp
from jax import lax
from jax.sharding import PartitionSpec as P

NU = 2
CITER = 4
BOX = 4
HALO = 4

WEIGHT = 2.0 / 3.0
ALL_AXES = ("grp", "gx", "gy")
PAIRS = ((0, 1), (0, -1), (1, 1), (1, -1), (2, 1), (2, -1))


def padded_size(shape):
    size = -(-shape[-1] // 128) * 128
    if len(shape) > 1:
        size *= -(-shape[-2] // 8) * 8
    for extent in shape[:-2]:
        size *= extent
    return size


def permute(slab, axis, pairs):
    count = slab.size
    if count % 128 == 0 and padded_size(slab.shape) > count + count // 4:
        return lax.ppermute(slab.reshape(-1, 128), axis, pairs).reshape(slab.shape)
    return lax.ppermute(slab, axis, pairs)


def exchange(cells, sides, width):
    for axis, dim in sides:
        count = lax.axis_size(axis)
        size = cells.shape[dim]
        head = lax.slice_in_dim(cells, 0, width, axis=dim)
        tail = lax.slice_in_dim(cells, size - width, size, axis=dim)
        if count == 1:
            before = jnp.zeros_like(tail)
            after = jnp.zeros_like(head)
        elif count == 2:
            index = lax.axis_index(axis)
            sent = jnp.where(index == 0, tail, head)
            got = permute(sent, axis, [(0, 1), (1, 0)])
            before = jnp.where(index == 1, got, 0.0)
            after = jnp.where(index == 0, got, 0.0)
        elif count % 2 == 0:
            index = lax.axis_index(axis)
            even = index % 2 == 0
            first = [(i + d, i + 1 - d) for i in range(0, count, 2) for d in (0, 1)]
            second = [(i + d, i + 1 - d) for i in range(1, count - 1, 2) for d in (0, 1)]
            got_first = permute(jnp.where(even, tail, head), axis, first)
            got_second = permute(jnp.where(even, head, tail), axis, second)
            before = jnp.where(even, got_second, got_first)
            after = jnp.where(even, got_first, got_second)
        else:
            before = permute(tail, axis, [(i, i + 1) for i in range(count - 1)])
            after = permute(head, axis, [(i + 1, i) for i in range(count - 1)])
        cells = jnp.concatenate([before, cells, after], axis=dim)
    return cells


def flat_shift(padded, rows, width, stride, dx, dy, dz):
    lead = stride + dy * stride + dz
    return padded[1 + dx:1 + dx + rows, lead:lead + width]


def neighbours(field, stride):
    rows, width = field.shape
    padded = jnp.pad(field, ((1, 1), (stride, stride)))
    steps = ((1, 0, 0), (-1, 0, 0), (0, 1, 0), (0, -1, 0), (0, 0, 1), (0, 0, -1))
    return [flat_shift(padded, rows, width, stride, *step) for step in steps]


def face_terms(conductance, stride):
    return [0.5 * (conductance + other) for other in neighbours(conductance, stride)]


def operate(field, storage, face_list, stride):
    summed = storage * field
    for face, other in zip(face_list, neighbours(field, stride)):
        summed = summed + face * (field - other)
    return summed


def inside_mask(rows, span_y, span_z):
    shape = (rows, span_y * span_z)
    column = lax.broadcasted_iota(jnp.int32, shape, 1)
    coords = (
        (lax.broadcasted_iota(jnp.int32, shape, 0), rows, "gx"),
        (column // span_z, span_y, "gy"),
        (column % span_z, span_z, "grp"),
    )
    mask = None
    for local_index, span, axis in coords:
        block = span - 2 * HALO
        where = lax.axis_index(axis) * block - HALO + local_index
        ok = (where >= 0) & (where < block * lax.axis_size(axis))
        mask = ok if mask is None else mask & ok
    return mask


def trimmed(flat, span_y, span_z):
    cube = flat.reshape(flat.shape[0], span_y, span_z)
    return cube[HALO:-HALO, HALO:-HALO, HALO:-HALO]


def grp_pool(vector):
    groups = lax.axis_size("grp")
    index = lax.axis_index("grp")
    parts = [vector]
    for step in range(1, groups):
        parts.append(lax.ppermute(vector, "grp", [(i, (i + step) % groups) for i in range(groups)]))
    stacked = jnp.stack(parts)
    order = (index - jnp.arange(groups)) % groups
    return jnp.take(stacked, order, axis=0)


def dot(left, right):
    return jnp.dot(left, right, precision=lax.Precision.HIGHEST)


def split_parts(values):
    high = lax.reduce_precision(values, exponent_bits=8, mantissa_bits=7)
    rest = values - high
    middle = lax.reduce_precision(rest, exponent_bits=8, mantissa_bits=7)
    low = rest - middle
    return tuple(part.astype(jnp.bfloat16) for part in (high, middle, low))


def select_dot(left, right, ones_left):
    if ones_left:
        ones = left.astype(jnp.bfloat16)
        parts = [jnp.dot(ones, part, preferred_element_type=jnp.float32) for part in split_parts(right)]
    else:
        ones = right.astype(jnp.bfloat16)
        parts = [jnp.dot(part, ones, preferred_element_type=jnp.float32) for part in split_parts(left)]
    return (parts[0] + parts[1]) + parts[2]


def box_matrix(boxes, cells, stride, offset, live, inner=None):
    box = lax.broadcasted_iota(jnp.int32, (boxes, cells), 0)
    cell = lax.broadcasted_iota(jnp.int32, (boxes, cells), 1)
    if inner is None:
        hit = (cell - offset >= box * BOX) & (cell - offset < box * BOX + BOX)
    else:
        outer_cell, inner_cell = cell // stride - offset, cell % stride - offset
        outer_box, inner_box = box // inner, box % inner
        hit = (outer_cell >= outer_box * BOX) & (outer_cell < outer_box * BOX + BOX)
        hit = hit & (inner_cell >= inner_box * BOX) & (inner_cell < inner_box * BOX + BOX)
    return (hit & live).astype(jnp.float32)


def everyone(vector):
    count = lax.axis_size(ALL_AXES)
    copies = jnp.broadcast_to(vector[None], (count,) + vector.shape)
    return lax.all_to_all(copies, ALL_AXES, 0, 0, tiled=True).reshape(-1)


def local(source, conductance, storage, aggregate_ids, coarse_values, coarse_columns):
    size_x, size_y, size_z = source.shape
    assert HALO == BOX and HALO >= 2 * NU and HALO >= NU + 2
    stacked = jnp.stack([source, conductance, storage])
    wide = exchange(stacked, (("grp", 3),), HALO)
    span_z = wide.shape[3]
    stride = span_z
    wide = wide.reshape(3, size_x, size_y * span_z)
    wide = exchange(wide, (("gy", 2),), HALO * span_z)
    wide = exchange(wide, (("gx", 1),), HALO)
    rows = wide.shape[1]
    span_y = wide.shape[2] // span_z
    src, cond, stor = wide[0], wide[1], wide[2]
    mask = inside_mask(rows, span_y, span_z)
    face_list = face_terms(cond, stride)
    diagonal = stor
    for position in range(6):
        diagonal = diagonal + face_list[position]

    def op(field):
        return operate(field, stor, face_list, stride)

    solution = jnp.where(mask, WEIGHT * src / diagonal, 0.0)
    for sweep_number in range(NU - 1):
        solution = jnp.where(mask, solution + WEIGHT * (src - op(solution)) / diagonal, 0.0)
    residual = src - op(solution)
    scaled = jnp.where(mask, residual / diagonal, 0.0)
    smoothed = residual - WEIGHT * op(scaled)

    bx, by, bz = size_x // BOX, size_y // BOX, size_z // BOX
    live = lax.axis_index("grp") >= 0
    pick_x = box_matrix(bx, rows, 1, HALO, live)
    pick_yz = box_matrix(by * bz, span_y * span_z, span_z, HALO, live, bz).T
    box_totals = select_dot(pick_x, select_dot(smoothed, pick_yz, False), True).reshape(-1)
    corner_ids = aggregate_ids[::BOX, ::BOX].reshape(bx * by, size_z).astype(source.dtype)
    first_z = lax.broadcasted_iota(jnp.int32, (size_z, bz), 0) == BOX * lax.broadcasted_iota(jnp.int32, (size_z, bz), 1)
    box_labels = dot(corner_ids, first_z.astype(source.dtype)).astype(jnp.int32).reshape(-1)
    placed = (
        box_labels[:, None] == lax.broadcasted_iota(jnp.int32, (box_labels.shape[0],) * 2, 1)
    ).astype(source.dtype)
    coarse_rhs = select_dot(box_totals[None, :], placed, False)[0]
    eye = lax.broadcasted_iota(jnp.int32, (64, 64), 0) == lax.broadcasted_iota(jnp.int32, (64, 64), 1)
    coarse_diag = jnp.sum(jnp.where(eye[None], coarse_values[:, :, :64], 0.0), axis=2).reshape(-1)
    block_rows = coarse_values.shape[0]
    grid_x = lax.axis_size("gx")
    grid_y = lax.axis_size("gy")
    groups = lax.axis_size("grp")
    tables = groups * grid_x * grid_y * block_rows
    pick = (
        coarse_columns.reshape(-1, 1) == lax.broadcasted_iota(jnp.int32, (coarse_columns.size, tables), 1)
    ).astype(source.dtype)
    coarse_error = coarse_rhs / coarse_diag
    for sweep_number in range(CITER - 1):
        pooled = everyone(coarse_error)
        blocks = select_dot(pick, pooled.reshape(tables, 64), True)
        blocks = blocks.reshape(block_rows, -1)
        applied = jnp.einsum(
            "bim,bm->bi", coarse_values, blocks, precision=lax.Precision.HIGHEST
        ).reshape(-1)
        coarse_error = coarse_error + (coarse_rhs - applied) / coarse_diag

    small = select_dot(placed, coarse_error[:, None], True).reshape(-1)
    every = everyone(small).reshape(groups, grid_x, grid_y, bx, by, bz)
    boxes = every.transpose(1, 3, 2, 4, 0, 5).reshape(grid_x * bx, grid_y * by, groups * bz)
    boxes = jnp.pad(boxes, 1)
    window = lax.dynamic_slice(
        boxes,
        (lax.axis_index("gx") * bx, lax.axis_index("gy") * by, lax.axis_index("grp") * bz),
        (bx + 2, by + 2, bz + 2),
    )
    window = window.reshape(bx + 2, (by + 2) * (bz + 2))
    spread_x = box_matrix(bx + 2, rows, 1, 0, live).T
    spread_yz = box_matrix((by + 2) * (bz + 2), span_y * span_z, span_z, 0, live, bz + 2)
    lifted = select_dot(spread_x, select_dot(window, spread_yz, False), True)
    solution = jnp.where(mask, solution + (lifted - WEIGHT * op(lifted) / diagonal), 0.0)
    for sweep_number in range(NU):
        solution = jnp.where(mask, solution + WEIGHT * (src - op(solution)) / diagonal, 0.0)
    return (trimmed(solution, span_y, span_z), coarse_error)


def solution(mesh):
    return jax.shard_map(
        local,
        mesh=mesh,
        in_specs=(
            P("gx", "gy", "grp"),
            P("gx", "gy", "grp"),
            P("gx", "gy", "grp"),
            P("gx", "gy", "grp"),
            P(("grp", "gx", "gy"), None, None),
            P(("grp", "gx", "gy"), None),
        ),
        out_specs=(P("gx", "gy", "grp"), P(("grp", "gx", "gy"))),
        check_vma=False,
    )
```

```python
import jax
import jax.numpy as jnp
from jax import lax
from jax.sharding import PartitionSpec as P

NU = 2
CITER = 4
BOX = 4
HALO = 4

WEIGHT = 2.0 / 3.0
ALL_AXES = ("grp", "gx", "gy")
PAIRS = ((0, 1), (0, -1), (1, 1), (1, -1), (2, 1), (2, -1))


def padded_size(shape):
    size = -(-shape[-1] // 128) * 128
    if len(shape) > 1:
        size *= -(-shape[-2] // 8) * 8
    for extent in shape[:-2]:
        size *= extent
    return size


def permute(slab, axis, pairs):
    count = slab.size
    if count % 128 == 0 and padded_size(slab.shape) > count + count // 4:
        return lax.ppermute(slab.reshape(-1, 128), axis, pairs).reshape(slab.shape)
    return lax.ppermute(slab, axis, pairs)


def exchange(cells, sides, width):
    for axis, dim in sides:
        count = lax.axis_size(axis)
        size = cells.shape[dim]
        head = lax.slice_in_dim(cells, 0, width, axis=dim)
        tail = lax.slice_in_dim(cells, size - width, size, axis=dim)
        if count == 1:
            before = jnp.zeros_like(tail)
            after = jnp.zeros_like(head)
        elif count == 2:
            index = lax.axis_index(axis)
            sent = jnp.where(index == 0, tail, head)
            got = permute(sent, axis, [(0, 1), (1, 0)])
            before = jnp.where(index == 1, got, 0.0)
            after = jnp.where(index == 0, got, 0.0)
        elif count % 2 == 0:
            index = lax.axis_index(axis)
            even = index % 2 == 0
            first = [(i + d, i + 1 - d) for i in range(0, count, 2) for d in (0, 1)]
            second = [(i + d, i + 1 - d) for i in range(1, count - 1, 2) for d in (0, 1)]
            got_first = permute(jnp.where(even, tail, head), axis, first)
            got_second = permute(jnp.where(even, head, tail), axis, second)
            before = jnp.where(even, got_second, got_first)
            after = jnp.where(even, got_first, got_second)
        else:
            before = permute(tail, axis, [(i, i + 1) for i in range(count - 1)])
            after = permute(head, axis, [(i + 1, i) for i in range(count - 1)])
        cells = jnp.concatenate([before, cells, after], axis=dim)
    return cells


def flat_shift(padded, rows, width, stride, dx, dy, dz):
    lead = stride + dy * stride + dz
    return padded[1 + dx:1 + dx + rows, lead:lead + width]


def neighbours(field, stride):
    rows, width = field.shape
    padded = jnp.pad(field, ((1, 1), (stride, stride)))
    steps = ((1, 0, 0), (-1, 0, 0), (0, 1, 0), (0, -1, 0), (0, 0, 1), (0, 0, -1))
    return [flat_shift(padded, rows, width, stride, *step) for step in steps]


def face_terms(conductance, stride):
    return [0.5 * (conductance + other) for other in neighbours(conductance, stride)]


def operate(field, storage, face_list, stride):
    summed = storage * field
    for face, other in zip(face_list, neighbours(field, stride)):
        summed = summed + face * (field - other)
    return summed


def inside_mask(rows, span_y, span_z):
    shape = (rows, span_y * span_z)
    column = lax.broadcasted_iota(jnp.int32, shape, 1)
    coords = (
        (lax.broadcasted_iota(jnp.int32, shape, 0), rows, "gx"),
        (column // span_z, span_y, "gy"),
        (column % span_z, span_z, "grp"),
    )
    mask = None
    for local_index, span, axis in coords:
        block = span - 2 * HALO
        where = lax.axis_index(axis) * block - HALO + local_index
        ok = (where >= 0) & (where < block * lax.axis_size(axis))
        mask = ok if mask is None else mask & ok
    return mask


def trimmed(flat, span_y, span_z):
    cube = flat.reshape(flat.shape[0], span_y, span_z)
    return cube[HALO:-HALO, HALO:-HALO, HALO:-HALO]


def grp_pool(vector):
    groups = lax.axis_size("grp")
    index = lax.axis_index("grp")
    parts = [vector]
    for step in range(1, groups):
        parts.append(lax.ppermute(vector, "grp", [(i, (i + step) % groups) for i in range(groups)]))
    stacked = jnp.stack(parts)
    order = (index - jnp.arange(groups)) % groups
    return jnp.take(stacked, order, axis=0)


def dot(left, right):
    return jnp.dot(left, right, precision=lax.Precision.HIGHEST)


def box_matrix(boxes, cells, stride, offset, live, inner=None):
    box = lax.broadcasted_iota(jnp.int32, (boxes, cells), 0)
    cell = lax.broadcasted_iota(jnp.int32, (boxes, cells), 1)
    if inner is None:
        hit = (cell - offset >= box * BOX) & (cell - offset < box * BOX + BOX)
    else:
        outer_cell, inner_cell = cell // stride - offset, cell % stride - offset
        outer_box, inner_box = box // inner, box % inner
        hit = (outer_cell >= outer_box * BOX) & (outer_cell < outer_box * BOX + BOX)
        hit = hit & (inner_cell >= inner_box * BOX) & (inner_cell < inner_box * BOX + BOX)
    return (hit & live).astype(jnp.float32)


def everyone(vector):
    count = lax.axis_size(ALL_AXES)
    copies = jnp.broadcast_to(vector[None], (count,) + vector.shape)
    return lax.all_to_all(copies, ALL_AXES, 0, 0, tiled=True).reshape(-1)


def local(source, conductance, storage, aggregate_ids, coarse_values, coarse_columns):
    size_x, size_y, size_z = source.shape
    assert HALO == BOX and HALO >= 2 * NU and HALO >= NU + 2
    stacked = jnp.stack([source, conductance, storage])
    wide = exchange(stacked, (("grp", 3),), HALO)
    span_z = wide.shape[3]
    stride = span_z
    wide = wide.reshape(3, size_x, size_y * span_z)
    wide = exchange(wide, (("gy", 2),), HALO * span_z)
    wide = exchange(wide, (("gx", 1),), HALO)
    rows = wide.shape[1]
    span_y = wide.shape[2] // span_z
    src, cond, stor = wide[0], wide[1], wide[2]
    mask = inside_mask(rows, span_y, span_z)
    face_list = face_terms(cond, stride)
    diagonal = stor
    for position in range(6):
        diagonal = diagonal + face_list[position]

    def op(field):
        return operate(field, stor, face_list, stride)

    solution = jnp.where(mask, WEIGHT * src / diagonal, 0.0)
    for sweep_number in range(NU - 1):
        solution = jnp.where(mask, solution + WEIGHT * (src - op(solution)) / diagonal, 0.0)
    residual = src - op(solution)
    scaled = jnp.where(mask, residual / diagonal, 0.0)
    smoothed = residual - WEIGHT * op(scaled)

    bx, by, bz = size_x // BOX, size_y // BOX, size_z // BOX
    live = lax.axis_index("grp") >= 0
    pick_x = box_matrix(bx, rows, 1, HALO, live)
    pick_yz = box_matrix(by * bz, span_y * span_z, span_z, HALO, live, bz).T
    box_totals = dot(pick_x, dot(smoothed, pick_yz)).reshape(-1)
    box_labels = aggregate_ids[::BOX, ::BOX, ::BOX].reshape(-1)
    placed = (
        box_labels[:, None] == lax.broadcasted_iota(jnp.int32, (box_labels.shape[0],) * 2, 1)
    ).astype(source.dtype)
    coarse_rhs = dot(box_totals[None, :], placed)[0]
    eye = lax.broadcasted_iota(jnp.int32, (64, 64), 0) == lax.broadcasted_iota(jnp.int32, (64, 64), 1)
    coarse_diag = jnp.sum(jnp.where(eye[None], coarse_values[:, :, :64], 0.0), axis=2).reshape(-1)
    block_rows = coarse_values.shape[0]
    grid_x = lax.axis_size("gx")
    grid_y = lax.axis_size("gy")
    groups = lax.axis_size("grp")
    devices = groups * grid_x * grid_y
    column_list = coarse_columns.reshape(-1, 1)
    pick = (
        column_list // block_rows == lax.broadcasted_iota(jnp.int32, (column_list.shape[0], devices), 1)
    ).astype(source.dtype)
    within = column_list % block_rows
    coarse_error = coarse_rhs / coarse_diag
    for sweep_number in range(CITER - 1):
        pooled = everyone(coarse_error)
        rows_of = dot(pick, pooled.reshape(devices, -1))
        blocks = rows_of[:, :64]
        for part in range(1, block_rows):
            blocks = jnp.where(within == part, rows_of[:, part * 64:(part + 1) * 64], blocks)
        blocks = blocks.reshape(block_rows, -1)
        applied = jnp.einsum(
            "bim,bm->bi", coarse_values, blocks, precision=lax.Precision.HIGHEST
        ).reshape(-1)
        coarse_error = coarse_error + (coarse_rhs - applied) / coarse_diag

    small = dot(placed, coarse_error[:, None]).reshape(-1)
    every = everyone(small).reshape(groups, grid_x, grid_y, bx, by, bz)
    boxes = every.transpose(1, 3, 2, 4, 0, 5).reshape(grid_x * bx, grid_y * by, groups * bz)
    boxes = jnp.pad(boxes, 1)
    window = lax.dynamic_slice(
        boxes,
        (lax.axis_index("gx") * bx, lax.axis_index("gy") * by, lax.axis_index("grp") * bz),
        (bx + 2, by + 2, bz + 2),
    )
    window = window.reshape(bx + 2, (by + 2) * (bz + 2))
    spread_x = box_matrix(bx + 2, rows, 1, 0, live).T
    spread_yz = box_matrix((by + 2) * (bz + 2), span_y * span_z, span_z, 0, live, bz + 2)
    lifted = dot(spread_x, dot(window, spread_yz))
    solution = jnp.where(mask, solution + (lifted - WEIGHT * op(lifted) / diagonal), 0.0)
    for sweep_number in range(NU):
        solution = jnp.where(mask, solution + WEIGHT * (src - op(solution)) / diagonal, 0.0)
    return (trimmed(solution, span_y, span_z), coarse_error)


def solution(mesh):
    return jax.shard_map(
        local,
        mesh=mesh,
        in_specs=(
            P("gx", "gy", "grp"),
            P("gx", "gy", "grp"),
            P("gx", "gy", "grp"),
            P("gx", "gy", "grp"),
            P(("grp", "gx", "gy"), None, None),
            P(("grp", "gx", "gy"), None),
        ),
        out_specs=(P("gx", "gy", "grp"), P(("grp", "gx", "gy"))),
        check_vma=False,
    )
```

```python
import jax
import jax.numpy as jnp
from jax import lax
from jax.sharding import PartitionSpec as P

NU = 2
CITER = 4
BOX = 4
HALO = 4

WEIGHT = 2.0 / 3.0
ALL_AXES = ("grp", "gx", "gy")
PAIRS = ((0, 1), (0, -1), (1, 1), (1, -1), (2, 1), (2, -1))


def padded_size(shape):
    size = -(-shape[-1] // 128) * 128
    if len(shape) > 1:
        size *= -(-shape[-2] // 8) * 8
    for extent in shape[:-2]:
        size *= extent
    return size


def permute(slab, axis, pairs):
    count = slab.size
    if count % 128 == 0 and padded_size(slab.shape) > count + count // 4:
        return lax.ppermute(slab.reshape(-1, 128), axis, pairs).reshape(slab.shape)
    return lax.ppermute(slab, axis, pairs)


def exchange(cells, sides, width):
    for axis, dim in sides:
        count = lax.axis_size(axis)
        size = cells.shape[dim]
        head = lax.slice_in_dim(cells, 0, width, axis=dim)
        tail = lax.slice_in_dim(cells, size - width, size, axis=dim)
        if count == 1:
            before = jnp.zeros_like(tail)
            after = jnp.zeros_like(head)
        elif count == 2:
            index = lax.axis_index(axis)
            sent = jnp.where(index == 0, tail, head)
            got = permute(sent, axis, [(0, 1), (1, 0)])
            before = jnp.where(index == 1, got, 0.0)
            after = jnp.where(index == 0, got, 0.0)
        elif count % 2 == 0:
            index = lax.axis_index(axis)
            even = index % 2 == 0
            first = [(i + d, i + 1 - d) for i in range(0, count, 2) for d in (0, 1)]
            second = [(i + d, i + 1 - d) for i in range(1, count - 1, 2) for d in (0, 1)]
            got_first = permute(jnp.where(even, tail, head), axis, first)
            got_second = permute(jnp.where(even, head, tail), axis, second)
            before = jnp.where(even, got_second, got_first)
            after = jnp.where(even, got_first, got_second)
        else:
            before = permute(tail, axis, [(i, i + 1) for i in range(count - 1)])
            after = permute(head, axis, [(i + 1, i) for i in range(count - 1)])
        cells = jnp.concatenate([before, cells, after], axis=dim)
    return cells


def flat_shift(padded, rows, width, stride, dx, dy, dz):
    lead = stride + dy * stride + dz
    return padded[1 + dx:1 + dx + rows, lead:lead + width]


def neighbours(field, stride):
    rows, width = field.shape
    padded = jnp.pad(field, ((1, 1), (stride, stride)))
    steps = ((1, 0, 0), (-1, 0, 0), (0, 1, 0), (0, -1, 0), (0, 0, 1), (0, 0, -1))
    return [flat_shift(padded, rows, width, stride, *step) for step in steps]


def face_terms(conductance, stride):
    return [0.5 * (conductance + other) for other in neighbours(conductance, stride)]


def operate(field, storage, face_list, stride):
    summed = storage * field
    for face, other in zip(face_list, neighbours(field, stride)):
        summed = summed + face * (field - other)
    return summed


def inside_mask(rows, span_y, span_z):
    shape = (rows, span_y * span_z)
    column = lax.broadcasted_iota(jnp.int32, shape, 1)
    coords = (
        (lax.broadcasted_iota(jnp.int32, shape, 0), rows, "gx"),
        (column // span_z, span_y, "gy"),
        (column % span_z, span_z, "grp"),
    )
    mask = None
    for local_index, span, axis in coords:
        block = span - 2 * HALO
        where = lax.axis_index(axis) * block - HALO + local_index
        ok = (where >= 0) & (where < block * lax.axis_size(axis))
        mask = ok if mask is None else mask & ok
    return mask


def trimmed(flat, span_y, span_z):
    cube = flat.reshape(flat.shape[0], span_y, span_z)
    return cube[HALO:-HALO, HALO:-HALO, HALO:-HALO]


def grp_pool(vector):
    groups = lax.axis_size("grp")
    index = lax.axis_index("grp")
    parts = [vector]
    for step in range(1, groups):
        parts.append(lax.ppermute(vector, "grp", [(i, (i + step) % groups) for i in range(groups)]))
    stacked = jnp.stack(parts)
    order = (index - jnp.arange(groups)) % groups
    return jnp.take(stacked, order, axis=0)


def dot(left, right):
    return jnp.dot(left, right, precision=lax.Precision.HIGHEST)


def box_matrix(boxes, cells, stride, offset, live, inner=None):
    box = lax.broadcasted_iota(jnp.int32, (boxes, cells), 0)
    cell = lax.broadcasted_iota(jnp.int32, (boxes, cells), 1)
    if inner is None:
        hit = (cell - offset >= box * BOX) & (cell - offset < box * BOX + BOX)
    else:
        outer_cell, inner_cell = cell // stride - offset, cell % stride - offset
        outer_box, inner_box = box // inner, box % inner
        hit = (outer_cell >= outer_box * BOX) & (outer_cell < outer_box * BOX + BOX)
        hit = hit & (inner_cell >= inner_box * BOX) & (inner_cell < inner_box * BOX + BOX)
    return (hit & live).astype(jnp.float32)


def everyone(vector):
    count = lax.axis_size(ALL_AXES)
    copies = jnp.broadcast_to(vector[None], (count,) + vector.shape)
    return lax.all_to_all(copies, ALL_AXES, 0, 0, tiled=True).reshape(-1)


def local(source, conductance, storage, aggregate_ids, coarse_values, coarse_columns):
    size_x, size_y, size_z = source.shape
    assert HALO == BOX and HALO >= 2 * NU and HALO >= NU + 2
    stacked = jnp.stack([source, conductance, storage])
    wide = exchange(stacked, (("grp", 3),), HALO)
    span_z = wide.shape[3]
    stride = span_z
    wide = wide.reshape(3, size_x, size_y * span_z)
    wide = exchange(wide, (("gy", 2),), HALO * span_z)
    wide = exchange(wide, (("gx", 1),), HALO)
    rows = wide.shape[1]
    span_y = wide.shape[2] // span_z
    src, cond, stor = wide[0], wide[1], wide[2]
    mask = inside_mask(rows, span_y, span_z)
    face_list = face_terms(cond, stride)
    diagonal = stor
    for position in range(6):
        diagonal = diagonal + face_list[position]

    def op(field):
        return operate(field, stor, face_list, stride)

    solution = jnp.where(mask, WEIGHT * src / diagonal, 0.0)
    for sweep_number in range(NU - 1):
        solution = jnp.where(mask, solution + WEIGHT * (src - op(solution)) / diagonal, 0.0)
    residual = src - op(solution)
    scaled = jnp.where(mask, residual / diagonal, 0.0)
    smoothed = residual - WEIGHT * op(scaled)

    bx, by, bz = size_x // BOX, size_y // BOX, size_z // BOX
    live = lax.axis_index("grp") >= 0
    pick_x = box_matrix(bx, rows, 1, HALO, live)
    pick_yz = box_matrix(by * bz, span_y * span_z, span_z, HALO, live, bz).T
    box_totals = dot(pick_x, dot(smoothed, pick_yz)).reshape(-1)
    box_labels = aggregate_ids[::BOX, ::BOX, ::BOX].reshape(-1)
    placed = box_labels[:, None] == lax.broadcasted_iota(jnp.int32, (box_labels.shape[0],) * 2, 1)
    coarse_rhs = jnp.sum(jnp.where(placed, box_totals[:, None], 0.0), axis=0)
    eye = lax.broadcasted_iota(jnp.int32, (64, 64), 0) == lax.broadcasted_iota(jnp.int32, (64, 64), 1)
    coarse_diag = jnp.sum(jnp.where(eye[None], coarse_values[:, :, :64], 0.0), axis=2).reshape(-1)
    block_rows = coarse_values.shape[0]
    grid_x = lax.axis_size("gx")
    grid_y = lax.axis_size("gy")
    groups = lax.axis_size("grp")
    devices = groups * grid_x * grid_y
    column_list = coarse_columns.reshape(-1, 1)
    pick = (
        column_list // block_rows == lax.broadcasted_iota(jnp.int32, (column_list.shape[0], devices), 1)
    ).astype(source.dtype)
    within = column_list % block_rows
    coarse_error = coarse_rhs / coarse_diag
    for sweep_number in range(CITER - 1):
        pooled = everyone(coarse_error)
        rows_of = dot(pick, pooled.reshape(devices, -1))
        blocks = rows_of[:, :64]
        for part in range(1, block_rows):
            blocks = jnp.where(within == part, rows_of[:, part * 64:(part + 1) * 64], blocks)
        blocks = blocks.reshape(block_rows, -1)
        applied = jnp.einsum(
            "bim,bm->bi", coarse_values, blocks, precision=lax.Precision.HIGHEST
        ).reshape(-1)
        coarse_error = coarse_error + (coarse_rhs - applied) / coarse_diag

    small = jnp.sum(jnp.where(placed, coarse_error[None, :], 0.0), axis=1)
    every = everyone(small).reshape(groups, grid_x, grid_y, bx, by, bz)
    boxes = every.transpose(1, 3, 2, 4, 0, 5).reshape(grid_x * bx, grid_y * by, groups * bz)
    boxes = jnp.pad(boxes, 1)
    window = lax.dynamic_slice(
        boxes,
        (lax.axis_index("gx") * bx, lax.axis_index("gy") * by, lax.axis_index("grp") * bz),
        (bx + 2, by + 2, bz + 2),
    )
    window = window.reshape(bx + 2, (by + 2) * (bz + 2))
    spread_x = box_matrix(bx + 2, rows, 1, 0, live).T
    spread_yz = box_matrix((by + 2) * (bz + 2), span_y * span_z, span_z, 0, live, bz + 2)
    lifted = dot(spread_x, dot(window, spread_yz))
    solution = jnp.where(mask, solution + (lifted - WEIGHT * op(lifted) / diagonal), 0.0)
    for sweep_number in range(NU):
        solution = jnp.where(mask, solution + WEIGHT * (src - op(solution)) / diagonal, 0.0)
    return (trimmed(solution, span_y, span_z), coarse_error)


def solution(mesh):
    return jax.shard_map(
        local,
        mesh=mesh,
        in_specs=(
            P("gx", "gy", "grp"),
            P("gx", "gy", "grp"),
            P("gx", "gy", "grp"),
            P("gx", "gy", "grp"),
            P(("grp", "gx", "gy"), None, None),
            P(("grp", "gx", "gy"), None),
        ),
        out_specs=(P("gx", "gy", "grp"), P(("grp", "gx", "gy"))),
        check_vma=False,
    )
```

```python
import jax
import jax.numpy as jnp
from jax import lax
from jax.sharding import PartitionSpec as P

NU = 2
CITER = 4
BOX = 4
HALO = 4

WEIGHT = 2.0 / 3.0
ALL_AXES = ("grp", "gx", "gy")
PAIRS = ((0, 1), (0, -1), (1, 1), (1, -1), (2, 1), (2, -1))


def padded_size(shape):
    size = -(-shape[-1] // 128) * 128
    if len(shape) > 1:
        size *= -(-shape[-2] // 8) * 8
    for extent in shape[:-2]:
        size *= extent
    return size


def permute(slab, axis, pairs):
    count = slab.size
    if count % 128 == 0 and padded_size(slab.shape) > count + count // 4:
        return lax.ppermute(slab.reshape(-1, 128), axis, pairs).reshape(slab.shape)
    return lax.ppermute(slab, axis, pairs)


def exchange(cells, sides, width):
    for axis, dim in sides:
        count = lax.axis_size(axis)
        size = cells.shape[dim]
        head = lax.slice_in_dim(cells, 0, width, axis=dim)
        tail = lax.slice_in_dim(cells, size - width, size, axis=dim)
        if count == 1:
            before = jnp.zeros_like(tail)
            after = jnp.zeros_like(head)
        elif count == 2:
            index = lax.axis_index(axis)
            sent = jnp.where(index == 0, tail, head)
            got = permute(sent, axis, [(0, 1), (1, 0)])
            before = jnp.where(index == 1, got, 0.0)
            after = jnp.where(index == 0, got, 0.0)
        elif count % 2 == 0:
            index = lax.axis_index(axis)
            even = index % 2 == 0
            first = [(i + d, i + 1 - d) for i in range(0, count, 2) for d in (0, 1)]
            second = [(i + d, i + 1 - d) for i in range(1, count - 1, 2) for d in (0, 1)]
            got_first = permute(jnp.where(even, tail, head), axis, first)
            got_second = permute(jnp.where(even, head, tail), axis, second)
            before = jnp.where(even, got_second, got_first)
            after = jnp.where(even, got_first, got_second)
        else:
            before = permute(tail, axis, [(i, i + 1) for i in range(count - 1)])
            after = permute(head, axis, [(i + 1, i) for i in range(count - 1)])
        cells = jnp.concatenate([before, cells, after], axis=dim)
    return cells


def flat_shift(padded, rows, width, stride, dx, dy, dz):
    lead = stride + dy * stride + dz
    return padded[1 + dx:1 + dx + rows, lead:lead + width]


def neighbours(field, stride):
    rows, width = field.shape
    padded = jnp.pad(field, ((1, 1), (stride, stride)))
    steps = ((1, 0, 0), (-1, 0, 0), (0, 1, 0), (0, -1, 0), (0, 0, 1), (0, 0, -1))
    return [flat_shift(padded, rows, width, stride, *step) for step in steps]


def face_terms(conductance, stride):
    return [0.5 * (conductance + other) for other in neighbours(conductance, stride)]


def operate(field, storage, face_list, stride):
    summed = storage * field
    for face, other in zip(face_list, neighbours(field, stride)):
        summed = summed + face * (field - other)
    return summed


def inside_mask(rows, span_y, span_z):
    shape = (rows, span_y * span_z)
    column = lax.broadcasted_iota(jnp.int32, shape, 1)
    coords = (
        (lax.broadcasted_iota(jnp.int32, shape, 0), rows, "gx"),
        (column // span_z, span_y, "gy"),
        (column % span_z, span_z, "grp"),
    )
    mask = None
    for local_index, span, axis in coords:
        block = span - 2 * HALO
        where = lax.axis_index(axis) * block - HALO + local_index
        ok = (where >= 0) & (where < block * lax.axis_size(axis))
        mask = ok if mask is None else mask & ok
    return mask


def trimmed(flat, span_y, span_z):
    cube = flat.reshape(flat.shape[0], span_y, span_z)
    return cube[HALO:-HALO, HALO:-HALO, HALO:-HALO]


def grp_pool(vector):
    groups = lax.axis_size("grp")
    index = lax.axis_index("grp")
    parts = [vector]
    for step in range(1, groups):
        parts.append(lax.ppermute(vector, "grp", [(i, (i + step) % groups) for i in range(groups)]))
    stacked = jnp.stack(parts)
    order = (index - jnp.arange(groups)) % groups
    return jnp.take(stacked, order, axis=0)


def dot(left, right):
    return jnp.dot(left, right, precision=lax.Precision.HIGHEST)


def box_matrix(boxes, cells, stride, offset, live, inner=None):
    box = lax.broadcasted_iota(jnp.int32, (boxes, cells), 0)
    cell = lax.broadcasted_iota(jnp.int32, (boxes, cells), 1)
    if inner is None:
        hit = (cell - offset >= box * BOX) & (cell - offset < box * BOX + BOX)
    else:
        outer_cell, inner_cell = cell // stride - offset, cell % stride - offset
        outer_box, inner_box = box // inner, box % inner
        hit = (outer_cell >= outer_box * BOX) & (outer_cell < outer_box * BOX + BOX)
        hit = hit & (inner_cell >= inner_box * BOX) & (inner_cell < inner_box * BOX + BOX)
    return (hit & live).astype(jnp.float32)


def everyone(vector):
    count = lax.axis_size(ALL_AXES)
    copies = jnp.broadcast_to(vector[None], (count,) + vector.shape)
    return lax.all_to_all(copies, ALL_AXES, 0, 0, tiled=True).reshape(-1)


def local(source, conductance, storage, aggregate_ids, coarse_values, coarse_columns):
    size_x, size_y, size_z = source.shape
    assert HALO == BOX and HALO >= 2 * NU and HALO >= NU + 2
    stacked = jnp.stack([source, conductance, storage])
    wide = exchange(stacked, (("grp", 3),), HALO)
    span_z = wide.shape[3]
    stride = span_z
    wide = wide.reshape(3, size_x, size_y * span_z)
    wide = exchange(wide, (("gy", 2),), HALO * span_z)
    wide = exchange(wide, (("gx", 1),), HALO)
    rows = wide.shape[1]
    span_y = wide.shape[2] // span_z
    src, cond, stor = wide[0], wide[1], wide[2]
    mask = inside_mask(rows, span_y, span_z)
    face_list = face_terms(cond, stride)
    diagonal = stor
    for position in range(6):
        diagonal = diagonal + face_list[position]

    def op(field):
        return operate(field, stor, face_list, stride)

    solution = jnp.where(mask, WEIGHT * src / diagonal, 0.0)
    for sweep_number in range(NU - 1):
        solution = jnp.where(mask, solution + WEIGHT * (src - op(solution)) / diagonal, 0.0)
    residual = src - op(solution)
    scaled = jnp.where(mask, residual / diagonal, 0.0)
    smoothed = residual - WEIGHT * op(scaled)

    bx, by, bz = size_x // BOX, size_y // BOX, size_z // BOX
    live = lax.axis_index("grp") >= 0
    pick_x = box_matrix(bx, rows, 1, HALO, live)
    pick_yz = box_matrix(by * bz, span_y * span_z, span_z, HALO, live, bz).T
    box_totals = dot(pick_x, dot(smoothed, pick_yz)).reshape(-1)
    corner_ids = aggregate_ids[::BOX, ::BOX].reshape(bx * by, size_z).astype(source.dtype)
    first_z = lax.broadcasted_iota(jnp.int32, (size_z, bz), 0) == BOX * lax.broadcasted_iota(jnp.int32, (size_z, bz), 1)
    box_labels = dot(corner_ids, first_z.astype(source.dtype)).astype(jnp.int32).reshape(-1)
    placed = box_labels[:, None] == lax.broadcasted_iota(jnp.int32, (box_labels.shape[0],) * 2, 1)
    coarse_rhs = jnp.sum(jnp.where(placed, box_totals[:, None], 0.0), axis=0)
    eye = lax.broadcasted_iota(jnp.int32, (64, 64), 0) == lax.broadcasted_iota(jnp.int32, (64, 64), 1)
    coarse_diag = jnp.sum(jnp.where(eye[None], coarse_values[:, :, :64], 0.0), axis=2).reshape(-1)
    block_rows = coarse_values.shape[0]
    grid_x = lax.axis_size("gx")
    grid_y = lax.axis_size("gy")
    groups = lax.axis_size("grp")
    devices = groups * grid_x * grid_y
    column_list = coarse_columns.reshape(-1, 1)
    pick = (
        column_list // block_rows == lax.broadcasted_iota(jnp.int32, (column_list.shape[0], devices), 1)
    ).astype(source.dtype)
    within = column_list % block_rows
    coarse_error = coarse_rhs / coarse_diag
    for sweep_number in range(CITER - 1):
        pooled = everyone(coarse_error)
        rows_of = dot(pick, pooled.reshape(devices, -1))
        blocks = rows_of[:, :64]
        for part in range(1, block_rows):
            blocks = jnp.where(within == part, rows_of[:, part * 64:(part + 1) * 64], blocks)
        blocks = blocks.reshape(block_rows, -1)
        applied = jnp.einsum(
            "bim,bm->bi", coarse_values, blocks, precision=lax.Precision.HIGHEST
        ).reshape(-1)
        coarse_error = coarse_error + (coarse_rhs - applied) / coarse_diag

    small = jnp.sum(jnp.where(placed, coarse_error[None, :], 0.0), axis=1)
    every = everyone(small).reshape(groups, grid_x, grid_y, bx, by, bz)
    boxes = every.transpose(1, 3, 2, 4, 0, 5).reshape(grid_x * bx, grid_y * by, groups * bz)
    boxes = jnp.pad(boxes, 1)
    window = lax.dynamic_slice(
        boxes,
        (lax.axis_index("gx") * bx, lax.axis_index("gy") * by, lax.axis_index("grp") * bz),
        (bx + 2, by + 2, bz + 2),
    )
    window = window.reshape(bx + 2, (by + 2) * (bz + 2))
    spread_x = box_matrix(bx + 2, rows, 1, 0, live).T
    spread_yz = box_matrix((by + 2) * (bz + 2), span_y * span_z, span_z, 0, live, bz + 2)
    lifted = dot(spread_x, dot(window, spread_yz))
    solution = jnp.where(mask, solution + (lifted - WEIGHT * op(lifted) / diagonal), 0.0)
    for sweep_number in range(NU):
        solution = jnp.where(mask, solution + WEIGHT * (src - op(solution)) / diagonal, 0.0)
    return (trimmed(solution, span_y, span_z), coarse_error)


def solution(mesh):
    return jax.shard_map(
        local,
        mesh=mesh,
        in_specs=(
            P("gx", "gy", "grp"),
            P("gx", "gy", "grp"),
            P("gx", "gy", "grp"),
            P("gx", "gy", "grp"),
            P(("grp", "gx", "gy"), None, None),
            P(("grp", "gx", "gy"), None),
        ),
        out_specs=(P("gx", "gy", "grp"), P(("grp", "gx", "gy"))),
        check_vma=False,
    )
```

```python
import jax
import jax.numpy as jnp
from jax import lax
from jax.sharding import PartitionSpec as P

NU = 2
CITER = 4
BOX = 4
HALO = 4

WEIGHT = 2.0 / 3.0
ALL_AXES = ("grp", "gx", "gy")
PAIRS = ((0, 1), (0, -1), (1, 1), (1, -1), (2, 1), (2, -1))


def padded_size(shape):
    size = -(-shape[-1] // 128) * 128
    if len(shape) > 1:
        size *= -(-shape[-2] // 8) * 8
    for extent in shape[:-2]:
        size *= extent
    return size


def permute(slab, axis, pairs):
    count = slab.size
    if count % 128 == 0 and padded_size(slab.shape) > count + count // 4:
        return lax.ppermute(slab.reshape(-1, 128), axis, pairs).reshape(slab.shape)
    return lax.ppermute(slab, axis, pairs)


def exchange(cells, sides, width):
    for axis, dim in sides:
        count = lax.axis_size(axis)
        size = cells.shape[dim]
        head = lax.slice_in_dim(cells, 0, width, axis=dim)
        tail = lax.slice_in_dim(cells, size - width, size, axis=dim)
        if count == 1:
            before = jnp.zeros_like(tail)
            after = jnp.zeros_like(head)
        elif count == 2:
            index = lax.axis_index(axis)
            sent = jnp.where(index == 0, tail, head)
            got = permute(sent, axis, [(0, 1), (1, 0)])
            before = jnp.where(index == 1, got, 0.0)
            after = jnp.where(index == 0, got, 0.0)
        elif count % 2 == 0:
            index = lax.axis_index(axis)
            even = index % 2 == 0
            first = [(i + d, i + 1 - d) for i in range(0, count, 2) for d in (0, 1)]
            second = [(i + d, i + 1 - d) for i in range(1, count - 1, 2) for d in (0, 1)]
            got_first = permute(jnp.where(even, tail, head), axis, first)
            got_second = permute(jnp.where(even, head, tail), axis, second)
            before = jnp.where(even, got_second, got_first)
            after = jnp.where(even, got_first, got_second)
        else:
            before = permute(tail, axis, [(i, i + 1) for i in range(count - 1)])
            after = permute(head, axis, [(i + 1, i) for i in range(count - 1)])
        cells = jnp.concatenate([before, cells, after], axis=dim)
    return cells


def flat_shift(padded, rows, width, stride, dx, dy, dz):
    lead = stride + dy * stride + dz
    return padded[1 + dx:1 + dx + rows, lead:lead + width]


def neighbours(field, stride):
    rows, width = field.shape
    padded = jnp.pad(field, ((1, 1), (stride, stride)))
    steps = ((1, 0, 0), (-1, 0, 0), (0, 1, 0), (0, -1, 0), (0, 0, 1), (0, 0, -1))
    return [flat_shift(padded, rows, width, stride, *step) for step in steps]


def face_terms(conductance, stride):
    return [0.5 * (conductance + other) for other in neighbours(conductance, stride)]


def operate(field, storage, face_list, stride):
    summed = storage * field
    for face, other in zip(face_list, neighbours(field, stride)):
        summed = summed + face * (field - other)
    return summed


def inside_mask(rows, span_y, span_z):
    shape = (rows, span_y * span_z)
    column = lax.broadcasted_iota(jnp.int32, shape, 1)
    coords = (
        (lax.broadcasted_iota(jnp.int32, shape, 0), rows, "gx"),
        (column // span_z, span_y, "gy"),
        (column % span_z, span_z, "grp"),
    )
    mask = None
    for local_index, span, axis in coords:
        block = span - 2 * HALO
        where = lax.axis_index(axis) * block - HALO + local_index
        ok = (where >= 0) & (where < block * lax.axis_size(axis))
        mask = ok if mask is None else mask & ok
    return mask


def trimmed(flat, span_y, span_z):
    cube = flat.reshape(flat.shape[0], span_y, span_z)
    return cube[HALO:-HALO, HALO:-HALO, HALO:-HALO]


def grp_pool(vector):
    groups = lax.axis_size("grp")
    index = lax.axis_index("grp")
    parts = [vector]
    for step in range(1, groups):
        parts.append(lax.ppermute(vector, "grp", [(i, (i + step) % groups) for i in range(groups)]))
    stacked = jnp.stack(parts)
    order = (index - jnp.arange(groups)) % groups
    return jnp.take(stacked, order, axis=0)


def dot(left, right):
    return jnp.dot(left, right, precision=lax.Precision.HIGHEST)


def box_matrix(boxes, cells, stride, offset, live, inner=None):
    cell = lax.broadcasted_iota(jnp.int32, (1, cells), 1)
    if inner is None:
        local = cell - offset
        owner = jnp.where((local >= 0) & (local < boxes * BOX), local // BOX, -1)
    else:
        outer_cell, inner_cell = cell // stride - offset, cell % stride - offset
        inside = (outer_cell >= 0) & (outer_cell < (boxes // inner) * BOX)
        inside = inside & (inner_cell >= 0) & (inner_cell < inner * BOX)
        owner = jnp.where(inside, (outer_cell // BOX) * inner + inner_cell // BOX, -1)
    box = lax.broadcasted_iota(jnp.int32, (boxes, cells), 0)
    return ((box == owner) & live).astype(jnp.float32)


def everyone(vector):
    count = lax.axis_size(ALL_AXES)
    copies = jnp.broadcast_to(vector[None], (count,) + vector.shape)
    return lax.all_to_all(copies, ALL_AXES, 0, 0, tiled=True).reshape(-1)


def local(source, conductance, storage, aggregate_ids, coarse_values, coarse_columns):
    size_x, size_y, size_z = source.shape
    assert HALO == BOX and HALO >= 2 * NU and HALO >= NU + 2
    stacked = jnp.stack([source, conductance, storage])
    wide = exchange(stacked, (("grp", 3),), HALO)
    span_z = wide.shape[3]
    stride = span_z
    wide = wide.reshape(3, size_x, size_y * span_z)
    wide = exchange(wide, (("gy", 2),), HALO * span_z)
    wide = exchange(wide, (("gx", 1),), HALO)
    rows = wide.shape[1]
    span_y = wide.shape[2] // span_z
    src, cond, stor = wide[0], wide[1], wide[2]
    mask = inside_mask(rows, span_y, span_z)
    face_list = face_terms(cond, stride)
    diagonal = stor
    for position in range(6):
        diagonal = diagonal + face_list[position]

    def op(field):
        return operate(field, stor, face_list, stride)

    solution = jnp.where(mask, WEIGHT * src / diagonal, 0.0)
    for sweep_number in range(NU - 1):
        solution = jnp.where(mask, solution + WEIGHT * (src - op(solution)) / diagonal, 0.0)
    residual = src - op(solution)
    scaled = jnp.where(mask, residual / diagonal, 0.0)
    smoothed = residual - WEIGHT * op(scaled)

    bx, by, bz = size_x // BOX, size_y // BOX, size_z // BOX
    live = lax.axis_index("grp") >= 0
    pick_x = box_matrix(bx, rows, 1, HALO, live)
    pick_yz = box_matrix(by * bz, span_y * span_z, span_z, HALO, live, bz).T
    box_totals = dot(pick_x, dot(smoothed, pick_yz)).reshape(-1)
    box_labels = aggregate_ids[::BOX, ::BOX, ::BOX].reshape(-1)
    placed = box_labels[:, None] == lax.broadcasted_iota(jnp.int32, (box_labels.shape[0],) * 2, 1)
    coarse_rhs = jnp.sum(jnp.where(placed, box_totals[:, None], 0.0), axis=0)
    eye = lax.broadcasted_iota(jnp.int32, (64, 64), 0) == lax.broadcasted_iota(jnp.int32, (64, 64), 1)
    coarse_diag = jnp.sum(jnp.where(eye[None], coarse_values[:, :, :64], 0.0), axis=2).reshape(-1)
    block_rows = coarse_values.shape[0]
    grid_x = lax.axis_size("gx")
    grid_y = lax.axis_size("gy")
    groups = lax.axis_size("grp")
    devices = groups * grid_x * grid_y
    column_list = coarse_columns.reshape(-1, 1)
    pick = (
        column_list // block_rows == lax.broadcasted_iota(jnp.int32, (column_list.shape[0], devices), 1)
    ).astype(source.dtype)
    within = column_list % block_rows
    coarse_error = coarse_rhs / coarse_diag
    for sweep_number in range(CITER - 1):
        pooled = everyone(coarse_error)
        rows_of = dot(pick, pooled.reshape(devices, -1))
        blocks = rows_of[:, :64]
        for part in range(1, block_rows):
            blocks = jnp.where(within == part, rows_of[:, part * 64:(part + 1) * 64], blocks)
        blocks = blocks.reshape(block_rows, -1)
        applied = jnp.einsum(
            "bim,bm->bi", coarse_values, blocks, precision=lax.Precision.HIGHEST
        ).reshape(-1)
        coarse_error = coarse_error + (coarse_rhs - applied) / coarse_diag

    small = jnp.sum(jnp.where(placed, coarse_error[None, :], 0.0), axis=1)
    every = everyone(small).reshape(groups, grid_x, grid_y, bx, by, bz)
    boxes = every.transpose(1, 3, 2, 4, 0, 5).reshape(grid_x * bx, grid_y * by, groups * bz)
    boxes = jnp.pad(boxes, 1)
    window = lax.dynamic_slice(
        boxes,
        (lax.axis_index("gx") * bx, lax.axis_index("gy") * by, lax.axis_index("grp") * bz),
        (bx + 2, by + 2, bz + 2),
    )
    window = window.reshape(bx + 2, (by + 2) * (bz + 2))
    spread_x = box_matrix(bx + 2, rows, 1, 0, live).T
    spread_yz = box_matrix((by + 2) * (bz + 2), span_y * span_z, span_z, 0, live, bz + 2)
    lifted = dot(spread_x, dot(window, spread_yz))
    solution = jnp.where(mask, solution + (lifted - WEIGHT * op(lifted) / diagonal), 0.0)
    for sweep_number in range(NU):
        solution = jnp.where(mask, solution + WEIGHT * (src - op(solution)) / diagonal, 0.0)
    return (trimmed(solution, span_y, span_z), coarse_error)


def solution(mesh):
    return jax.shard_map(
        local,
        mesh=mesh,
        in_specs=(
            P("gx", "gy", "grp"),
            P("gx", "gy", "grp"),
            P("gx", "gy", "grp"),
            P("gx", "gy", "grp"),
            P(("grp", "gx", "gy"), None, None),
            P(("grp", "gx", "gy"), None),
        ),
        out_specs=(P("gx", "gy", "grp"), P(("grp", "gx", "gy"))),
        check_vma=False,
    )
```

```python
import jax
import jax.numpy as jnp
from jax import lax
from jax.sharding import PartitionSpec as P

NU = 2
CITER = 4
BOX = 4
HALO = 4

WEIGHT = 2.0 / 3.0
ALL_AXES = ("grp", "gx", "gy")
PAIRS = ((0, 1), (0, -1), (1, 1), (1, -1), (2, 1), (2, -1))


def padded_size(shape):
    size = -(-shape[-1] // 128) * 128
    if len(shape) > 1:
        size *= -(-shape[-2] // 8) * 8
    for extent in shape[:-2]:
        size *= extent
    return size


def permute(slab, axis, pairs):
    count = slab.size
    if count % 128 == 0 and padded_size(slab.shape) > count + count // 4:
        return lax.ppermute(slab.reshape(-1, 128), axis, pairs).reshape(slab.shape)
    return lax.ppermute(slab, axis, pairs)


def exchange(cells, sides, width):
    for axis, dim in sides:
        count = lax.axis_size(axis)
        size = cells.shape[dim]
        head = lax.slice_in_dim(cells, 0, width, axis=dim)
        tail = lax.slice_in_dim(cells, size - width, size, axis=dim)
        if count == 1:
            before = jnp.zeros_like(tail)
            after = jnp.zeros_like(head)
        elif count == 2:
            index = lax.axis_index(axis)
            sent = jnp.where(index == 0, tail, head)
            got = permute(sent, axis, [(0, 1), (1, 0)])
            before = jnp.where(index == 1, got, 0.0)
            after = jnp.where(index == 0, got, 0.0)
        elif count % 2 == 0:
            index = lax.axis_index(axis)
            even = index % 2 == 0
            first = [(i + d, i + 1 - d) for i in range(0, count, 2) for d in (0, 1)]
            second = [(i + d, i + 1 - d) for i in range(1, count - 1, 2) for d in (0, 1)]
            got_first = permute(jnp.where(even, tail, head), axis, first)
            got_second = permute(jnp.where(even, head, tail), axis, second)
            before = jnp.where(even, got_second, got_first)
            after = jnp.where(even, got_first, got_second)
        else:
            before = permute(tail, axis, [(i, i + 1) for i in range(count - 1)])
            after = permute(head, axis, [(i + 1, i) for i in range(count - 1)])
        cells = jnp.concatenate([before, cells, after], axis=dim)
    return cells


def flat_shift(padded, rows, width, stride, dx, dy, dz):
    lead = stride + dy * stride + dz
    return padded[1 + dx:1 + dx + rows, lead:lead + width]


def neighbours(field, stride):
    rows, width = field.shape
    padded = jnp.pad(field, ((1, 1), (stride, stride)))
    steps = ((1, 0, 0), (-1, 0, 0), (0, 1, 0), (0, -1, 0), (0, 0, 1), (0, 0, -1))
    return [flat_shift(padded, rows, width, stride, *step) for step in steps]


def face_terms(conductance, stride):
    return [0.5 * (conductance + other) for other in neighbours(conductance, stride)]


def operate(field, storage, face_list, stride):
    summed = storage * field
    for face, other in zip(face_list, neighbours(field, stride)):
        summed = summed + face * (field - other)
    return summed


def inside_mask(rows, span_y, span_z):
    shape = (rows, span_y * span_z)
    column = lax.broadcasted_iota(jnp.int32, shape, 1)
    coords = (
        (lax.broadcasted_iota(jnp.int32, shape, 0), rows, "gx"),
        (column // span_z, span_y, "gy"),
        (column % span_z, span_z, "grp"),
    )
    mask = None
    for local_index, span, axis in coords:
        block = span - 2 * HALO
        where = lax.axis_index(axis) * block - HALO + local_index
        ok = (where >= 0) & (where < block * lax.axis_size(axis))
        mask = ok if mask is None else mask & ok
    return mask


def trimmed(flat, span_y, span_z):
    cube = flat.reshape(flat.shape[0], span_y, span_z)
    return cube[HALO:-HALO, HALO:-HALO, HALO:-HALO]


def grp_pool(vector):
    groups = lax.axis_size("grp")
    index = lax.axis_index("grp")
    parts = [vector]
    for step in range(1, groups):
        parts.append(lax.ppermute(vector, "grp", [(i, (i + step) % groups) for i in range(groups)]))
    stacked = jnp.stack(parts)
    order = (index - jnp.arange(groups)) % groups
    return jnp.take(stacked, order, axis=0)


def dot(left, right):
    return jnp.dot(left, right, precision=lax.Precision.HIGHEST)


def box_matrix(boxes, cells, stride, offset, live, inner=None):
    cell = lax.broadcasted_iota(jnp.int32, (1, cells), 1)
    if inner is None:
        local = cell - offset
        owner = jnp.where((local >= 0) & (local < boxes * BOX), local // BOX, -1)
    else:
        outer_cell, inner_cell = cell // stride - offset, cell % stride - offset
        inside = (outer_cell >= 0) & (outer_cell < (boxes // inner) * BOX)
        inside = inside & (inner_cell >= 0) & (inner_cell < inner * BOX)
        owner = jnp.where(inside, (outer_cell // BOX) * inner + inner_cell // BOX, -1)
    box = lax.broadcasted_iota(jnp.int32, (boxes, cells), 0)
    return ((box == owner) & live).astype(jnp.float32)


def everyone(vector):
    count = lax.axis_size(ALL_AXES)
    copies = jnp.broadcast_to(vector[None], (count,) + vector.shape)
    return lax.all_to_all(copies, ALL_AXES, 0, 0, tiled=True).reshape(-1)


def local(source, conductance, storage, aggregate_ids, coarse_values, coarse_columns):
    size_x, size_y, size_z = source.shape
    assert HALO == BOX and HALO >= 2 * NU and HALO >= NU + 2
    stacked = jnp.stack([source, conductance, storage])
    wide = exchange(stacked, (("grp", 3),), HALO)
    wide, box_labels = lax.optimization_barrier(
        (wide, aggregate_ids[::BOX, ::BOX, ::BOX].reshape(-1))
    )
    span_z = wide.shape[3]
    stride = span_z
    wide = wide.reshape(3, size_x, size_y * span_z)
    wide = exchange(wide, (("gy", 2),), HALO * span_z)
    wide = exchange(wide, (("gx", 1),), HALO)
    rows = wide.shape[1]
    span_y = wide.shape[2] // span_z
    src, cond, stor = wide[0], wide[1], wide[2]
    mask = inside_mask(rows, span_y, span_z)
    face_list = face_terms(cond, stride)
    diagonal = stor
    for position in range(6):
        diagonal = diagonal + face_list[position]

    def op(field):
        return operate(field, stor, face_list, stride)

    solution = jnp.where(mask, WEIGHT * src / diagonal, 0.0)
    for sweep_number in range(NU - 1):
        solution = jnp.where(mask, solution + WEIGHT * (src - op(solution)) / diagonal, 0.0)
    residual = src - op(solution)
    scaled = jnp.where(mask, residual / diagonal, 0.0)
    smoothed = residual - WEIGHT * op(scaled)

    bx, by, bz = size_x // BOX, size_y // BOX, size_z // BOX
    live = lax.axis_index("grp") >= 0
    pick_x = box_matrix(bx, rows, 1, HALO, live)
    pick_yz = box_matrix(by * bz, span_y * span_z, span_z, HALO, live, bz).T
    box_totals = dot(pick_x, dot(smoothed, pick_yz)).reshape(-1)
    placed = box_labels[:, None] == lax.broadcasted_iota(jnp.int32, (box_labels.shape[0],) * 2, 1)
    coarse_rhs = jnp.sum(jnp.where(placed, box_totals[:, None], 0.0), axis=0)
    eye = lax.broadcasted_iota(jnp.int32, (64, 64), 0) == lax.broadcasted_iota(jnp.int32, (64, 64), 1)
    coarse_diag = jnp.sum(jnp.where(eye[None], coarse_values[:, :, :64], 0.0), axis=2).reshape(-1)
    block_rows = coarse_values.shape[0]
    grid_x = lax.axis_size("gx")
    grid_y = lax.axis_size("gy")
    groups = lax.axis_size("grp")
    devices = groups * grid_x * grid_y
    column_list = coarse_columns.reshape(-1, 1)
    pick = (
        column_list // block_rows == lax.broadcasted_iota(jnp.int32, (column_list.shape[0], devices), 1)
    ).astype(source.dtype)
    within = column_list % block_rows
    coarse_error = coarse_rhs / coarse_diag
    for sweep_number in range(CITER - 1):
        pooled = everyone(coarse_error)
        rows_of = dot(pick, pooled.reshape(devices, -1))
        blocks = rows_of[:, :64]
        for part in range(1, block_rows):
            blocks = jnp.where(within == part, rows_of[:, part * 64:(part + 1) * 64], blocks)
        blocks = blocks.reshape(block_rows, -1)
        applied = jnp.einsum(
            "bim,bm->bi", coarse_values, blocks, precision=lax.Precision.HIGHEST
        ).reshape(-1)
        coarse_error = coarse_error + (coarse_rhs - applied) / coarse_diag

    small = jnp.sum(jnp.where(placed, coarse_error[None, :], 0.0), axis=1)
    every = everyone(small).reshape(groups, grid_x, grid_y, bx, by, bz)
    boxes = every.transpose(1, 3, 2, 4, 0, 5).reshape(grid_x * bx, grid_y * by, groups * bz)
    boxes = jnp.pad(boxes, 1)
    window = lax.dynamic_slice(
        boxes,
        (lax.axis_index("gx") * bx, lax.axis_index("gy") * by, lax.axis_index("grp") * bz),
        (bx + 2, by + 2, bz + 2),
    )
    window = window.reshape(bx + 2, (by + 2) * (bz + 2))
    spread_x = box_matrix(bx + 2, rows, 1, 0, live).T
    spread_yz = box_matrix((by + 2) * (bz + 2), span_y * span_z, span_z, 0, live, bz + 2)
    lifted = dot(spread_x, dot(window, spread_yz))
    solution = jnp.where(mask, solution + (lifted - WEIGHT * op(lifted) / diagonal), 0.0)
    for sweep_number in range(NU):
        solution = jnp.where(mask, solution + WEIGHT * (src - op(solution)) / diagonal, 0.0)
    return (trimmed(solution, span_y, span_z), coarse_error)


def solution(mesh):
    return jax.shard_map(
        local,
        mesh=mesh,
        in_specs=(
            P("gx", "gy", "grp"),
            P("gx", "gy", "grp"),
            P("gx", "gy", "grp"),
            P("gx", "gy", "grp"),
            P(("grp", "gx", "gy"), None, None),
            P(("grp", "gx", "gy"), None),
        ),
        out_specs=(P("gx", "gy", "grp"), P(("grp", "gx", "gy"))),
        check_vma=False,
    )
```

```python
import jax
import jax.numpy as jnp
from jax import lax
from jax.sharding import PartitionSpec as P

NU = 2
CITER = 4
BOX = 4
HALO = 4

WEIGHT = 2.0 / 3.0
ALL_AXES = ("grp", "gx", "gy")
PAIRS = ((0, 1), (0, -1), (1, 1), (1, -1), (2, 1), (2, -1))


def padded_size(shape):
    size = -(-shape[-1] // 128) * 128
    if len(shape) > 1:
        size *= -(-shape[-2] // 8) * 8
    for extent in shape[:-2]:
        size *= extent
    return size


def permute(slab, axis, pairs):
    count = slab.size
    if count % 128 == 0 and padded_size(slab.shape) > count + count // 4:
        return lax.ppermute(slab.reshape(-1, 128), axis, pairs).reshape(slab.shape)
    return lax.ppermute(slab, axis, pairs)


def exchange(cells, sides, width):
    for axis, dim in sides:
        count = lax.axis_size(axis)
        size = cells.shape[dim]
        head = lax.slice_in_dim(cells, 0, width, axis=dim)
        tail = lax.slice_in_dim(cells, size - width, size, axis=dim)
        if count == 1:
            before = jnp.zeros_like(tail)
            after = jnp.zeros_like(head)
        elif count == 2:
            index = lax.axis_index(axis)
            sent = jnp.where(index == 0, tail, head)
            got = permute(sent, axis, [(0, 1), (1, 0)])
            before = jnp.where(index == 1, got, 0.0)
            after = jnp.where(index == 0, got, 0.0)
        elif count % 2 == 0:
            index = lax.axis_index(axis)
            even = index % 2 == 0
            first = [(i + d, i + 1 - d) for i in range(0, count, 2) for d in (0, 1)]
            second = [(i + d, i + 1 - d) for i in range(1, count - 1, 2) for d in (0, 1)]
            got_first = permute(jnp.where(even, tail, head), axis, first)
            got_second = permute(jnp.where(even, head, tail), axis, second)
            before = jnp.where(even, got_second, got_first)
            after = jnp.where(even, got_first, got_second)
        else:
            before = permute(tail, axis, [(i, i + 1) for i in range(count - 1)])
            after = permute(head, axis, [(i + 1, i) for i in range(count - 1)])
        cells = jnp.concatenate([before, cells, after], axis=dim)
    return cells


def flat_shift(padded, rows, width, stride, dx, dy, dz):
    lead = stride + dy * stride + dz
    return padded[1 + dx:1 + dx + rows, lead:lead + width]


def neighbours(field, stride):
    rows, width = field.shape
    padded = jnp.pad(field, ((1, 1), (stride, stride)))
    steps = ((1, 0, 0), (-1, 0, 0), (0, 1, 0), (0, -1, 0), (0, 0, 1), (0, 0, -1))
    return [flat_shift(padded, rows, width, stride, *step) for step in steps]


def face_terms(conductance, stride):
    return [0.5 * (conductance + other) for other in neighbours(conductance, stride)]


def operate(field, storage, face_list, stride):
    summed = storage * field
    for face, other in zip(face_list, neighbours(field, stride)):
        summed = summed + face * (field - other)
    return summed


def inside_mask(rows, span_y, span_z):
    shape = (rows, span_y * span_z)
    column = lax.broadcasted_iota(jnp.int32, shape, 1)
    coords = (
        (lax.broadcasted_iota(jnp.int32, shape, 0), rows, "gx"),
        (column // span_z, span_y, "gy"),
        (column % span_z, span_z, "grp"),
    )
    mask = None
    for local_index, span, axis in coords:
        block = span - 2 * HALO
        where = lax.axis_index(axis) * block - HALO + local_index
        ok = (where >= 0) & (where < block * lax.axis_size(axis))
        mask = ok if mask is None else mask & ok
    return mask


def trimmed(flat, span_y, span_z):
    cube = flat.reshape(flat.shape[0], span_y, span_z)
    return cube[HALO:-HALO, HALO:-HALO, HALO:-HALO]


def grp_pool(vector):
    groups = lax.axis_size("grp")
    index = lax.axis_index("grp")
    parts = [vector]
    for step in range(1, groups):
        parts.append(lax.ppermute(vector, "grp", [(i, (i + step) % groups) for i in range(groups)]))
    stacked = jnp.stack(parts)
    order = (index - jnp.arange(groups)) % groups
    return jnp.take(stacked, order, axis=0)


def dot(left, right):
    return jnp.dot(left, right, precision=lax.Precision.HIGHEST)


def box_matrix(boxes, cells, stride, offset, live, inner=None):
    cell = lax.broadcasted_iota(jnp.int32, (1, cells), 1)
    if inner is None:
        local = cell - offset
        owner = jnp.where((local >= 0) & (local < boxes * BOX), local // BOX, -1)
    else:
        outer_cell, inner_cell = cell // stride - offset, cell % stride - offset
        inside = (outer_cell >= 0) & (outer_cell < (boxes // inner) * BOX)
        inside = inside & (inner_cell >= 0) & (inner_cell < inner * BOX)
        owner = jnp.where(inside, (outer_cell // BOX) * inner + inner_cell // BOX, -1)
    box = lax.broadcasted_iota(jnp.int32, (boxes, cells), 0)
    return ((box == owner) & live).astype(jnp.float32)


def everyone(vector):
    count = lax.axis_size(ALL_AXES)
    copies = jnp.broadcast_to(vector[None], (count,) + vector.shape)
    return lax.all_to_all(copies, ALL_AXES, 0, 0, tiled=True).reshape(-1)


def local(source, conductance, storage, aggregate_ids, coarse_values, coarse_columns):
    size_x, size_y, size_z = source.shape
    assert HALO == BOX and HALO >= 2 * NU and HALO >= NU + 2
    stacked = jnp.stack([source, conductance, storage])
    wide = exchange(stacked, (("grp", 3),), HALO)
    span_z = wide.shape[3]
    stride = span_z
    wide = wide.reshape(3, size_x, size_y * span_z)
    wide = exchange(wide, (("gy", 2),), HALO * span_z)
    wide = exchange(wide, (("gx", 1),), HALO)
    rows = wide.shape[1]
    span_y = wide.shape[2] // span_z
    src, cond, stor = wide[0], wide[1], wide[2]
    mask = inside_mask(rows, span_y, span_z)
    face_list = face_terms(cond, stride)
    diagonal = stor
    for position in range(6):
        diagonal = diagonal + face_list[position]

    def op(field):
        return operate(field, stor, face_list, stride)

    solution = jnp.where(mask, WEIGHT * src / diagonal, 0.0)
    for sweep_number in range(NU - 1):
        solution = jnp.where(mask, solution + WEIGHT * (src - op(solution)) / diagonal, 0.0)
    residual = src - op(solution)
    scaled = jnp.where(mask, residual / diagonal, 0.0)
    smoothed = residual - WEIGHT * op(scaled)

    bx, by, bz = size_x // BOX, size_y // BOX, size_z // BOX
    live = lax.axis_index("grp") >= 0
    pick_x = box_matrix(bx, rows, 1, HALO, live)
    pick_yz = box_matrix(by * bz, span_y * span_z, span_z, HALO, live, bz).T
    box_totals = dot(pick_x, dot(smoothed, pick_yz)).reshape(-1)
    box_labels = aggregate_ids[::BOX, ::BOX, ::BOX].reshape(-1)
    placed = box_labels[:, None] == lax.broadcasted_iota(jnp.int32, (box_labels.shape[0],) * 2, 1)
    coarse_rhs = jnp.sum(jnp.where(placed, box_totals[:, None], 0.0), axis=0)
    eye = lax.broadcasted_iota(jnp.int32, (64, 64), 0) == lax.broadcasted_iota(jnp.int32, (64, 64), 1)
    coarse_diag = jnp.sum(jnp.where(eye[None], coarse_values[:, :, :64], 0.0), axis=2).reshape(-1)
    block_rows = coarse_values.shape[0]
    grid_x = lax.axis_size("gx")
    grid_y = lax.axis_size("gy")
    groups = lax.axis_size("grp")
    devices = groups * grid_x * grid_y
    column_list = coarse_columns.reshape(-1, 1)
    pick = (
        column_list // block_rows == lax.broadcasted_iota(jnp.int32, (column_list.shape[0], devices), 1)
    ).astype(source.dtype)
    within = column_list % block_rows
    coarse_error = coarse_rhs / coarse_diag
    me = lax.axis_index(ALL_AXES)
    for sweep_number in range(CITER - 1):
        pooled = everyone(coarse_error).reshape(devices, -1)
        coarse_error = lax.dynamic_index_in_dim(pooled, me, axis=0, keepdims=False)
        rows_of = dot(pick, pooled)
        blocks = rows_of[:, :64]
        for part in range(1, block_rows):
            blocks = jnp.where(within == part, rows_of[:, part * 64:(part + 1) * 64], blocks)
        blocks = blocks.reshape(block_rows, -1)
        applied = jnp.einsum(
            "bim,bm->bi", coarse_values, blocks, precision=lax.Precision.HIGHEST
        ).reshape(-1)
        coarse_error = coarse_error + (coarse_rhs - applied) / coarse_diag

    small = jnp.sum(jnp.where(placed, coarse_error[None, :], 0.0), axis=1)
    every = everyone(small).reshape(groups, grid_x, grid_y, bx, by, bz)
    boxes = every.transpose(1, 3, 2, 4, 0, 5).reshape(grid_x * bx, grid_y * by, groups * bz)
    boxes = jnp.pad(boxes, 1)
    window = lax.dynamic_slice(
        boxes,
        (lax.axis_index("gx") * bx, lax.axis_index("gy") * by, lax.axis_index("grp") * bz),
        (bx + 2, by + 2, bz + 2),
    )
    window = window.reshape(bx + 2, (by + 2) * (bz + 2))
    spread_x = box_matrix(bx + 2, rows, 1, 0, live).T
    spread_yz = box_matrix((by + 2) * (bz + 2), span_y * span_z, span_z, 0, live, bz + 2)
    lifted = dot(spread_x, dot(window, spread_yz))
    solution = jnp.where(mask, solution + (lifted - WEIGHT * op(lifted) / diagonal), 0.0)
    for sweep_number in range(NU):
        solution = jnp.where(mask, solution + WEIGHT * (src - op(solution)) / diagonal, 0.0)
    return (trimmed(solution, span_y, span_z), coarse_error)


def solution(mesh):
    return jax.shard_map(
        local,
        mesh=mesh,
        in_specs=(
            P("gx", "gy", "grp"),
            P("gx", "gy", "grp"),
            P("gx", "gy", "grp"),
            P("gx", "gy", "grp"),
            P(("grp", "gx", "gy"), None, None),
            P(("grp", "gx", "gy"), None),
        ),
        out_specs=(P("gx", "gy", "grp"), P(("grp", "gx", "gy"))),
        check_vma=False,
    )
```

```python
import jax
import jax.numpy as jnp
from jax import lax
from jax.sharding import PartitionSpec as P

NU = 2
CITER = 4
BOX = 4
HALO = 4

WEIGHT = 2.0 / 3.0
ALL_AXES = ("grp", "gx", "gy")
PAIRS = ((0, 1), (0, -1), (1, 1), (1, -1), (2, 1), (2, -1))


def padded_size(shape):
    size = -(-shape[-1] // 128) * 128
    if len(shape) > 1:
        size *= -(-shape[-2] // 8) * 8
    for extent in shape[:-2]:
        size *= extent
    return size


def permute(slab, axis, pairs):
    count = slab.size
    if count % 128 == 0 and padded_size(slab.shape) > count + count // 4:
        return lax.ppermute(slab.reshape(-1, 128), axis, pairs).reshape(slab.shape)
    return lax.ppermute(slab, axis, pairs)


def exchange(cells, sides, width):
    for axis, dim in sides:
        count = lax.axis_size(axis)
        size = cells.shape[dim]
        head = lax.slice_in_dim(cells, 0, width, axis=dim)
        tail = lax.slice_in_dim(cells, size - width, size, axis=dim)
        if count == 1:
            before = jnp.zeros_like(tail)
            after = jnp.zeros_like(head)
        elif count == 2:
            index = lax.axis_index(axis)
            sent = jnp.where(index == 0, tail, head)
            got = permute(sent, axis, [(0, 1), (1, 0)])
            before = jnp.where(index == 1, got, 0.0)
            after = jnp.where(index == 0, got, 0.0)
        elif count % 2 == 0:
            index = lax.axis_index(axis)
            even = index % 2 == 0
            first = [(i + d, i + 1 - d) for i in range(0, count, 2) for d in (0, 1)]
            second = [(i + d, i + 1 - d) for i in range(1, count - 1, 2) for d in (0, 1)]
            got_first = permute(jnp.where(even, tail, head), axis, first)
            got_second = permute(jnp.where(even, head, tail), axis, second)
            before = jnp.where(even, got_second, got_first)
            after = jnp.where(even, got_first, got_second)
        else:
            before = permute(tail, axis, [(i, i + 1) for i in range(count - 1)])
            after = permute(head, axis, [(i + 1, i) for i in range(count - 1)])
        cells = jnp.concatenate([before, cells, after], axis=dim)
    return cells


def flat_shift(padded, rows, width, stride, dx, dy, dz):
    lead = stride + dy * stride + dz
    return padded[1 + dx:1 + dx + rows, lead:lead + width]


def neighbours(field, stride):
    rows, width = field.shape
    padded = jnp.pad(field, ((1, 1), (stride, stride)))
    steps = ((1, 0, 0), (-1, 0, 0), (0, 1, 0), (0, -1, 0), (0, 0, 1), (0, 0, -1))
    return [flat_shift(padded, rows, width, stride, *step) for step in steps]


def face_terms(conductance, stride):
    return [0.5 * (conductance + other) for other in neighbours(conductance, stride)]


def operate(field, storage, face_list, stride):
    summed = storage * field
    for face, other in zip(face_list, neighbours(field, stride)):
        summed = summed + face * (field - other)
    return summed


def inside_mask(rows, span_y, span_z):
    column = lax.broadcasted_iota(jnp.int32, (1, span_y * span_z), 1)
    coords = (
        (lax.broadcasted_iota(jnp.int32, (rows, 1), 0), rows, "gx"),
        (column // span_z, span_y, "gy"),
        (column % span_z, span_z, "grp"),
    )
    mask = None
    for local_index, span, axis in coords:
        block = span - 2 * HALO
        where = lax.axis_index(axis) * block - HALO + local_index
        ok = (where >= 0) & (where < block * lax.axis_size(axis))
        mask = ok if mask is None else mask & ok
    return jnp.broadcast_to(mask, (rows, span_y * span_z))


def trimmed(flat, span_y, span_z):
    cube = flat.reshape(flat.shape[0], span_y, span_z)
    return cube[HALO:-HALO, HALO:-HALO, HALO:-HALO]


def grp_pool(vector):
    groups = lax.axis_size("grp")
    index = lax.axis_index("grp")
    parts = [vector]
    for step in range(1, groups):
        parts.append(lax.ppermute(vector, "grp", [(i, (i + step) % groups) for i in range(groups)]))
    stacked = jnp.stack(parts)
    order = (index - jnp.arange(groups)) % groups
    return jnp.take(stacked, order, axis=0)


def dot(left, right):
    return jnp.dot(left, right, precision=lax.Precision.HIGHEST)


def box_matrix(boxes, cells, stride, offset, live, inner=None):
    cell = lax.broadcasted_iota(jnp.int32, (1, cells), 1)
    if inner is None:
        local = cell - offset
        owner = jnp.where((local >= 0) & (local < boxes * BOX), local // BOX, -1)
    else:
        outer_cell, inner_cell = cell // stride - offset, cell % stride - offset
        inside = (outer_cell >= 0) & (outer_cell < (boxes // inner) * BOX)
        inside = inside & (inner_cell >= 0) & (inner_cell < inner * BOX)
        owner = jnp.where(inside, (outer_cell // BOX) * inner + inner_cell // BOX, -1)
    box = lax.broadcasted_iota(jnp.int32, (boxes, cells), 0)
    return ((box == owner) & live).astype(jnp.float32)


def everyone(vector):
    count = lax.axis_size(ALL_AXES)
    copies = jnp.broadcast_to(vector[None], (count,) + vector.shape)
    return lax.all_to_all(copies, ALL_AXES, 0, 0, tiled=True).reshape(-1)


def local(source, conductance, storage, aggregate_ids, coarse_values, coarse_columns):
    size_x, size_y, size_z = source.shape
    assert HALO == BOX and HALO >= 2 * NU and HALO >= NU + 2
    stacked = jnp.stack([source, conductance, storage])
    wide = exchange(stacked, (("grp", 3),), HALO)
    span_z = wide.shape[3]
    stride = span_z
    wide = wide.reshape(3, size_x, size_y * span_z)
    wide = exchange(wide, (("gy", 2),), HALO * span_z)
    wide = exchange(wide, (("gx", 1),), HALO)
    rows = wide.shape[1]
    span_y = wide.shape[2] // span_z
    src, cond, stor = wide[0], wide[1], wide[2]
    mask = inside_mask(rows, span_y, span_z)
    face_list = face_terms(cond, stride)
    diagonal = stor
    for position in range(6):
        diagonal = diagonal + face_list[position]

    def op(field):
        return operate(field, stor, face_list, stride)

    solution = jnp.where(mask, WEIGHT * src / diagonal, 0.0)
    for sweep_number in range(NU - 1):
        solution = jnp.where(mask, solution + WEIGHT * (src - op(solution)) / diagonal, 0.0)
    residual = src - op(solution)
    scaled = jnp.where(mask, residual / diagonal, 0.0)
    smoothed = residual - WEIGHT * op(scaled)

    bx, by, bz = size_x // BOX, size_y // BOX, size_z // BOX
    live = lax.axis_index("grp") >= 0
    pick_x = box_matrix(bx, rows, 1, HALO, live)
    pick_yz = box_matrix(by * bz, span_y * span_z, span_z, HALO, live, bz).T
    box_totals = dot(pick_x, dot(smoothed, pick_yz)).reshape(-1)
    box_labels = aggregate_ids[::BOX, ::BOX, ::BOX].reshape(-1)
    placed = box_labels[:, None] == lax.broadcasted_iota(jnp.int32, (box_labels.shape[0],) * 2, 1)
    coarse_rhs = jnp.sum(jnp.where(placed, box_totals[:, None], 0.0), axis=0)
    eye = lax.broadcasted_iota(jnp.int32, (64, 64), 0) == lax.broadcasted_iota(jnp.int32, (64, 64), 1)
    coarse_diag = jnp.sum(jnp.where(eye[None], coarse_values[:, :, :64], 0.0), axis=2).reshape(-1)
    block_rows = coarse_values.shape[0]
    grid_x = lax.axis_size("gx")
    grid_y = lax.axis_size("gy")
    groups = lax.axis_size("grp")
    devices = groups * grid_x * grid_y
    column_list = coarse_columns.reshape(-1, 1)
    pick = (
        column_list // block_rows == lax.broadcasted_iota(jnp.int32, (column_list.shape[0], devices), 1)
    ).astype(source.dtype)
    within = column_list % block_rows
    coarse_error = coarse_rhs / coarse_diag
    for sweep_number in range(CITER - 1):
        pooled = everyone(coarse_error)
        rows_of = dot(pick, pooled.reshape(devices, -1))
        blocks = rows_of[:, :64]
        for part in range(1, block_rows):
            blocks = jnp.where(within == part, rows_of[:, part * 64:(part + 1) * 64], blocks)
        blocks = blocks.reshape(block_rows, -1)
        applied = jnp.einsum(
            "bim,bm->bi", coarse_values, blocks, precision=lax.Precision.HIGHEST
        ).reshape(-1)
        coarse_error = coarse_error + (coarse_rhs - applied) / coarse_diag

    small = jnp.sum(jnp.where(placed, coarse_error[None, :], 0.0), axis=1)
    every = everyone(small).reshape(groups, grid_x, grid_y, bx, by, bz)
    boxes = every.transpose(1, 3, 2, 4, 0, 5).reshape(grid_x * bx, grid_y * by, groups * bz)
    boxes = jnp.pad(boxes, 1)
    window = lax.dynamic_slice(
        boxes,
        (lax.axis_index("gx") * bx, lax.axis_index("gy") * by, lax.axis_index("grp") * bz),
        (bx + 2, by + 2, bz + 2),
    )
    window = window.reshape(bx + 2, (by + 2) * (bz + 2))
    spread_x = box_matrix(bx + 2, rows, 1, 0, live).T
    spread_yz = box_matrix((by + 2) * (bz + 2), span_y * span_z, span_z, 0, live, bz + 2)
    lifted = dot(spread_x, dot(window, spread_yz))
    solution = jnp.where(mask, solution + (lifted - WEIGHT * op(lifted) / diagonal), 0.0)
    for sweep_number in range(NU):
        solution = jnp.where(mask, solution + WEIGHT * (src - op(solution)) / diagonal, 0.0)
    return (trimmed(solution, span_y, span_z), coarse_error)


def solution(mesh):
    return jax.shard_map(
        local,
        mesh=mesh,
        in_specs=(
            P("gx", "gy", "grp"),
            P("gx", "gy", "grp"),
            P("gx", "gy", "grp"),
            P("gx", "gy", "grp"),
            P(("grp", "gx", "gy"), None, None),
            P(("grp", "gx", "gy"), None),
        ),
        out_specs=(P("gx", "gy", "grp"), P(("grp", "gx", "gy"))),
        check_vma=False,
    )
```

```python
import jax
import jax.numpy as jnp
from jax import lax
from jax.sharding import PartitionSpec as P

NU = 2
CITER = 4
BOX = 4
HALO = 4

WEIGHT = 2.0 / 3.0
ALL_AXES = ("grp", "gx", "gy")
PAIRS = ((0, 1), (0, -1), (1, 1), (1, -1), (2, 1), (2, -1))


def padded_size(shape):
    size = -(-shape[-1] // 128) * 128
    if len(shape) > 1:
        size *= -(-shape[-2] // 8) * 8
    for extent in shape[:-2]:
        size *= extent
    return size


def permute(slab, axis, pairs):
    count = slab.size
    if count % 128 == 0 and padded_size(slab.shape) > count + count // 4:
        return lax.ppermute(slab.reshape(-1, 128), axis, pairs).reshape(slab.shape)
    return lax.ppermute(slab, axis, pairs)


def exchange(cells, sides, width):
    for axis, dim in sides:
        count = lax.axis_size(axis)
        size = cells.shape[dim]
        head = lax.slice_in_dim(cells, 0, width, axis=dim)
        tail = lax.slice_in_dim(cells, size - width, size, axis=dim)
        if count == 1:
            before = jnp.zeros_like(tail)
            after = jnp.zeros_like(head)
        elif count == 2:
            index = lax.axis_index(axis)
            sent = jnp.where(index == 0, tail, head)
            got = permute(sent, axis, [(0, 1), (1, 0)])
            before = jnp.where(index == 1, got, 0.0)
            after = jnp.where(index == 0, got, 0.0)
        elif count % 2 == 0:
            index = lax.axis_index(axis)
            even = index % 2 == 0
            first = [(i + d, i + 1 - d) for i in range(0, count, 2) for d in (0, 1)]
            second = [(i + d, i + 1 - d) for i in range(1, count - 1, 2) for d in (0, 1)]
            got_first = permute(jnp.where(even, tail, head), axis, first)
            got_second = permute(jnp.where(even, head, tail), axis, second)
            before = jnp.where(even, got_second, got_first)
            after = jnp.where(even, got_first, got_second)
        else:
            before = permute(tail, axis, [(i, i + 1) for i in range(count - 1)])
            after = permute(head, axis, [(i + 1, i) for i in range(count - 1)])
        cells = jnp.concatenate([before, cells, after], axis=dim)
    return cells


def flat_shift(padded, rows, width, stride, dx, dy, dz):
    lead = stride + dy * stride + dz
    return padded[1 + dx:1 + dx + rows, lead:lead + width]


def neighbours(field, stride):
    rows, width = field.shape
    padded = jnp.pad(field, ((1, 1), (stride, stride)))
    steps = ((1, 0, 0), (-1, 0, 0), (0, 1, 0), (0, -1, 0), (0, 0, 1), (0, 0, -1))
    return [flat_shift(padded, rows, width, stride, *step) for step in steps]


def face_terms(conductance, stride):
    return [0.5 * (conductance + other) for other in neighbours(conductance, stride)]


def operate(field, storage, face_list, stride):
    summed = storage * field
    for face, other in zip(face_list, neighbours(field, stride)):
        summed = summed + face * (field - other)
    return summed


def inside_mask(rows, span_y, span_z):
    column = lax.broadcasted_iota(jnp.int32, (1, span_y * span_z), 1)
    coords = (
        (lax.broadcasted_iota(jnp.int32, (rows, 1), 0), rows, "gx"),
        (column // span_z, span_y, "gy"),
        (column % span_z, span_z, "grp"),
    )
    mask = None
    for local_index, span, axis in coords:
        block = span - 2 * HALO
        where = lax.axis_index(axis) * block - HALO + local_index
        ok = (where >= 0) & (where < block * lax.axis_size(axis))
        mask = ok if mask is None else mask & ok
    return jnp.broadcast_to(mask, (rows, span_y * span_z))


def trimmed(flat, span_y, span_z):
    cube = flat.reshape(flat.shape[0], span_y, span_z)
    return cube[HALO:-HALO, HALO:-HALO, HALO:-HALO]


def grp_pool(vector):
    groups = lax.axis_size("grp")
    index = lax.axis_index("grp")
    parts = [vector]
    for step in range(1, groups):
        parts.append(lax.ppermute(vector, "grp", [(i, (i + step) % groups) for i in range(groups)]))
    stacked = jnp.stack(parts)
    order = (index - jnp.arange(groups)) % groups
    return jnp.take(stacked, order, axis=0)


def dot(left, right):
    return jnp.dot(left, right, precision=lax.Precision.HIGHEST)


def box_matrix(boxes, cells, stride, offset, live, inner=None):
    cell = lax.broadcasted_iota(jnp.int32, (1, cells), 1)
    if inner is None:
        local = cell - offset
        owner = jnp.where((local >= 0) & (local < boxes * BOX), local // BOX, -1)
    else:
        outer_cell, inner_cell = cell // stride - offset, cell % stride - offset
        inside = (outer_cell >= 0) & (outer_cell < (boxes // inner) * BOX)
        inside = inside & (inner_cell >= 0) & (inner_cell < inner * BOX)
        owner = jnp.where(inside, (outer_cell // BOX) * inner + inner_cell // BOX, -1)
    box = lax.broadcasted_iota(jnp.int32, (boxes, cells), 0)
    return ((box == owner) & live).astype(jnp.float32)


def everyone(vector):
    count = lax.axis_size(ALL_AXES)
    copies = jnp.broadcast_to(vector[None], (count,) + vector.shape)
    return lax.all_to_all(copies, ALL_AXES, 0, 0, tiled=True).reshape(-1)


def local(source, conductance, storage, aggregate_ids, coarse_values, coarse_columns):
    size_x, size_y, size_z = source.shape
    assert HALO == BOX and HALO >= 2 * NU and HALO >= NU + 2
    stacked = jnp.stack([source, conductance, storage])
    wide = exchange(stacked, (("grp", 3),), HALO)
    span_z = wide.shape[3]
    stride = span_z
    wide = wide.reshape(3, size_x, size_y * span_z)
    wide = exchange(wide, (("gy", 2),), HALO * span_z)
    wide = exchange(wide, (("gx", 1),), HALO)
    rows = wide.shape[1]
    span_y = wide.shape[2] // span_z
    src, cond, stor = wide[0], wide[1], wide[2]
    mask = inside_mask(rows, span_y, span_z)
    face_list = face_terms(cond, stride)
    diagonal = stor
    for position in range(6):
        diagonal = diagonal + face_list[position]

    def op(field):
        return operate(field, stor, face_list, stride)

    solution = jnp.where(mask, WEIGHT * src / diagonal, 0.0)
    for sweep_number in range(NU - 1):
        solution = jnp.where(mask, solution + WEIGHT * (src - op(solution)) / diagonal, 0.0)
    residual = src - op(solution)
    scaled = jnp.where(mask, residual / diagonal, 0.0)
    smoothed = residual - WEIGHT * op(scaled)

    bx, by, bz = size_x // BOX, size_y // BOX, size_z // BOX
    live = lax.axis_index("grp") >= 0
    pick_x = box_matrix(bx, rows, 1, HALO, live)
    pick_yz = box_matrix(by * bz, span_y * span_z, span_z, HALO, live, bz).T
    box_totals = dot(pick_x, dot(smoothed, pick_yz)).reshape(-1)
    box_labels = aggregate_ids[::BOX, ::BOX].reshape(bx, by, bz, BOX)[:, :, :, 0].reshape(-1)
    placed = box_labels[:, None] == lax.broadcasted_iota(jnp.int32, (box_labels.shape[0],) * 2, 1)
    coarse_rhs = jnp.sum(jnp.where(placed, box_totals[:, None], 0.0), axis=0)
    eye = lax.broadcasted_iota(jnp.int32, (64, 64), 0) == lax.broadcasted_iota(jnp.int32, (64, 64), 1)
    coarse_diag = jnp.sum(jnp.where(eye[None], coarse_values[:, :, :64], 0.0), axis=2).reshape(-1)
    block_rows = coarse_values.shape[0]
    grid_x = lax.axis_size("gx")
    grid_y = lax.axis_size("gy")
    groups = lax.axis_size("grp")
    devices = groups * grid_x * grid_y
    column_list = coarse_columns.reshape(-1, 1)
    pick = (
        column_list // block_rows == lax.broadcasted_iota(jnp.int32, (column_list.shape[0], devices), 1)
    ).astype(source.dtype)
    within = column_list % block_rows
    coarse_error = coarse_rhs / coarse_diag
    for sweep_number in range(CITER - 1):
        pooled = everyone(coarse_error)
        rows_of = dot(pick, pooled.reshape(devices, -1))
        blocks = rows_of[:, :64]
        for part in range(1, block_rows):
            blocks = jnp.where(within == part, rows_of[:, part * 64:(part + 1) * 64], blocks)
        blocks = blocks.reshape(block_rows, -1)
        applied = jnp.einsum(
            "bim,bm->bi", coarse_values, blocks, precision=lax.Precision.HIGHEST
        ).reshape(-1)
        coarse_error = coarse_error + (coarse_rhs - applied) / coarse_diag

    small = jnp.sum(jnp.where(placed, coarse_error[None, :], 0.0), axis=1)
    every = everyone(small).reshape(groups, grid_x, grid_y, bx, by, bz)
    boxes = every.transpose(1, 3, 2, 4, 0, 5).reshape(grid_x * bx, grid_y * by, groups * bz)
    boxes = jnp.pad(boxes, 1)
    window = lax.dynamic_slice(
        boxes,
        (lax.axis_index("gx") * bx, lax.axis_index("gy") * by, lax.axis_index("grp") * bz),
        (bx + 2, by + 2, bz + 2),
    )
    window = window.reshape(bx + 2, (by + 2) * (bz + 2))
    spread_x = box_matrix(bx + 2, rows, 1, 0, live).T
    spread_yz = box_matrix((by + 2) * (bz + 2), span_y * span_z, span_z, 0, live, bz + 2)
    lifted = dot(spread_x, dot(window, spread_yz))
    solution = jnp.where(mask, solution + (lifted - WEIGHT * op(lifted) / diagonal), 0.0)
    for sweep_number in range(NU):
        solution = jnp.where(mask, solution + WEIGHT * (src - op(solution)) / diagonal, 0.0)
    return (trimmed(solution, span_y, span_z), coarse_error)


def solution(mesh):
    return jax.shard_map(
        local,
        mesh=mesh,
        in_specs=(
            P("gx", "gy", "grp"),
            P("gx", "gy", "grp"),
            P("gx", "gy", "grp"),
            P("gx", "gy", "grp"),
            P(("grp", "gx", "gy"), None, None),
            P(("grp", "gx", "gy"), None),
        ),
        out_specs=(P("gx", "gy", "grp"), P(("grp", "gx", "gy"))),
        check_vma=False,
    )
```

```python
import jax
import jax.numpy as jnp
from jax import lax
from jax.sharding import PartitionSpec as P

NU = 2
CITER = 4
BOX = 4
HALO = 4

WEIGHT = 2.0 / 3.0
ALL_AXES = ("grp", "gx", "gy")
PAIRS = ((0, 1), (0, -1), (1, 1), (1, -1), (2, 1), (2, -1))


def padded_size(shape):
    size = -(-shape[-1] // 128) * 128
    if len(shape) > 1:
        size *= -(-shape[-2] // 8) * 8
    for extent in shape[:-2]:
        size *= extent
    return size


def permute(slab, axis, pairs):
    count = slab.size
    if count % 128 == 0 and padded_size(slab.shape) > count + count // 4:
        return lax.ppermute(slab.reshape(-1, 128), axis, pairs).reshape(slab.shape)
    return lax.ppermute(slab, axis, pairs)


def exchange(cells, sides, width):
    for axis, dim in sides:
        count = lax.axis_size(axis)
        size = cells.shape[dim]
        head = lax.slice_in_dim(cells, 0, width, axis=dim)
        tail = lax.slice_in_dim(cells, size - width, size, axis=dim)
        if count == 1:
            before = jnp.zeros_like(tail)
            after = jnp.zeros_like(head)
        elif count == 2:
            index = lax.axis_index(axis)
            sent = jnp.where(index == 0, tail, head)
            got = permute(sent, axis, [(0, 1), (1, 0)])
            before = jnp.where(index == 1, got, 0.0)
            after = jnp.where(index == 0, got, 0.0)
        elif count % 2 == 0:
            index = lax.axis_index(axis)
            even = index % 2 == 0
            first = [(i + d, i + 1 - d) for i in range(0, count, 2) for d in (0, 1)]
            second = [(i + d, i + 1 - d) for i in range(1, count - 1, 2) for d in (0, 1)]
            got_first = permute(jnp.where(even, tail, head), axis, first)
            got_second = permute(jnp.where(even, head, tail), axis, second)
            before = jnp.where(even, got_second, got_first)
            after = jnp.where(even, got_first, got_second)
        else:
            before = permute(tail, axis, [(i, i + 1) for i in range(count - 1)])
            after = permute(head, axis, [(i + 1, i) for i in range(count - 1)])
        cells = jnp.concatenate([before, cells, after], axis=dim)
    return cells


def flat_shift(padded, rows, width, stride, dx, dy, dz):
    lead = stride + dy * stride + dz
    return padded[1 + dx:1 + dx + rows, lead:lead + width]


def neighbours(field, stride):
    rows, width = field.shape
    padded = jnp.pad(field, ((1, 1), (stride, stride)))
    steps = ((1, 0, 0), (-1, 0, 0), (0, 1, 0), (0, -1, 0), (0, 0, 1), (0, 0, -1))
    return [flat_shift(padded, rows, width, stride, *step) for step in steps]


def face_terms(conductance, stride):
    return [0.5 * (conductance + other) for other in neighbours(conductance, stride)]


def operate(field, storage, face_list, stride):
    summed = storage * field
    for face, other in zip(face_list, neighbours(field, stride)):
        summed = summed + face * (field - other)
    return summed


def inside_mask(rows, span_y, span_z):
    column = lax.broadcasted_iota(jnp.int32, (1, span_y * span_z), 1)
    coords = (
        (lax.broadcasted_iota(jnp.int32, (rows, 1), 0), rows, "gx"),
        (column // span_z, span_y, "gy"),
        (column % span_z, span_z, "grp"),
    )
    mask = None
    for local_index, span, axis in coords:
        block = span - 2 * HALO
        where = lax.axis_index(axis) * block - HALO + local_index
        ok = (where >= 0) & (where < block * lax.axis_size(axis))
        mask = ok if mask is None else mask & ok
    return jnp.broadcast_to(mask, (rows, span_y * span_z))


def trimmed(flat, span_y, span_z):
    cube = flat.reshape(flat.shape[0], span_y, span_z)
    return cube[HALO:-HALO, HALO:-HALO, HALO:-HALO]


def grp_pool(vector):
    groups = lax.axis_size("grp")
    index = lax.axis_index("grp")
    parts = [vector]
    for step in range(1, groups):
        parts.append(lax.ppermute(vector, "grp", [(i, (i + step) % groups) for i in range(groups)]))
    stacked = jnp.stack(parts)
    order = (index - jnp.arange(groups)) % groups
    return jnp.take(stacked, order, axis=0)


def dot(left, right):
    return jnp.dot(left, right, precision=lax.Precision.HIGHEST)


def box_matrix(boxes, cells, stride, offset, live, inner=None):
    cell = lax.broadcasted_iota(jnp.int32, (1, cells), 1)
    if inner is None:
        local = cell - offset
        owner = jnp.where((local >= 0) & (local < boxes * BOX), local // BOX, -1)
    else:
        outer_cell, inner_cell = cell // stride - offset, cell % stride - offset
        inside = (outer_cell >= 0) & (outer_cell < (boxes // inner) * BOX)
        inside = inside & (inner_cell >= 0) & (inner_cell < inner * BOX)
        owner = jnp.where(inside, (outer_cell // BOX) * inner + inner_cell // BOX, -1)
    box = lax.broadcasted_iota(jnp.int32, (boxes, cells), 0)
    return ((box == owner) & live).astype(jnp.float32)


def everyone(vector):
    count = lax.axis_size(ALL_AXES)
    copies = jnp.broadcast_to(vector[None], (count,) + vector.shape)
    return lax.all_to_all(copies, ALL_AXES, 0, 0, tiled=True).reshape(-1)


def local(source, conductance, storage, aggregate_ids, coarse_values, coarse_columns):
    size_x, size_y, size_z = source.shape
    assert HALO == BOX and HALO >= 2 * NU and HALO >= NU + 2
    stacked = jnp.stack([source, conductance, storage])
    wide = exchange(stacked, (("grp", 3),), HALO)
    span_z = wide.shape[3]
    stride = span_z
    wide = wide.reshape(3, size_x, size_y * span_z)
    wide = exchange(wide, (("gy", 2),), HALO * span_z)
    wide = exchange(wide, (("gx", 1),), HALO)
    rows = wide.shape[1]
    span_y = wide.shape[2] // span_z
    src, cond, stor = wide[0], wide[1], wide[2]
    mask = inside_mask(rows, span_y, span_z)
    face_list = face_terms(cond, stride)
    diagonal = stor
    for position in range(6):
        diagonal = diagonal + face_list[position]

    def op(field):
        return operate(field, stor, face_list, stride)

    solution = jnp.where(mask, WEIGHT * src / diagonal, 0.0)
    for sweep_number in range(NU - 1):
        solution = jnp.where(mask, solution + WEIGHT * (src - op(solution)) / diagonal, 0.0)
    residual = src - op(solution)
    scaled = jnp.where(mask, residual / diagonal, 0.0)
    smoothed = residual - WEIGHT * op(scaled)

    bx, by, bz = size_x // BOX, size_y // BOX, size_z // BOX
    live = lax.axis_index("grp") >= 0
    pick_x = box_matrix(bx, rows, 1, HALO, live)
    pick_yz = box_matrix(by * bz, span_y * span_z, span_z, HALO, live, bz).T
    box_totals = dot(pick_x, dot(smoothed, pick_yz)).reshape(-1)
    box_labels = aggregate_ids[::BOX, ::BOX, ::BOX].reshape(-1)
    placed = box_labels[:, None] == lax.broadcasted_iota(jnp.int32, (box_labels.shape[0],) * 2, 1)
    coarse_rhs = jnp.sum(jnp.where(placed, box_totals[:, None], 0.0), axis=0)
    eye = lax.broadcasted_iota(jnp.int32, (64, 64), 0) == lax.broadcasted_iota(jnp.int32, (64, 64), 1)
    coarse_diag = jnp.sum(jnp.where(eye[None], coarse_values[:, :, :64], 0.0), axis=2).reshape(-1)
    block_rows = coarse_values.shape[0]
    grid_x = lax.axis_size("gx")
    grid_y = lax.axis_size("gy")
    groups = lax.axis_size("grp")
    devices = groups * grid_x * grid_y
    column_list = coarse_columns.reshape(-1, 1)
    pick = (
        column_list // block_rows == lax.broadcasted_iota(jnp.int32, (column_list.shape[0], devices), 1)
    ).astype(source.dtype)
    within = column_list % block_rows
    coarse_error = coarse_rhs / coarse_diag
    for sweep_number in range(CITER - 1):
        pooled = everyone(coarse_error)
        rows_of = dot(pick, pooled.reshape(devices, -1))
        blocks = rows_of[:, :64]
        for part in range(1, block_rows):
            blocks = jnp.where(within == part, rows_of[:, part * 64:(part + 1) * 64], blocks)
        blocks = blocks.reshape(block_rows, -1)
        applied = jnp.einsum(
            "bim,bm->bi", coarse_values, blocks, precision=lax.Precision.HIGHEST
        ).reshape(-1)
        coarse_error = coarse_error + (coarse_rhs - applied) / coarse_diag

    small = jnp.sum(jnp.where(placed, coarse_error[None, :], 0.0), axis=1)
    every = everyone(small).reshape(groups, grid_x, grid_y, bx, by, bz)
    boxes = every.transpose(1, 3, 2, 4, 0, 5).reshape(grid_x * bx, grid_y * by, groups * bz)
    boxes = jnp.pad(boxes, 1)
    window = lax.dynamic_slice(
        boxes,
        (lax.axis_index("gx") * bx, lax.axis_index("gy") * by, lax.axis_index("grp") * bz),
        (bx + 2, by + 2, bz + 2),
    )
    window = window.reshape(bx + 2, (by + 2) * (bz + 2))
    spread_yz = box_matrix((by + 2) * (bz + 2), span_y * span_z, span_z, 0, live, bz + 2)
    lifted = jnp.repeat(dot(window, spread_yz), BOX, axis=0)
    solution = jnp.where(mask, solution + (lifted - WEIGHT * op(lifted) / diagonal), 0.0)
    for sweep_number in range(NU):
        solution = jnp.where(mask, solution + WEIGHT * (src - op(solution)) / diagonal, 0.0)
    return (trimmed(solution, span_y, span_z), coarse_error)


def solution(mesh):
    return jax.shard_map(
        local,
        mesh=mesh,
        in_specs=(
            P("gx", "gy", "grp"),
            P("gx", "gy", "grp"),
            P("gx", "gy", "grp"),
            P("gx", "gy", "grp"),
            P(("grp", "gx", "gy"), None, None),
            P(("grp", "gx", "gy"), None),
        ),
        out_specs=(P("gx", "gy", "grp"), P(("grp", "gx", "gy"))),
        check_vma=False,
    )
```

```python
import jax
import jax.numpy as jnp
from jax import lax
from jax.sharding import PartitionSpec as P

NU = 2
CITER = 4
BOX = 4
HALO = 4

WEIGHT = 2.0 / 3.0
ALL_AXES = ("grp", "gx", "gy")
PAIRS = ((0, 1), (0, -1), (1, 1), (1, -1), (2, 1), (2, -1))


def padded_size(shape):
    size = -(-shape[-1] // 128) * 128
    if len(shape) > 1:
        size *= -(-shape[-2] // 8) * 8
    for extent in shape[:-2]:
        size *= extent
    return size


def permute(slab, axis, pairs):
    count = slab.size
    if count % 128 == 0 and padded_size(slab.shape) > count + count // 4:
        return lax.ppermute(slab.reshape(-1, 128), axis, pairs).reshape(slab.shape)
    return lax.ppermute(slab, axis, pairs)


def exchange(cells, sides, width):
    for axis, dim in sides:
        count = lax.axis_size(axis)
        size = cells.shape[dim]
        head = lax.slice_in_dim(cells, 0, width, axis=dim)
        tail = lax.slice_in_dim(cells, size - width, size, axis=dim)
        if count == 1:
            before = jnp.zeros_like(tail)
            after = jnp.zeros_like(head)
        elif count == 2:
            index = lax.axis_index(axis)
            sent = jnp.where(index == 0, tail, head)
            got = permute(sent, axis, [(0, 1), (1, 0)])
            before = jnp.where(index == 1, got, 0.0)
            after = jnp.where(index == 0, got, 0.0)
        elif count % 2 == 0:
            index = lax.axis_index(axis)
            even = index % 2 == 0
            first = [(i + d, i + 1 - d) for i in range(0, count, 2) for d in (0, 1)]
            second = [(i + d, i + 1 - d) for i in range(1, count - 1, 2) for d in (0, 1)]
            got_first = permute(jnp.where(even, tail, head), axis, first)
            got_second = permute(jnp.where(even, head, tail), axis, second)
            before = jnp.where(even, got_second, got_first)
            after = jnp.where(even, got_first, got_second)
        else:
            before = permute(tail, axis, [(i, i + 1) for i in range(count - 1)])
            after = permute(head, axis, [(i + 1, i) for i in range(count - 1)])
        cells = jnp.concatenate([before, cells, after], axis=dim)
    return cells


def flat_shift(padded, rows, width, stride, dx, dy, dz):
    lead = stride + dy * stride + dz
    return padded[1 + dx:1 + dx + rows, lead:lead + width]


def neighbours(field, stride):
    return [
        jnp.roll(field, -1, axis=0),
        jnp.roll(field, 1, axis=0),
        jnp.roll(field, -stride, axis=1),
        jnp.roll(field, stride, axis=1),
        jnp.roll(field, -1, axis=1),
        jnp.roll(field, 1, axis=1),
    ]


def face_terms(conductance, stride):
    return [0.5 * (conductance + other) for other in neighbours(conductance, stride)]


def operate(field, storage, face_list, stride):
    summed = storage * field
    for face, other in zip(face_list, neighbours(field, stride)):
        summed = summed + face * (field - other)
    return summed


def inside_mask(rows, span_y, span_z):
    column = lax.broadcasted_iota(jnp.int32, (1, span_y * span_z), 1)
    coords = (
        (lax.broadcasted_iota(jnp.int32, (rows, 1), 0), rows, "gx"),
        (column // span_z, span_y, "gy"),
        (column % span_z, span_z, "grp"),
    )
    mask = None
    for local_index, span, axis in coords:
        block = span - 2 * HALO
        where = lax.axis_index(axis) * block - HALO + local_index
        ok = (where >= 0) & (where < block * lax.axis_size(axis))
        mask = ok if mask is None else mask & ok
    return jnp.broadcast_to(mask, (rows, span_y * span_z))


def trimmed(flat, span_y, span_z):
    cube = flat.reshape(flat.shape[0], span_y, span_z)
    return cube[HALO:-HALO, HALO:-HALO, HALO:-HALO]


def grp_pool(vector):
    groups = lax.axis_size("grp")
    index = lax.axis_index("grp")
    parts = [vector]
    for step in range(1, groups):
        parts.append(lax.ppermute(vector, "grp", [(i, (i + step) % groups) for i in range(groups)]))
    stacked = jnp.stack(parts)
    order = (index - jnp.arange(groups)) % groups
    return jnp.take(stacked, order, axis=0)


def dot(left, right):
    return jnp.dot(left, right, precision=lax.Precision.HIGHEST)


def box_matrix(boxes, cells, stride, offset, live, inner=None):
    cell = lax.broadcasted_iota(jnp.int32, (1, cells), 1)
    if inner is None:
        local = cell - offset
        owner = jnp.where((local >= 0) & (local < boxes * BOX), local // BOX, -1)
    else:
        outer_cell, inner_cell = cell // stride - offset, cell % stride - offset
        inside = (outer_cell >= 0) & (outer_cell < (boxes // inner) * BOX)
        inside = inside & (inner_cell >= 0) & (inner_cell < inner * BOX)
        owner = jnp.where(inside, (outer_cell // BOX) * inner + inner_cell // BOX, -1)
    box = lax.broadcasted_iota(jnp.int32, (boxes, cells), 0)
    return ((box == owner) & live).astype(jnp.float32)


def everyone(vector):
    count = lax.axis_size(ALL_AXES)
    copies = jnp.broadcast_to(vector[None], (count,) + vector.shape)
    return lax.all_to_all(copies, ALL_AXES, 0, 0, tiled=True).reshape(-1)


def local(source, conductance, storage, aggregate_ids, coarse_values, coarse_columns):
    size_x, size_y, size_z = source.shape
    assert HALO == BOX and HALO >= 2 * NU and HALO >= NU + 2
    stacked = jnp.stack([source, conductance, storage])
    wide = exchange(stacked, (("grp", 3),), HALO)
    span_z = wide.shape[3]
    stride = span_z
    wide = wide.reshape(3, size_x, size_y * span_z)
    wide = exchange(wide, (("gy", 2),), HALO * span_z)
    wide = exchange(wide, (("gx", 1),), HALO)
    rows = wide.shape[1]
    span_y = wide.shape[2] // span_z
    src, cond, stor = wide[0], wide[1], wide[2]
    mask = inside_mask(rows, span_y, span_z)
    face_list = face_terms(cond, stride)
    diagonal = stor
    for position in range(6):
        diagonal = diagonal + face_list[position]

    def op(field):
        return operate(field, stor, face_list, stride)

    solution = jnp.where(mask, WEIGHT * src / diagonal, 0.0)
    for sweep_number in range(NU - 1):
        solution = jnp.where(mask, solution + WEIGHT * (src - op(solution)) / diagonal, 0.0)
    residual = src - op(solution)
    scaled = jnp.where(mask, residual / diagonal, 0.0)
    smoothed = residual - WEIGHT * op(scaled)

    bx, by, bz = size_x // BOX, size_y // BOX, size_z // BOX
    live = lax.axis_index("grp") >= 0
    pick_x = box_matrix(bx, rows, 1, HALO, live)
    pick_yz = box_matrix(by * bz, span_y * span_z, span_z, HALO, live, bz).T
    box_totals = dot(pick_x, dot(smoothed, pick_yz)).reshape(-1)
    box_labels = aggregate_ids[::BOX, ::BOX, ::BOX].reshape(-1)
    placed = box_labels[:, None] == lax.broadcasted_iota(jnp.int32, (box_labels.shape[0],) * 2, 1)
    coarse_rhs = jnp.sum(jnp.where(placed, box_totals[:, None], 0.0), axis=0)
    eye = lax.broadcasted_iota(jnp.int32, (64, 64), 0) == lax.broadcasted_iota(jnp.int32, (64, 64), 1)
    coarse_diag = jnp.sum(jnp.where(eye[None], coarse_values[:, :, :64], 0.0), axis=2).reshape(-1)
    block_rows = coarse_values.shape[0]
    grid_x = lax.axis_size("gx")
    grid_y = lax.axis_size("gy")
    groups = lax.axis_size("grp")
    devices = groups * grid_x * grid_y
    column_list = coarse_columns.reshape(-1, 1)
    pick = (
        column_list // block_rows == lax.broadcasted_iota(jnp.int32, (column_list.shape[0], devices), 1)
    ).astype(source.dtype)
    within = column_list % block_rows
    coarse_error = coarse_rhs / coarse_diag
    for sweep_number in range(CITER - 1):
        pooled = everyone(coarse_error)
        rows_of = dot(pick, pooled.reshape(devices, -1))
        blocks = rows_of[:, :64]
        for part in range(1, block_rows):
            blocks = jnp.where(within == part, rows_of[:, part * 64:(part + 1) * 64], blocks)
        blocks = blocks.reshape(block_rows, -1)
        applied = jnp.einsum(
            "bim,bm->bi", coarse_values, blocks, precision=lax.Precision.HIGHEST
        ).reshape(-1)
        coarse_error = coarse_error + (coarse_rhs - applied) / coarse_diag

    small = jnp.sum(jnp.where(placed, coarse_error[None, :], 0.0), axis=1)
    every = everyone(small).reshape(groups, grid_x, grid_y, bx, by, bz)
    boxes = every.transpose(1, 3, 2, 4, 0, 5).reshape(grid_x * bx, grid_y * by, groups * bz)
    boxes = jnp.pad(boxes, 1)
    window = lax.dynamic_slice(
        boxes,
        (lax.axis_index("gx") * bx, lax.axis_index("gy") * by, lax.axis_index("grp") * bz),
        (bx + 2, by + 2, bz + 2),
    )
    window = window.reshape(bx + 2, (by + 2) * (bz + 2))
    spread_x = box_matrix(bx + 2, rows, 1, 0, live).T
    spread_yz = box_matrix((by + 2) * (bz + 2), span_y * span_z, span_z, 0, live, bz + 2)
    lifted = dot(spread_x, dot(window, spread_yz))
    solution = jnp.where(mask, solution + (lifted - WEIGHT * op(lifted) / diagonal), 0.0)
    for sweep_number in range(NU):
        solution = jnp.where(mask, solution + WEIGHT * (src - op(solution)) / diagonal, 0.0)
    return (trimmed(solution, span_y, span_z), coarse_error)


def solution(mesh):
    return jax.shard_map(
        local,
        mesh=mesh,
        in_specs=(
            P("gx", "gy", "grp"),
            P("gx", "gy", "grp"),
            P("gx", "gy", "grp"),
            P("gx", "gy", "grp"),
            P(("grp", "gx", "gy"), None, None),
            P(("grp", "gx", "gy"), None),
        ),
        out_specs=(P("gx", "gy", "grp"), P(("grp", "gx", "gy"))),
        check_vma=False,
    )
```

```python
import jax
import jax.numpy as jnp
from jax import lax
from jax.sharding import PartitionSpec as P

NU = 2
CITER = 4
BOX = 4
HALO = 4

WEIGHT = 2.0 / 3.0
ALL_AXES = ("grp", "gx", "gy")
PAIRS = ((0, 1), (0, -1), (1, 1), (1, -1), (2, 1), (2, -1))


def padded_size(shape):
    size = -(-shape[-1] // 128) * 128
    if len(shape) > 1:
        size *= -(-shape[-2] // 8) * 8
    for extent in shape[:-2]:
        size *= extent
    return size


def permute(slab, axis, pairs):
    count = slab.size
    if count % 128 == 0 and padded_size(slab.shape) > count + count // 4:
        return lax.ppermute(slab.reshape(-1, 128), axis, pairs).reshape(slab.shape)
    return lax.ppermute(slab, axis, pairs)


def exchange(cells, sides, width):
    for axis, dim in sides:
        count = lax.axis_size(axis)
        size = cells.shape[dim]
        head = lax.slice_in_dim(cells, 0, width, axis=dim)
        tail = lax.slice_in_dim(cells, size - width, size, axis=dim)
        if count == 1:
            before = jnp.zeros_like(tail)
            after = jnp.zeros_like(head)
        elif count == 2:
            index = lax.axis_index(axis)
            sent = jnp.where(index == 0, tail, head)
            got = permute(sent, axis, [(0, 1), (1, 0)])
            before = jnp.where(index == 1, got, 0.0)
            after = jnp.where(index == 0, got, 0.0)
        elif count % 2 == 0:
            index = lax.axis_index(axis)
            even = index % 2 == 0
            first = [(i + d, i + 1 - d) for i in range(0, count, 2) for d in (0, 1)]
            second = [(i + d, i + 1 - d) for i in range(1, count - 1, 2) for d in (0, 1)]
            got_first = permute(jnp.where(even, tail, head), axis, first)
            got_second = permute(jnp.where(even, head, tail), axis, second)
            before = jnp.where(even, got_second, got_first)
            after = jnp.where(even, got_first, got_second)
        else:
            before = permute(tail, axis, [(i, i + 1) for i in range(count - 1)])
            after = permute(head, axis, [(i + 1, i) for i in range(count - 1)])
        cells = jnp.concatenate([before, cells, after], axis=dim)
    return cells


def flat_shift(padded, rows, width, stride, dx, dy, dz):
    lead = stride + dy * stride + dz
    return padded[1 + dx:1 + dx + rows, lead:lead + width]


def neighbours(field, stride):
    rows, width = field.shape
    padded = jnp.pad(field, ((1, 1), (stride, stride)))
    steps = ((1, 0, 0), (-1, 0, 0), (0, 1, 0), (0, -1, 0), (0, 0, 1), (0, 0, -1))
    return [flat_shift(padded, rows, width, stride, *step) for step in steps]


def face_terms(conductance, stride):
    return [0.5 * (conductance + other) for other in neighbours(conductance, stride)]


def operate(field, storage, face_list, stride):
    summed = storage * field
    for face, other in zip(face_list, neighbours(field, stride)):
        summed = summed + face * (field - other)
    return summed


def inside_mask(rows, span_y, span_z):
    column = lax.broadcasted_iota(jnp.int32, (1, span_y * span_z), 1)
    coords = (
        (lax.broadcasted_iota(jnp.int32, (rows, 1), 0), rows, "gx"),
        (column // span_z, span_y, "gy"),
        (column % span_z, span_z, "grp"),
    )
    mask = None
    for local_index, span, axis in coords:
        block = span - 2 * HALO
        where = lax.axis_index(axis) * block - HALO + local_index
        ok = (where >= 0) & (where < block * lax.axis_size(axis))
        mask = ok if mask is None else mask & ok
    return jnp.broadcast_to(mask, (rows, span_y * span_z))


def trimmed(flat, span_y, span_z):
    cube = flat.reshape(flat.shape[0], span_y, span_z)
    return cube[HALO:-HALO, HALO:-HALO, HALO:-HALO]


def grp_pool(vector):
    groups = lax.axis_size("grp")
    index = lax.axis_index("grp")
    parts = [vector]
    for step in range(1, groups):
        parts.append(lax.ppermute(vector, "grp", [(i, (i + step) % groups) for i in range(groups)]))
    stacked = jnp.stack(parts)
    order = (index - jnp.arange(groups)) % groups
    return jnp.take(stacked, order, axis=0)


def dot(left, right):
    return jnp.dot(left, right, precision=lax.Precision.HIGHEST)


def box_matrix(boxes, cells, stride, offset, live, inner=None, cells_first=False):
    cell = lax.broadcasted_iota(jnp.int32, (cells, 1), 0) if cells_first else lax.broadcasted_iota(jnp.int32, (1, cells), 1)
    if inner is None:
        local = cell - offset
        owner = jnp.where((local >= 0) & (local < boxes * BOX), local // BOX, -1)
    else:
        outer_cell, inner_cell = cell // stride - offset, cell % stride - offset
        inside = (outer_cell >= 0) & (outer_cell < (boxes // inner) * BOX)
        inside = inside & (inner_cell >= 0) & (inner_cell < inner * BOX)
        owner = jnp.where(inside, (outer_cell // BOX) * inner + inner_cell // BOX, -1)
    if cells_first:
        box = lax.broadcasted_iota(jnp.int32, (cells, boxes), 1)
    else:
        box = lax.broadcasted_iota(jnp.int32, (boxes, cells), 0)
    return ((box == owner) & live).astype(jnp.float32)


def everyone(vector):
    count = lax.axis_size(ALL_AXES)
    copies = jnp.broadcast_to(vector[None], (count,) + vector.shape)
    return lax.all_to_all(copies, ALL_AXES, 0, 0, tiled=True).reshape(-1)


def local(source, conductance, storage, aggregate_ids, coarse_values, coarse_columns):
    size_x, size_y, size_z = source.shape
    assert HALO == BOX and HALO >= 2 * NU and HALO >= NU + 2
    stacked = jnp.stack([source, conductance, storage])
    wide = exchange(stacked, (("grp", 3),), HALO)
    span_z = wide.shape[3]
    stride = span_z
    wide = wide.reshape(3, size_x, size_y * span_z)
    wide = exchange(wide, (("gy", 2),), HALO * span_z)
    wide = exchange(wide, (("gx", 1),), HALO)
    rows = wide.shape[1]
    span_y = wide.shape[2] // span_z
    src, cond, stor = wide[0], wide[1], wide[2]
    mask = inside_mask(rows, span_y, span_z)
    face_list = face_terms(cond, stride)
    diagonal = stor
    for position in range(6):
        diagonal = diagonal + face_list[position]

    def op(field):
        return operate(field, stor, face_list, stride)

    solution = jnp.where(mask, WEIGHT * src / diagonal, 0.0)
    for sweep_number in range(NU - 1):
        solution = jnp.where(mask, solution + WEIGHT * (src - op(solution)) / diagonal, 0.0)
    residual = src - op(solution)
    scaled = jnp.where(mask, residual / diagonal, 0.0)
    smoothed = residual - WEIGHT * op(scaled)

    bx, by, bz = size_x // BOX, size_y // BOX, size_z // BOX
    live = lax.axis_index("grp") >= 0
    pick_x = box_matrix(bx, rows, 1, HALO, live)
    pick_yz = box_matrix(by * bz, span_y * span_z, span_z, HALO, live, bz, cells_first=True)
    box_totals = dot(pick_x, dot(smoothed, pick_yz)).reshape(-1)
    box_labels = aggregate_ids[::BOX, ::BOX, ::BOX].reshape(-1)
    placed = box_labels[:, None] == lax.broadcasted_iota(jnp.int32, (box_labels.shape[0],) * 2, 1)
    coarse_rhs = jnp.sum(jnp.where(placed, box_totals[:, None], 0.0), axis=0)
    eye = lax.broadcasted_iota(jnp.int32, (64, 64), 0) == lax.broadcasted_iota(jnp.int32, (64, 64), 1)
    coarse_diag = jnp.sum(jnp.where(eye[None], coarse_values[:, :, :64], 0.0), axis=2).reshape(-1)
    block_rows = coarse_values.shape[0]
    grid_x = lax.axis_size("gx")
    grid_y = lax.axis_size("gy")
    groups = lax.axis_size("grp")
    devices = groups * grid_x * grid_y
    column_list = coarse_columns.reshape(-1, 1)
    pick = (
        column_list // block_rows == lax.broadcasted_iota(jnp.int32, (column_list.shape[0], devices), 1)
    ).astype(source.dtype)
    within = column_list % block_rows
    coarse_error = coarse_rhs / coarse_diag
    for sweep_number in range(CITER - 1):
        pooled = everyone(coarse_error)
        rows_of = dot(pick, pooled.reshape(devices, -1))
        blocks = rows_of[:, :64]
        for part in range(1, block_rows):
            blocks = jnp.where(within == part, rows_of[:, part * 64:(part + 1) * 64], blocks)
        blocks = blocks.reshape(block_rows, -1)
        applied = jnp.einsum(
            "bim,bm->bi", coarse_values, blocks, precision=lax.Precision.HIGHEST
        ).reshape(-1)
        coarse_error = coarse_error + (coarse_rhs - applied) / coarse_diag

    small = jnp.sum(jnp.where(placed, coarse_error[None, :], 0.0), axis=1)
    every = everyone(small).reshape(groups, grid_x, grid_y, bx, by, bz)
    boxes = every.transpose(1, 3, 2, 4, 0, 5).reshape(grid_x * bx, grid_y * by, groups * bz)
    boxes = jnp.pad(boxes, 1)
    window = lax.dynamic_slice(
        boxes,
        (lax.axis_index("gx") * bx, lax.axis_index("gy") * by, lax.axis_index("grp") * bz),
        (bx + 2, by + 2, bz + 2),
    )
    window = window.reshape(bx + 2, (by + 2) * (bz + 2))
    spread_x = box_matrix(bx + 2, rows, 1, 0, live).T
    spread_yz = box_matrix((by + 2) * (bz + 2), span_y * span_z, span_z, 0, live, bz + 2)
    lifted = dot(spread_x, dot(window, spread_yz))
    solution = jnp.where(mask, solution + (lifted - WEIGHT * op(lifted) / diagonal), 0.0)
    for sweep_number in range(NU):
        solution = jnp.where(mask, solution + WEIGHT * (src - op(solution)) / diagonal, 0.0)
    return (trimmed(solution, span_y, span_z), coarse_error)


def solution(mesh):
    return jax.shard_map(
        local,
        mesh=mesh,
        in_specs=(
            P("gx", "gy", "grp"),
            P("gx", "gy", "grp"),
            P("gx", "gy", "grp"),
            P("gx", "gy", "grp"),
            P(("grp", "gx", "gy"), None, None),
            P(("grp", "gx", "gy"), None),
        ),
        out_specs=(P("gx", "gy", "grp"), P(("grp", "gx", "gy"))),
        check_vma=False,
    )
```

```python
import jax
import jax.numpy as jnp
from jax import lax
from jax.sharding import PartitionSpec as P

NU = 2
CITER = 4
BOX = 4
HALO = 4

WEIGHT = 2.0 / 3.0
ALL_AXES = ("grp", "gx", "gy")
PAIRS = ((0, 1), (0, -1), (1, 1), (1, -1), (2, 1), (2, -1))


def padded_size(shape):
    size = -(-shape[-1] // 128) * 128
    if len(shape) > 1:
        size *= -(-shape[-2] // 8) * 8
    for extent in shape[:-2]:
        size *= extent
    return size


def permute(slab, axis, pairs):
    count = slab.size
    if count % 128 == 0 and padded_size(slab.shape) > count + count // 4:
        return lax.ppermute(slab.reshape(-1, 128), axis, pairs).reshape(slab.shape)
    return lax.ppermute(slab, axis, pairs)


def exchange(cells, sides, width):
    for axis, dim in sides:
        count = lax.axis_size(axis)
        size = cells.shape[dim]
        head = lax.slice_in_dim(cells, 0, width, axis=dim)
        tail = lax.slice_in_dim(cells, size - width, size, axis=dim)
        if count == 1:
            before = jnp.zeros_like(tail)
            after = jnp.zeros_like(head)
        elif count == 2:
            index = lax.axis_index(axis)
            sent = jnp.where(index == 0, tail, head)
            got = permute(sent, axis, [(0, 1), (1, 0)])
            before = jnp.where(index == 1, got, 0.0)
            after = jnp.where(index == 0, got, 0.0)
        elif count % 2 == 0:
            index = lax.axis_index(axis)
            even = index % 2 == 0
            first = [(i + d, i + 1 - d) for i in range(0, count, 2) for d in (0, 1)]
            second = [(i + d, i + 1 - d) for i in range(1, count - 1, 2) for d in (0, 1)]
            got_first = permute(jnp.where(even, tail, head), axis, first)
            got_second = permute(jnp.where(even, head, tail), axis, second)
            before = jnp.where(even, got_second, got_first)
            after = jnp.where(even, got_first, got_second)
        else:
            before = permute(tail, axis, [(i, i + 1) for i in range(count - 1)])
            after = permute(head, axis, [(i + 1, i) for i in range(count - 1)])
        cells = jnp.concatenate([before, cells, after], axis=dim)
    return cells


def flat_shift(padded, rows, width, stride, dx, dy, dz):
    lead = stride + dy * stride + dz
    return padded[1 + dx:1 + dx + rows, lead:lead + width]


def neighbours(field, stride):
    rows, width = field.shape
    padded = jnp.pad(field, ((1, 1), (stride, stride)))
    steps = ((1, 0, 0), (-1, 0, 0), (0, 1, 0), (0, -1, 0), (0, 0, 1), (0, 0, -1))
    return [flat_shift(padded, rows, width, stride, *step) for step in steps]


def face_terms(conductance, stride):
    return [0.5 * (conductance + other) for other in neighbours(conductance, stride)]


def operate(field, storage, face_list, stride):
    summed = storage * field
    for face, other in zip(face_list, neighbours(field, stride)):
        summed = summed + face * (field - other)
    return summed


def inside_mask(rows, span_y, span_z):
    column = lax.broadcasted_iota(jnp.int32, (1, span_y * span_z), 1)
    coords = (
        (lax.broadcasted_iota(jnp.int32, (rows, 1), 0), rows, "gx"),
        (column // span_z, span_y, "gy"),
        (column % span_z, span_z, "grp"),
    )
    mask = None
    for local_index, span, axis in coords:
        block = span - 2 * HALO
        where = lax.axis_index(axis) * block - HALO + local_index
        ok = (where >= 0) & (where < block * lax.axis_size(axis))
        mask = ok if mask is None else mask & ok
    return jnp.broadcast_to(mask, (rows, span_y * span_z))


def trimmed(flat, span_y, span_z):
    cube = flat[HALO:-HALO].reshape(flat.shape[0] - 2 * HALO, span_y, span_z)
    return cube[:, HALO:-HALO, HALO:-HALO]


def grp_pool(vector):
    groups = lax.axis_size("grp")
    index = lax.axis_index("grp")
    parts = [vector]
    for step in range(1, groups):
        parts.append(lax.ppermute(vector, "grp", [(i, (i + step) % groups) for i in range(groups)]))
    stacked = jnp.stack(parts)
    order = (index - jnp.arange(groups)) % groups
    return jnp.take(stacked, order, axis=0)


def dot(left, right):
    return jnp.dot(left, right, precision=lax.Precision.HIGHEST)


def box_matrix(boxes, cells, stride, offset, live, inner=None):
    cell = lax.broadcasted_iota(jnp.int32, (1, cells), 1)
    if inner is None:
        local = cell - offset
        owner = jnp.where((local >= 0) & (local < boxes * BOX), local // BOX, -1)
    else:
        outer_cell, inner_cell = cell // stride - offset, cell % stride - offset
        inside = (outer_cell >= 0) & (outer_cell < (boxes // inner) * BOX)
        inside = inside & (inner_cell >= 0) & (inner_cell < inner * BOX)
        owner = jnp.where(inside, (outer_cell // BOX) * inner + inner_cell // BOX, -1)
    box = lax.broadcasted_iota(jnp.int32, (boxes, cells), 0)
    return ((box == owner) & live).astype(jnp.float32)


def everyone(vector):
    count = lax.axis_size(ALL_AXES)
    copies = jnp.broadcast_to(vector[None], (count,) + vector.shape)
    return lax.all_to_all(copies, ALL_AXES, 0, 0, tiled=True).reshape(-1)


def local(source, conductance, storage, aggregate_ids, coarse_values, coarse_columns):
    size_x, size_y, size_z = source.shape
    assert HALO == BOX and HALO >= 2 * NU and HALO >= NU + 2
    stacked = jnp.stack([source, conductance, storage])
    wide = exchange(stacked, (("grp", 3),), HALO)
    span_z = wide.shape[3]
    stride = span_z
    wide = wide.reshape(3, size_x, size_y * span_z)
    wide = exchange(wide, (("gy", 2),), HALO * span_z)
    wide = exchange(wide, (("gx", 1),), HALO)
    rows = wide.shape[1]
    span_y = wide.shape[2] // span_z
    src, cond, stor = wide[0], wide[1], wide[2]
    mask = inside_mask(rows, span_y, span_z)
    face_list = face_terms(cond, stride)
    diagonal = stor
    for position in range(6):
        diagonal = diagonal + face_list[position]

    def op(field):
        return operate(field, stor, face_list, stride)

    solution = jnp.where(mask, WEIGHT * src / diagonal, 0.0)
    for sweep_number in range(NU - 1):
        solution = jnp.where(mask, solution + WEIGHT * (src - op(solution)) / diagonal, 0.0)
    residual = src - op(solution)
    scaled = jnp.where(mask, residual / diagonal, 0.0)
    smoothed = residual - WEIGHT * op(scaled)

    bx, by, bz = size_x // BOX, size_y // BOX, size_z // BOX
    live = lax.axis_index("grp") >= 0
    pick_x = box_matrix(bx, rows, 1, HALO, live)
    pick_yz = box_matrix(by * bz, span_y * span_z, span_z, HALO, live, bz).T
    box_totals = dot(pick_x, dot(smoothed, pick_yz)).reshape(-1)
    box_labels = aggregate_ids[::BOX, ::BOX, ::BOX].reshape(-1)
    placed = box_labels[:, None] == lax.broadcasted_iota(jnp.int32, (box_labels.shape[0],) * 2, 1)
    coarse_rhs = jnp.sum(jnp.where(placed, box_totals[:, None], 0.0), axis=0)
    eye = lax.broadcasted_iota(jnp.int32, (64, 64), 0) == lax.broadcasted_iota(jnp.int32, (64, 64), 1)
    coarse_diag = jnp.sum(jnp.where(eye[None], coarse_values[:, :, :64], 0.0), axis=2).reshape(-1)
    block_rows = coarse_values.shape[0]
    grid_x = lax.axis_size("gx")
    grid_y = lax.axis_size("gy")
    groups = lax.axis_size("grp")
    devices = groups * grid_x * grid_y
    column_list = coarse_columns.reshape(-1, 1)
    pick = (
        column_list // block_rows == lax.broadcasted_iota(jnp.int32, (column_list.shape[0], devices), 1)
    ).astype(source.dtype)
    within = column_list % block_rows
    coarse_error = coarse_rhs / coarse_diag
    for sweep_number in range(CITER - 1):
        pooled = everyone(coarse_error)
        rows_of = dot(pick, pooled.reshape(devices, -1))
        blocks = rows_of[:, :64]
        for part in range(1, block_rows):
            blocks = jnp.where(within == part, rows_of[:, part * 64:(part + 1) * 64], blocks)
        blocks = blocks.reshape(block_rows, -1)
        applied = jnp.einsum(
            "bim,bm->bi", coarse_values, blocks, precision=lax.Precision.HIGHEST
        ).reshape(-1)
        coarse_error = coarse_error + (coarse_rhs - applied) / coarse_diag

    small = jnp.sum(jnp.where(placed, coarse_error[None, :], 0.0), axis=1)
    every = everyone(small).reshape(groups, grid_x, grid_y, bx, by, bz)
    boxes = every.transpose(1, 3, 2, 4, 0, 5).reshape(grid_x * bx, grid_y * by, groups * bz)
    boxes = jnp.pad(boxes, 1)
    window = lax.dynamic_slice(
        boxes,
        (lax.axis_index("gx") * bx, lax.axis_index("gy") * by, lax.axis_index("grp") * bz),
        (bx + 2, by + 2, bz + 2),
    )
    window = window.reshape(bx + 2, (by + 2) * (bz + 2))
    spread_x = box_matrix(bx + 2, rows, 1, 0, live).T
    spread_yz = box_matrix((by + 2) * (bz + 2), span_y * span_z, span_z, 0, live, bz + 2)
    lifted = dot(spread_x, dot(window, spread_yz))
    solution = jnp.where(mask, solution + (lifted - WEIGHT * op(lifted) / diagonal), 0.0)
    for sweep_number in range(NU):
        solution = jnp.where(mask, solution + WEIGHT * (src - op(solution)) / diagonal, 0.0)
    return (trimmed(solution, span_y, span_z), coarse_error)


def solution(mesh):
    return jax.shard_map(
        local,
        mesh=mesh,
        in_specs=(
            P("gx", "gy", "grp"),
            P("gx", "gy", "grp"),
            P("gx", "gy", "grp"),
            P("gx", "gy", "grp"),
            P(("grp", "gx", "gy"), None, None),
            P(("grp", "gx", "gy"), None),
        ),
        out_specs=(P("gx", "gy", "grp"), P(("grp", "gx", "gy"))),
        check_vma=False,
    )
```
